32 devices in a mesh: grp: 2 (over core), lat: 4 (over z), lon: 4 (over y, x).
Axes of the slice: x: 2, y: 2, z: 4, core: 2. Of those that a mesh axis runs over, the one named last changes fastest.
Arguments:
- state: float32 [2, 3, 8, 128, 1024], P('grp', None, None, 'lat', 'lon'), may hold values from -6 to 6
- surface: float32 [2, 3, 128, 1024], P('grp', None, 'lat', 'lon'), may hold values from -6 to 6
- sea_mask: int32 [2, 128, 1024], P('grp', 'lat', 'lon'), may hold values 0 or 1
- coeffs: float32 [2, 4, 8], P('grp'), may hold values from 0.05 to 0.2
- remap_weights: float32 [2, 8, 256, 256], P('grp'), may hold values from -0.1875 to 0.1875
- link_dest: int32 [2, 2048, 1], P('grp', ('lat', 'lon')), may hold values from 0 to 15; in each aligned block of 128 rows (0 to 127, 128 to 255, ..., all dimensions but the last counted through in order) at most 16 rows name the same one
- link_src_row: int32 [2, 2048], P('grp', ('lat', 'lon')), may hold values from 0 to 31
- link_dst_row: int32 [2, 2048], P('grp', ('lat', 'lon')), may hold values from 0 to 31
- link_tile: int32 [2, 2048], P('grp', ('lat', 'lon')), may hold values from 0 to 7
Outputs:
- new_state: float32 [2, 3, 8, 128, 1024], P('grp', None, None, 'lat', 'lon')
- new_surface: float32 [2, 3, 128, 1024], P('grp', None, 'lat', 'lon')
The draws below stay inside these ranges and needn't reach their ends.
Inputs may be any that keep to these rules, and one draw needn't show every extreme that they name: `link_dest`: at most 16 of the 128 links held by one device name the same destination owner, and some device has that many for some owner.
All inputs are finite; a program needn't handle non-finite values. No bound on the sum of `sea_mask` on one device may be relied on, other than what follows from the above.
Results may differ from the reference program's by a relative error of at most 0.0001.
Values sent between devices are 32-bit elements; how exact they have to be, the bound alone decides.
No kernel may reach another device: no remote copies, remote signals or barrier semaphores. Data moves between devices by JAX's collectives and lax.ppermute only.
A program may use at most 64 MiB of HBM per device.

```python
import math
import jax
import jax.numpy as jnp
import numpy as np
from jax import lax

LEVELS = 8
ROWS = 32
COLS = 256
TILE_KINDS = 8
SUBSTEPS = 2
LINKS = 128
SLOTS = 16
LAT_ROWS = 128
LON_COLS = 1024
LINKS_ALL = 2048
N_LAT = 4
N_LON = 4


def set_ends(drawn, rng, smallest, largest):
    spot = [jax.random.randint(jax.random.fold_in(rng, axis), (), 0, length) for axis, length in enumerate(drawn.shape)]
    longest = drawn.shape.index(max(drawn.shape))
    neighbour = spot[:longest] + [(spot[longest] + 1) % drawn.shape[longest]] + spot[longest + 1:]
    return drawn.at[tuple(spot)].set(smallest).at[tuple(neighbour)].set(largest)


def level_of(key, dims, cuts, low, high):
    def one(position, shards_of):
        heights = jax.random.uniform(jax.random.fold_in(jax.random.fold_in(key, 6), position), (shards_of,), jnp.float32, low / len(cuts), high / len(cuts))
        return jnp.repeat(jnp.exp(heights), dims[position] // shards_of).reshape((-1,) + (1,) * (len(dims) - position - 1))

    loudness = one(*cuts[0])
    for cut in cuts[1:]:
        loudness = loudness * one(*cut)
    return loudness


def routed_block(rng, own, number, rows, amount, top, most, skew):
    order = jax.random.permutation(rng, amount)
    packed, ordinary = load_shares(amount, rows * top, most, skew, True), load_shares(amount, rows * top, most, skew, False)
    places = jnp.arange(amount)

    def named(lengths, offset_by):
        used = int((lengths > 0).sum())
        fixed = max(1, used // 4)
        passed = fixed + (places - fixed + offset_by * (used - fixed)) % max(1, amount - fixed)
        return jnp.zeros((amount,), jnp.int32).at[order[jnp.where(places < fixed, places, passed)]].set(jnp.asarray(lengths, jnp.int32))

    lengths = jnp.where(number % 4 == 0, named(packed, number // 4), named(ordinary, number - number // 4 - 1))
    mixed = jax.random.permutation(jax.random.fold_in(own, 3), amount)
    donor, receiver = mixed[0:amount // 2 * 2:2], mixed[1:amount // 2 * 2:2]
    room = jnp.minimum(lengths[donor] - 1, most - lengths[receiver]) // 2
    room = jnp.where((donor == order[0]) | (receiver == order[0]) | (lengths[receiver] == 0), 0, jnp.maximum(room, 0))
    passed = jax.random.randint(jax.random.fold_in(own, 4), (amount // 2,), 0, 1 << 20) % (room + 1)
    lengths = lengths.at[donor].add(-passed).at[receiver].add(passed)
    labels = jnp.searchsorted(jnp.cumsum(lengths), jnp.arange(rows * top), side="right").astype(jnp.int32)
    listing = labels.reshape(top, rows).T
    listing = listing[jax.random.permutation(jax.random.fold_in(own, 1), rows)]
    offset_by = jax.random.randint(jax.random.fold_in(own, 2), (rows, 1), 0, top)
    return jnp.take_along_axis(listing, (jnp.arange(top)[None, :] + offset_by) % top, axis=1)


def load_shares(number_of, total, bound, lean, full):
    weights = [(1 << 20) // math.isqrt(standing ** lean) + 1 for standing in range(1, number_of + 1)]
    largest = bound if full else min(bound, max(-(-total // number_of), total * weights[0] // sum(weights)))
    least = 1 if total - largest >= number_of - 1 else 0
    counts, spare = [largest] + [least] * (number_of - 1), total - largest - least * (number_of - 1)
    while spare > 0:
        candidates = [i for i in range(1, number_of) if counts[i] < largest] or [i for i in range(1, number_of) if counts[i] < bound]
        pool, budget = sum([weights[i] for i in candidates]), spare
        for i in candidates:
            addition = min(bound - counts[i], max(1, budget * weights[i] // pool), spare)
            counts[i] = counts[i] + addition
            spare = spare - addition
    return np.array(counts)


def gaussian(key, dims, scale, most, cuts=(), kind=jnp.bfloat16):
    entries = jax.random.normal(key, dims, jnp.float32) * scale
    if len(cuts) > 0:
        entries = level_of(key, dims, cuts, -0.22, 0.18) * entries
    return jnp.clip(entries, min=-most, max=most).astype(kind)


def setup_inputs(seed: int = 0) -> dict:
    splits = jax.random.split(jax.random.key(seed), 10)
    state = gaussian(splits[0], (2, 3, LEVELS, LAT_ROWS, LON_COLS), 1.0, 6.0, ((0, 2), (3, 4), (4, 4)), jnp.float32)
    surface = gaussian(splits[1], (2, 3, LAT_ROWS, LON_COLS), 1.0, 6.0, ((0, 2), (2, 4), (3, 4)), jnp.float32)
    sea_mask = set_ends((jax.random.randint(splits[2], (2, LAT_ROWS, LON_COLS), 0, 4) < 3).astype(jnp.int32), jax.random.fold_in(splits[2], 1), 0, 1)
    coeffs = jnp.clip(0.05 + 0.15 * jax.random.uniform(splits[3], (2, 4, LEVELS), jnp.float32) ** level_of(splits[3], (2, 4, LEVELS), ((0, 2),), -0.2, 0.2), 0.05, 0.2)
    remap_weights = gaussian(splits[4], (2, TILE_KINDS, COLS, COLS), (4 * COLS) ** -0.5, 0.1875, ((0, 2),), jnp.float32)
    link_dest_keys = jax.random.split(jax.random.fold_in(splits[5], 1), 2 * LINKS_ALL // LINKS)
    link_dest_turns = jax.random.permutation(jax.random.fold_in(splits[5], 3), 2 * LINKS_ALL // LINKS)
    link_dest = jax.vmap(lambda own, number: routed_block(jax.random.fold_in(splits[5], 2), own, number, LINKS, N_LAT * N_LON, 1, SLOTS, 2))(link_dest_keys, link_dest_turns).reshape((2, LINKS_ALL, 1))
    link_src_row = set_ends(jax.random.randint(splits[6], (2, LINKS_ALL), 0, ROWS), jax.random.fold_in(splits[6], 1), 0, ROWS - 1).astype(jnp.int32)
    link_dst_row = set_ends(jax.random.randint(splits[7], (2, LINKS_ALL), 0, ROWS), jax.random.fold_in(splits[7], 1), 0, ROWS - 1).astype(jnp.int32)
    link_tile = set_ends(jax.random.randint(splits[8], (2, LINKS_ALL), 0, TILE_KINDS), jax.random.fold_in(splits[8], 1), 0, TILE_KINDS - 1).astype(jnp.int32)
    return {"state": state, "surface": surface, "sea_mask": sea_mask, "coeffs": coeffs, "remap_weights": remap_weights, "link_dest": link_dest, "link_src_row": link_src_row, "link_dst_row": link_dst_row, "link_tile": link_tile}


air_gain = 0.3
ocean_gain = 0.5
drag_coeff = 0.5
heat_coeff = 0.5
gust_speed = 0.5
coriolis_scale = 0.25

def surface_export(ground, previous, sea_float, ocean_side):
    slip_east = ground[0] - previous[0]
    slip_north = ground[1] - previous[1]
    wind_speed = jnp.sqrt(slip_east * slip_east + slip_north * slip_north + gust_speed * gust_speed)
    bulk_flux = jnp.stack([drag_coeff * wind_speed * slip_east, drag_coeff * wind_speed * slip_north, heat_coeff * wind_speed * (previous[2] - ground[2])])
    return jnp.where(ocean_side, ground, bulk_flux) * sea_float

def substep(padded, mask_out, top_row, total_rows, level_coef):
    center = padded[:, :, 1:-1, 1:-1]
    north = padded[:, :, 2:, 1:-1]
    south = padded[:, :, :-2, 1:-1]
    east = padded[:, :, 1:-1, 2:]
    west = padded[:, :, 1:-1, :-2]
    diffuse = level_coef[0][None, :, None, None]
    advect_east = level_coef[1][None, :, None, None]
    advect_north = level_coef[2][None, :, None, None]
    mixing = level_coef[3][None, :, None, None]
    laplace = north + south + east + west - 4.0 * center
    above = jnp.concatenate([center[:, 1:], center[:, -1:]], 1)
    below = jnp.concatenate([center[:, :1], center[:, :-1]], 1)
    height = center.shape[2]
    row_index = top_row + jnp.arange(height, dtype=jnp.int32)
    latitude = jnp.pi * (-1.0 / 3.0 + 2.0 / 3.0 * (row_index.astype(center.dtype) + 0.5) / total_rows)
    coriolis = (coriolis_scale * jnp.sin(latitude))[:, None]
    turning = jnp.stack([coriolis * center[1], -coriolis * center[0], jnp.zeros_like(center[2])])
    inside = ((row_index >= 0) & (row_index < total_rows)).astype(center.dtype)[:, None]
    updated = center + diffuse * laplace - advect_east * (east - west) - advect_north * (north - south) + mixing * (above + below - 2.0 * center) + turning
    return updated * (mask_out * inside)

def remap(exported, targets, src_rows, dst_rows, kinds, tile_table, sea_float):
    peer_count = N_LAT * N_LON
    blocks = exported.reshape(3, N_LAT, ROWS, N_LON, COLS).transpose(1, 3, 0, 2, 4).reshape(peer_count, 3, ROWS, COLS)
    src_two = src_rows.reshape(peer_count, LINKS)
    kind_two = kinds.reshape(peer_count, LINKS)

    def per_device(operands):
        block, rows_here, kinds_here = operands
        combos = jnp.einsum('cax,wxy->wcay', block, tile_table, precision=lax.Precision.HIGHEST)
        return combos[kinds_here, :, rows_here, :]
    pieces = lax.map(per_device, (blocks, src_two, kind_two)).reshape(peer_count * LINKS, 3, COLS)
    segment = (targets * ROWS + dst_rows).astype(jnp.int32)
    summed = jax.ops.segment_sum(pieces, segment, num_segments=peer_count * ROWS)
    summed = summed.reshape(N_LAT, N_LON, ROWS, 3, COLS).transpose(3, 0, 2, 1, 4).reshape(3, LAT_ROWS, LON_COLS)
    return summed * sea_float

def reference(state, surface, sea_mask, coeffs, remap_weights, link_dest, link_src_row, link_dst_row, link_tile):
    results = []
    exports = []
    for side in range(2):
        fields = state[side]
        previous = surface[side]
        sea_float = sea_mask[side].astype(state.dtype)
        ocean_side = side == 1
        exports.append(surface_export(fields[:, 0], previous, sea_float, ocean_side))
        gain = ocean_gain if ocean_side else air_gain
        damping = 0.0 if ocean_side else air_gain
        ground = fields[:, 0] + sea_float * (gain * previous - damping * fields[:, 0])
        fields = jnp.concatenate([ground[:, None], fields[:, 1:]], 1)
        state_mask = sea_float if ocean_side else jnp.ones_like(sea_float)
        for substep_index in range(SUBSTEPS):
            padded = jnp.pad(fields, ((0, 0), (0, 0), (0, 0), (1, 1)), mode='wrap')
            padded = jnp.pad(padded, ((0, 0), (0, 0), (1, 1), (0, 0)))
            fields = substep(padded, state_mask, 0, LAT_ROWS, coeffs[side])
        results.append(fields)
    imports = []
    for side in range(2):
        source = 1 - side
        imports.append(remap(exports[source], link_dest[source, :, 0], link_src_row[source], link_dst_row[source], link_tile[source], remap_weights[source], sea_mask[side].astype(state.dtype)))
    return (jnp.stack(results), jnp.stack(imports))
```

```python
import jax
import jax.numpy as jnp
from jax import lax
from jax.sharding import PartitionSpec as P

SUBSTEPS = 2


air_gain = 0.3
ocean_gain = 0.5
drag_coeff = 0.5
heat_coeff = 0.5
gust_speed = 0.5
coriolis_scale = 0.25

HIGHEST = lax.Precision.HIGHEST


def shifted(part, axis, closed, forward):
    count = lax.axis_size(axis)
    ends = count if closed else count - 1
    if forward:
        route = [(i, (i + 1) % count) for i in range(ends)]
    else:
        route = [((i + 1) % count, i) for i in range(ends)]
    flat = lax.ppermute(part.reshape(-1), axis, route)
    return flat.reshape(part.shape)


def with_halo(cells, width):
    head = cells[:, :, :width]
    tail = cells[:, :, -width:]
    cells = jnp.concatenate(
        [shifted(tail, "lon", True, True), cells, shifted(head, "lon", True, False)], axis=2
    )
    head = cells[:, :width, :]
    tail = cells[:, -width:, :]
    return jnp.concatenate(
        [shifted(tail, "lat", False, True), cells, shifted(head, "lat", False, False)], axis=1
    )


def surface_export(ground, previous, sea_float, ocean_side):
    slip_east = ground[0] - previous[0]
    slip_north = ground[1] - previous[1]
    wind_speed = jnp.sqrt(slip_east * slip_east + slip_north * slip_north + gust_speed * gust_speed)
    bulk_flux = jnp.stack(
        [
            drag_coeff * wind_speed * slip_east,
            drag_coeff * wind_speed * slip_north,
            heat_coeff * wind_speed * (previous[2] - ground[2]),
        ]
    )
    return jnp.where(ocean_side, ground, bulk_flux) * sea_float


def substep(padded, mask_out, top_row, total_rows, level_coef):
    center = padded[:, :, 1:-1, 1:-1]
    north = padded[:, :, 2:, 1:-1]
    south = padded[:, :, :-2, 1:-1]
    east = padded[:, :, 1:-1, 2:]
    west = padded[:, :, 1:-1, :-2]
    diffuse = level_coef[0][None, :, None, None]
    advect_east = level_coef[1][None, :, None, None]
    advect_north = level_coef[2][None, :, None, None]
    mixing = level_coef[3][None, :, None, None]
    laplace = north + south + east + west - 4.0 * center
    above = jnp.concatenate([center[:, 1:], center[:, -1:]], 1)
    below = jnp.concatenate([center[:, :1], center[:, :-1]], 1)
    height = center.shape[2]
    row_index = top_row + jnp.arange(height, dtype=jnp.int32)
    latitude = jnp.pi * (
        -1.0 / 3.0 + 2.0 / 3.0 * (row_index.astype(center.dtype) + 0.5) / total_rows
    )
    coriolis = (coriolis_scale * jnp.sin(latitude))[:, None]
    turning = jnp.stack([coriolis * center[1], -coriolis * center[0], jnp.zeros_like(center[2])])
    inside = ((row_index >= 0) & (row_index < total_rows)).astype(center.dtype)[:, None]
    updated = (
        center
        + diffuse * laplace
        - advect_east * (east - west)
        - advect_north * (north - south)
        + mixing * (above + below - 2.0 * center)
        + turning
    )
    return updated * (mask_out * inside)


def body(
    state,
    surface,
    sea_mask,
    coeffs,
    remap_weights,
    link_dest,
    link_src_row,
    link_dst_row,
    link_tile,
):
    fields = state[0]
    previous = surface[0]
    sea_float = sea_mask[0].astype(jnp.float32)
    level_coef = coeffs[0]
    tile_table = remap_weights[0]
    field_count, level_count, row_count, col_count = fields.shape
    tile_count = tile_table.shape[0]
    ocean_side = lax.axis_index("grp") == 1
    first_row = lax.axis_index("lat") * row_count
    total_rows = row_count * lax.axis_size("lat")
    peer_count = lax.axis_size("lat") * lax.axis_size("lon")
    width = field_count * col_count

    exported = surface_export(fields[:, 0], previous, sea_float, ocean_side)
    combos = jnp.einsum("crx,txy->trcy", exported, tile_table, precision=HIGHEST)
    combos = combos.reshape(tile_count * row_count, width)
    targets = link_dest[0, :, 0]
    link_count = targets.shape[0]
    slot_count = max(2, 2 * link_count // peer_count)
    link_order = jnp.arange(link_count, dtype=jnp.int32)
    earlier_same = (targets[:, None] == targets[None, :]) & (
        link_order[None, :] < link_order[:, None]
    )
    link_rank = jnp.sum(earlier_same.astype(jnp.int32), axis=1)
    position = targets * slot_count + link_rank
    slot_ids = jnp.arange(peer_count * slot_count, dtype=jnp.int32)
    in_slot = (position[None, :] == slot_ids[:, None]).astype(jnp.int32)
    picked = link_tile[0] * row_count + link_src_row[0]
    slot_pick = jnp.sum(in_slot * (picked + 1)[None, :], axis=1) - 1
    slot_row = jnp.sum(in_slot * (link_dst_row[0] + 1)[None, :], axis=1) - 1
    chooser = (
        slot_pick[:, None] == jnp.arange(tile_count * row_count, dtype=jnp.int32)[None, :]
    ).astype(jnp.float32)
    outgoing = jnp.dot(chooser, combos, precision=HIGHEST)
    row_tags = jnp.zeros((peer_count, 1, width), jnp.float32)
    row_tags = row_tags.at[:, 0, :slot_count].set(
        slot_row.reshape(peer_count, slot_count).astype(jnp.float32)
    )
    outgoing = jnp.concatenate(
        [outgoing.reshape(peer_count, slot_count, width), row_tags], axis=1
    ).reshape(peer_count * (slot_count + 1), width)
    arrived = lax.all_to_all(outgoing, ("lat", "lon"), split_axis=0, concat_axis=0, tiled=True)
    arrived = arrived.reshape(peer_count, slot_count + 1, width)
    arrived_rows = arrived[:, slot_count, :slot_count].reshape(-1)
    arrived_pieces = arrived[:, :slot_count, :].reshape(peer_count * slot_count, width)
    selector = (
        arrived_rows[None, :] == jnp.arange(row_count, dtype=jnp.float32)[:, None]
    ).astype(jnp.float32)
    summed_here = jnp.dot(selector, arrived_pieces, precision=HIGHEST)
    summed_here = summed_here.reshape(row_count, field_count, col_count).transpose(1, 0, 2)
    imported = lax.ppermute(summed_here, "grp", [(0, 1), (1, 0)]) * sea_float

    gain = jnp.where(ocean_side, ocean_gain, air_gain)
    damping = jnp.where(ocean_side, 0.0, air_gain)
    ground = fields[:, 0] + sea_float * (gain * previous - damping * fields[:, 0])
    fields = jnp.concatenate([ground[:, None], fields[:, 1:]], 1)
    state_mask = jnp.where(ocean_side, sea_float, jnp.ones_like(sea_float))
    planes = jnp.concatenate(
        [fields.reshape(field_count * level_count, row_count, col_count), state_mask[None]], 0
    )
    planes = with_halo(planes, SUBSTEPS)
    mask_wide = planes[-1]
    fields = planes[:-1].reshape(
        field_count, level_count, row_count + 2 * SUBSTEPS, col_count + 2 * SUBSTEPS
    )
    for substep_index in range(SUBSTEPS):
        halo = SUBSTEPS - substep_index - 1
        edge = substep_index + 1
        mask_out = mask_wide[edge : mask_wide.shape[0] - edge, edge : mask_wide.shape[1] - edge]
        fields = substep(fields, mask_out, first_row - halo, total_rows, level_coef)
    return (fields[None], imported[None])


def solution(mesh):
    placed = (
        P("grp", None, None, "lat", "lon"),
        P("grp", None, "lat", "lon"),
        P("grp", "lat", "lon"),
        P("grp", None, None),
        P("grp", None, None, None),
        P("grp", ("lat", "lon"), None),
        P("grp", ("lat", "lon")),
        P("grp", ("lat", "lon")),
        P("grp", ("lat", "lon")),
    )
    return jax.shard_map(
        body,
        mesh=mesh,
        in_specs=placed,
        out_specs=(P("grp", None, None, "lat", "lon"), P("grp", None, "lat", "lon")),
        check_vma=False,
    )
```

```python
import jax
import jax.numpy as jnp
from jax import lax
from jax.sharding import PartitionSpec as P
from jax.experimental import pallas as pl
from jax.experimental.pallas import tpu as pltpu

SUBSTEPS = 2


air_gain = 0.3
ocean_gain = 0.5
drag_coeff = 0.5
heat_coeff = 0.5
gust_speed = 0.5
coriolis_scale = 0.25

HIGHEST = lax.Precision.HIGHEST
INTERPRET = False


def shifted(part, axis, closed, forward):
    count = lax.axis_size(axis)
    ends = count if closed else count - 1
    if forward:
        route = [(i, (i + 1) % count) for i in range(ends)]
    else:
        route = [((i + 1) % count, i) for i in range(ends)]
    flat = lax.ppermute(part.reshape(-1), axis, route)
    return flat.reshape(part.shape)


def with_halo(cells, width, wide_cols, wide_rows):
    planes, rows, cols = cells.shape
    head = cells[:, :, :width]
    tail = cells[:, :, -width:]
    gap = jnp.zeros((planes, rows, wide_cols - cols - 2 * width), cells.dtype)
    cells = jnp.concatenate(
        [cells, shifted(head, "lon", True, False), gap, shifted(tail, "lon", True, True)], axis=2
    )
    head = cells[:, :width, :]
    tail = cells[:, rows - width : rows, :]
    gap = jnp.zeros((planes, wide_rows - rows - 2 * width, wide_cols), cells.dtype)
    return jnp.concatenate(
        [cells, shifted(head, "lat", False, False), gap, shifted(tail, "lat", False, True)], axis=1
    )


def stencil_kernel(coef_ref, row_ref, wide_ref, out_ref, mid_ref):
    field_count, level_count, row_count, col_count = out_ref.shape[1:]
    wide_rows, wide_cols = wide_ref.shape[1:]
    turning = row_ref[0]
    keep = wide_ref[field_count * level_count] * row_ref[1]

    def step(read, write):
        for field in range(field_count):
            for level in range(level_count):
                diffuse = coef_ref[0, 0, level]
                advect_east = coef_ref[0, 1, level]
                advect_north = coef_ref[0, 2, level]
                mixing = coef_ref[0, 3, level]
                center = read(field, level)
                north = pltpu.roll(center, wide_rows - 1, 0)
                south = pltpu.roll(center, 1, 0)
                east = pltpu.roll(center, wide_cols - 1, 1)
                west = pltpu.roll(center, 1, 1)
                above = read(field, min(level + 1, level_count - 1))
                below = read(field, max(level - 1, 0))
                laplace = north + south + east + west - 4.0 * center
                updated = (
                    center
                    + diffuse * laplace
                    - advect_east * (east - west)
                    - advect_north * (north - south)
                    + mixing * (above + below - 2.0 * center)
                )
                if field == 0:
                    updated = updated + turning * read(1, level)
                elif field == 1:
                    updated = updated + (-turning) * read(0, level)
                write(field, level, updated * keep)

    def from_wide(field, level):
        return wide_ref[field * level_count + level]

    def to_mid(field, level, value):
        mid_ref[field * level_count + level] = value

    def from_mid(field, level):
        return mid_ref[field * level_count + level]

    def to_out(field, level, value):
        out_ref[0, field, level] = value[:row_count, :col_count]

    step(from_wide, to_mid)
    step(from_mid, to_out)


def dynamics(coeffs, row_terms, wide, field_count, level_count, row_count, col_count):
    planes, wide_rows, wide_cols = wide.shape
    return pl.pallas_call(
        stencil_kernel,
        out_shape=jax.ShapeDtypeStruct((1, field_count, level_count, row_count, col_count), jnp.float32),
        in_specs=[
            pl.BlockSpec(memory_space=pltpu.SMEM),
            pl.BlockSpec(memory_space=pltpu.VMEM),
            pl.BlockSpec(memory_space=pltpu.VMEM),
        ],
        out_specs=pl.BlockSpec(memory_space=pltpu.VMEM),
        scratch_shapes=[pltpu.VMEM((planes - 1, wide_rows, wide_cols), jnp.float32)],
        interpret=INTERPRET,
    )(coeffs, row_terms, wide)


def surface_export(ground, previous, sea_float, ocean_side):
    slip_east = ground[0] - previous[0]
    slip_north = ground[1] - previous[1]
    wind_speed = jnp.sqrt(slip_east * slip_east + slip_north * slip_north + gust_speed * gust_speed)
    bulk_flux = jnp.stack(
        [
            drag_coeff * wind_speed * slip_east,
            drag_coeff * wind_speed * slip_north,
            heat_coeff * wind_speed * (previous[2] - ground[2]),
        ]
    )
    return jnp.where(ocean_side, ground, bulk_flux) * sea_float


def body(
    state,
    surface,
    sea_mask,
    coeffs,
    remap_weights,
    link_dest,
    link_src_row,
    link_dst_row,
    link_tile,
):
    fields = state[0]
    previous = surface[0]
    sea_float = sea_mask[0].astype(jnp.float32)
    level_coef = coeffs[0]
    tile_table = remap_weights[0]
    field_count, level_count, row_count, col_count = fields.shape
    tile_count = tile_table.shape[0]
    ocean_side = lax.axis_index("grp") == 1
    first_row = lax.axis_index("lat") * row_count
    total_rows = row_count * lax.axis_size("lat")
    peer_count = lax.axis_size("lat") * lax.axis_size("lon")
    width = field_count * col_count

    exported = surface_export(fields[:, 0], previous, sea_float, ocean_side)
    combos = jnp.einsum("crx,txy->trcy", exported, tile_table, precision=HIGHEST)
    combos = combos.reshape(tile_count * row_count, width)
    targets = link_dest[0, :, 0]
    link_count = targets.shape[0]
    slot_count = max(2, 2 * link_count // peer_count)
    link_order = jnp.arange(link_count, dtype=jnp.int32)
    earlier_same = (targets[:, None] == targets[None, :]) & (
        link_order[None, :] < link_order[:, None]
    )
    link_rank = jnp.sum(earlier_same.astype(jnp.int32), axis=1)
    position = targets * slot_count + link_rank
    slot_ids = jnp.arange(peer_count * slot_count, dtype=jnp.int32)
    in_slot = (position[None, :] == slot_ids[:, None]).astype(jnp.int32)
    picked = link_tile[0] * row_count + link_src_row[0]
    slot_pick = jnp.sum(in_slot * (picked + 1)[None, :], axis=1) - 1
    slot_row = jnp.sum(in_slot * (link_dst_row[0] + 1)[None, :], axis=1) - 1
    chooser = (
        slot_pick[:, None] == jnp.arange(tile_count * row_count, dtype=jnp.int32)[None, :]
    ).astype(jnp.float32)
    outgoing = jnp.dot(chooser, combos, precision=HIGHEST)
    row_tags = jnp.zeros((peer_count, 1, width), jnp.float32)
    row_tags = row_tags.at[:, 0, :slot_count].set(
        slot_row.reshape(peer_count, slot_count).astype(jnp.float32)
    )
    outgoing = jnp.concatenate(
        [outgoing.reshape(peer_count, slot_count, width), row_tags], axis=1
    ).reshape(peer_count * (slot_count + 1), width)
    arrived = lax.all_to_all(outgoing, ("lat", "lon"), split_axis=0, concat_axis=0, tiled=True)
    arrived = arrived.reshape(peer_count, slot_count + 1, width)
    arrived_rows = arrived[:, slot_count, :slot_count].reshape(-1)
    arrived_pieces = arrived[:, :slot_count, :].reshape(peer_count * slot_count, width)
    selector = (
        arrived_rows[None, :] == jnp.arange(row_count, dtype=jnp.float32)[:, None]
    ).astype(jnp.float32)
    summed_here = jnp.dot(selector, arrived_pieces, precision=HIGHEST)
    summed_here = summed_here.reshape(row_count, field_count, col_count).transpose(1, 0, 2)
    imported = lax.ppermute(summed_here, "grp", [(0, 1), (1, 0)]) * sea_float

    gain = jnp.where(ocean_side, ocean_gain, air_gain)
    damping = jnp.where(ocean_side, 0.0, air_gain)
    ground = fields[:, 0] + sea_float * (gain * previous - damping * fields[:, 0])
    fields = jnp.concatenate([ground[:, None], fields[:, 1:]], 1)
    state_mask = jnp.where(ocean_side, sea_float, jnp.ones_like(sea_float))
    planes = jnp.concatenate(
        [fields.reshape(field_count * level_count, row_count, col_count), state_mask[None]], 0
    )
    wide_rows = -(-(row_count + 4 * SUBSTEPS) // 8) * 8
    wide_cols = -(-(col_count + 4 * SUBSTEPS) // 128) * 128
    wide = with_halo(planes, SUBSTEPS, wide_cols, wide_rows)
    local = jnp.arange(wide_rows, dtype=jnp.int32)
    row_index = first_row + jnp.where(local < wide_rows // 2 + row_count // 2, local, local - wide_rows)
    latitude = jnp.pi * (
        -1.0 / 3.0 + 2.0 / 3.0 * (row_index.astype(jnp.float32) + 0.5) / total_rows
    )
    coriolis = coriolis_scale * jnp.sin(latitude)
    inside = ((row_index >= 0) & (row_index < total_rows)).astype(jnp.float32)
    row_terms = jnp.broadcast_to(jnp.stack([coriolis, inside])[:, :, None], (2, wide_rows, wide_cols))
    fields = dynamics(coeffs, row_terms, wide, field_count, level_count, row_count, col_count)
    return (fields, imported[None])


def solution(mesh):
    placed = (
        P("grp", None, None, "lat", "lon"),
        P("grp", None, "lat", "lon"),
        P("grp", "lat", "lon"),
        P("grp", None, None),
        P("grp", None, None, None),
        P("grp", ("lat", "lon"), None),
        P("grp", ("lat", "lon")),
        P("grp", ("lat", "lon")),
        P("grp", ("lat", "lon")),
    )
    return jax.shard_map(
        body,
        mesh=mesh,
        in_specs=placed,
        out_specs=(P("grp", None, None, "lat", "lon"), P("grp", None, "lat", "lon")),
        check_vma=False,
    )
```

```python
import jax
import jax.numpy as jnp
from jax import lax
from jax.sharding import PartitionSpec as P
from jax.experimental import pallas as pl
from jax.experimental.pallas import tpu as pltpu

SUBSTEPS = 2


air_gain = 0.3
ocean_gain = 0.5
drag_coeff = 0.5
heat_coeff = 0.5
gust_speed = 0.5
coriolis_scale = 0.25

HIGHEST = lax.Precision.HIGHEST
INTERPRET = False


def shifted(part, axis, closed, forward):
    count = lax.axis_size(axis)
    ends = count if closed else count - 1
    if forward:
        route = [(i, (i + 1) % count) for i in range(ends)]
    else:
        route = [((i + 1) % count, i) for i in range(ends)]
    flat = lax.ppermute(part.reshape(-1), axis, route)
    return flat.reshape(part.shape)


def with_halo(cells, width, wide_cols, wide_rows):
    planes, rows, cols = cells.shape
    head = cells[:, :, :width]
    tail = cells[:, :, -width:]
    gap = jnp.zeros((planes, rows, wide_cols - cols - 2 * width), cells.dtype)
    cells = jnp.concatenate(
        [cells, shifted(head, "lon", True, False), gap, shifted(tail, "lon", True, True)], axis=2
    )
    head = cells[:, :width, :]
    tail = cells[:, rows - width : rows, :]
    gap = jnp.zeros((planes, wide_rows - rows - 2 * width, wide_cols), cells.dtype)
    return jnp.concatenate(
        [cells, shifted(head, "lat", False, False), gap, shifted(tail, "lat", False, True)], axis=1
    )


def stencil_kernel(coef_ref, row_ref, wide_ref, out_ref, mid_ref):
    field_count, level_count, row_count, col_count = out_ref.shape[1:]
    wide_rows, wide_cols = wide_ref.shape[1:]
    turning = row_ref[0]
    keep = wide_ref[field_count * level_count] * row_ref[1]

    def step(read, write):
        for field in range(field_count):
            for level in range(level_count):
                diffuse = coef_ref[0, 0, level]
                advect_east = coef_ref[0, 1, level]
                advect_north = coef_ref[0, 2, level]
                mixing = coef_ref[0, 3, level]
                center = read(field, level)
                north = pltpu.roll(center, wide_rows - 1, 0)
                south = pltpu.roll(center, 1, 0)
                east = pltpu.roll(center, wide_cols - 1, 1)
                west = pltpu.roll(center, 1, 1)
                above = read(field, min(level + 1, level_count - 1))
                below = read(field, max(level - 1, 0))
                laplace = north + south + east + west - 4.0 * center
                updated = (
                    center
                    + diffuse * laplace
                    - advect_east * (east - west)
                    - advect_north * (north - south)
                    + mixing * (above + below - 2.0 * center)
                )
                if field == 0:
                    updated = updated + turning * read(1, level)
                elif field == 1:
                    updated = updated + (-turning) * read(0, level)
                write(field, level, updated * keep)

    def from_wide(field, level):
        return wide_ref[field * level_count + level]

    def to_mid(field, level, value):
        mid_ref[field * level_count + level] = value

    def from_mid(field, level):
        return mid_ref[field * level_count + level]

    def to_out(field, level, value):
        out_ref[0, field, level] = value[:row_count, :col_count]

    step(from_wide, to_mid)
    step(from_mid, to_out)


def dynamics(coeffs, row_terms, wide, field_count, level_count, row_count, col_count):
    planes, wide_rows, wide_cols = wide.shape
    return pl.pallas_call(
        stencil_kernel,
        out_shape=jax.ShapeDtypeStruct((1, field_count, level_count, row_count, col_count), jnp.float32),
        in_specs=[
            pl.BlockSpec(memory_space=pltpu.SMEM),
            pl.BlockSpec(memory_space=pltpu.VMEM),
            pl.BlockSpec(memory_space=pltpu.VMEM),
        ],
        out_specs=pl.BlockSpec(memory_space=pltpu.VMEM),
        scratch_shapes=[pltpu.VMEM((planes - 1, wide_rows, wide_cols), jnp.float32)],
        interpret=INTERPRET,
    )(coeffs, row_terms, wide)


def gather_kernel(arrived_ref, out_ref):
    peer_count, tagged, width = arrived_ref.shape
    slot_count = tagged - 1
    field_count, row_count, col_count = out_ref.shape
    row_ids = lax.broadcasted_iota(jnp.int32, (row_count, slot_count), 0).astype(jnp.float32)

    def one_peer(peer, total):
        block = arrived_ref[peer]
        selector = (block[slot_count : slot_count + 1, :slot_count] == row_ids).astype(jnp.float32)
        return total + jnp.dot(
            selector, block[:slot_count, :], precision=HIGHEST, preferred_element_type=jnp.float32
        )

    total = lax.fori_loop(
        0, peer_count, one_peer, jnp.zeros((row_count, width), jnp.float32), unroll=peer_count <= 16
    )
    for field in range(field_count):
        out_ref[field] = total[:, field * col_count : (field + 1) * col_count]


def gathered(arrived, field_count, row_count, col_count):
    return pl.pallas_call(
        gather_kernel,
        out_shape=jax.ShapeDtypeStruct((field_count, row_count, col_count), jnp.float32),
        in_specs=[pl.BlockSpec(memory_space=pltpu.VMEM)],
        out_specs=pl.BlockSpec(memory_space=pltpu.VMEM),
        interpret=INTERPRET,
    )(arrived)


def surface_export(ground, previous, sea_float, ocean_side):
    slip_east = ground[0] - previous[0]
    slip_north = ground[1] - previous[1]
    wind_speed = jnp.sqrt(slip_east * slip_east + slip_north * slip_north + gust_speed * gust_speed)
    bulk_flux = jnp.stack(
        [
            drag_coeff * wind_speed * slip_east,
            drag_coeff * wind_speed * slip_north,
            heat_coeff * wind_speed * (previous[2] - ground[2]),
        ]
    )
    return jnp.where(ocean_side, ground, bulk_flux) * sea_float


def body(
    state,
    surface,
    sea_mask,
    coeffs,
    remap_weights,
    link_dest,
    link_src_row,
    link_dst_row,
    link_tile,
):
    fields = state[0]
    previous = surface[0]
    sea_float = sea_mask[0].astype(jnp.float32)
    level_coef = coeffs[0]
    tile_table = remap_weights[0]
    field_count, level_count, row_count, col_count = fields.shape
    tile_count = tile_table.shape[0]
    ocean_side = lax.axis_index("grp") == 1
    first_row = lax.axis_index("lat") * row_count
    total_rows = row_count * lax.axis_size("lat")
    peer_count = lax.axis_size("lat") * lax.axis_size("lon")
    width = field_count * col_count

    exported = surface_export(fields[:, 0], previous, sea_float, ocean_side)
    combos = jnp.einsum("crx,txy->trcy", exported, tile_table, precision=HIGHEST)
    combos = combos.reshape(tile_count * row_count, width)
    targets = link_dest[0, :, 0]
    link_count = targets.shape[0]
    slot_count = max(2, 2 * link_count // peer_count)
    link_order = jnp.arange(link_count, dtype=jnp.int32)
    earlier_same = (targets[:, None] == targets[None, :]) & (
        link_order[None, :] < link_order[:, None]
    )
    link_rank = jnp.sum(earlier_same.astype(jnp.int32), axis=1)
    position = targets * slot_count + link_rank
    slot_ids = jnp.arange(peer_count * slot_count, dtype=jnp.int32)
    in_slot = (position[None, :] == slot_ids[:, None]).astype(jnp.int32)
    picked = link_tile[0] * row_count + link_src_row[0]
    slot_pick = jnp.sum(in_slot * (picked + 1)[None, :], axis=1) - 1
    slot_row = jnp.sum(in_slot * (link_dst_row[0] + 1)[None, :], axis=1) - 1
    chooser = (
        slot_pick[:, None] == jnp.arange(tile_count * row_count, dtype=jnp.int32)[None, :]
    ).astype(jnp.float32)
    outgoing = jnp.dot(chooser, combos, precision=HIGHEST)
    row_tags = jnp.zeros((peer_count, 1, width), jnp.float32)
    row_tags = row_tags.at[:, 0, :slot_count].set(
        slot_row.reshape(peer_count, slot_count).astype(jnp.float32)
    )
    outgoing = jnp.concatenate(
        [outgoing.reshape(peer_count, slot_count, width), row_tags], axis=1
    ).reshape(peer_count * (slot_count + 1), width)
    arrived = lax.all_to_all(outgoing, ("lat", "lon"), split_axis=0, concat_axis=0, tiled=True)
    arrived = arrived.reshape(peer_count, slot_count + 1, width)
    summed_here = gathered(arrived, field_count, row_count, col_count)
    imported = lax.ppermute(summed_here, "grp", [(0, 1), (1, 0)]) * sea_float

    gain = jnp.where(ocean_side, ocean_gain, air_gain)
    damping = jnp.where(ocean_side, 0.0, air_gain)
    ground = fields[:, 0] + sea_float * (gain * previous - damping * fields[:, 0])
    fields = jnp.concatenate([ground[:, None], fields[:, 1:]], 1)
    state_mask = jnp.where(ocean_side, sea_float, jnp.ones_like(sea_float))
    planes = jnp.concatenate(
        [fields.reshape(field_count * level_count, row_count, col_count), state_mask[None]], 0
    )
    wide_rows = -(-(row_count + 4 * SUBSTEPS) // 8) * 8
    wide_cols = -(-(col_count + 4 * SUBSTEPS) // 128) * 128
    wide = with_halo(planes, SUBSTEPS, wide_cols, wide_rows)
    local = jnp.arange(wide_rows, dtype=jnp.int32)
    row_index = first_row + jnp.where(local < wide_rows // 2 + row_count // 2, local, local - wide_rows)
    latitude = jnp.pi * (
        -1.0 / 3.0 + 2.0 / 3.0 * (row_index.astype(jnp.float32) + 0.5) / total_rows
    )
    coriolis = coriolis_scale * jnp.sin(latitude)
    inside = ((row_index >= 0) & (row_index < total_rows)).astype(jnp.float32)
    row_terms = jnp.broadcast_to(jnp.stack([coriolis, inside])[:, :, None], (2, wide_rows, wide_cols))
    fields = dynamics(coeffs, row_terms, wide, field_count, level_count, row_count, col_count)
    return (fields, imported[None])


def solution(mesh):
    placed = (
        P("grp", None, None, "lat", "lon"),
        P("grp", None, "lat", "lon"),
        P("grp", "lat", "lon"),
        P("grp", None, None),
        P("grp", None, None, None),
        P("grp", ("lat", "lon"), None),
        P("grp", ("lat", "lon")),
        P("grp", ("lat", "lon")),
        P("grp", ("lat", "lon")),
    )
    return jax.shard_map(
        body,
        mesh=mesh,
        in_specs=placed,
        out_specs=(P("grp", None, None, "lat", "lon"), P("grp", None, "lat", "lon")),
        check_vma=False,
    )
```

```python
import jax
import jax.numpy as jnp
from jax import lax
from jax.sharding import PartitionSpec as P
from jax.experimental import pallas as pl
from jax.experimental.pallas import tpu as pltpu

SUBSTEPS = 2


air_gain = 0.3
ocean_gain = 0.5
drag_coeff = 0.5
heat_coeff = 0.5
gust_speed = 0.5
coriolis_scale = 0.25

HIGHEST = lax.Precision.HIGHEST
INTERPRET = False


def shifted(part, axis, closed, forward):
    count = lax.axis_size(axis)
    ends = count if closed else count - 1
    if forward:
        route = [(i, (i + 1) % count) for i in range(ends)]
    else:
        route = [((i + 1) % count, i) for i in range(ends)]
    flat = lax.ppermute(part.reshape(-1), axis, route)
    return flat.reshape(part.shape)


def with_halo(cells, width, wide_cols, wide_rows):
    planes, rows, cols = cells.shape
    head = cells[:, :, :width]
    tail = cells[:, :, -width:]
    gap = jnp.zeros((planes, rows, wide_cols - cols - 2 * width), cells.dtype)
    cells = jnp.concatenate(
        [cells, shifted(head, "lon", True, False), gap, shifted(tail, "lon", True, True)], axis=2
    )
    head = cells[:, :width, :]
    tail = cells[:, rows - width : rows, :]
    gap = jnp.zeros((planes, wide_rows - rows - 2 * width, wide_cols), cells.dtype)
    return jnp.concatenate(
        [cells, shifted(head, "lat", False, False), gap, shifted(tail, "lat", False, True)], axis=1
    )


def stencil_kernel(coef_ref, row_ref, wide_ref, out_ref, mid_ref):
    field_count, level_count, row_count, col_count = out_ref.shape[1:]
    wide_rows, wide_cols = wide_ref.shape[1:]
    turning = row_ref[0]
    keep = wide_ref[field_count * level_count] * row_ref[1]

    def step(read, write):
        for field in range(field_count):
            for level in range(level_count):
                diffuse = coef_ref[0, 0, level]
                advect_east = coef_ref[0, 1, level]
                advect_north = coef_ref[0, 2, level]
                mixing = coef_ref[0, 3, level]
                center = read(field, level)
                north = pltpu.roll(center, wide_rows - 1, 0)
                south = pltpu.roll(center, 1, 0)
                east = pltpu.roll(center, wide_cols - 1, 1)
                west = pltpu.roll(center, 1, 1)
                above = read(field, min(level + 1, level_count - 1))
                below = read(field, max(level - 1, 0))
                laplace = north + south + east + west - 4.0 * center
                updated = (
                    center
                    + diffuse * laplace
                    - advect_east * (east - west)
                    - advect_north * (north - south)
                    + mixing * (above + below - 2.0 * center)
                )
                if field == 0:
                    updated = updated + turning * read(1, level)
                elif field == 1:
                    updated = updated + (-turning) * read(0, level)
                write(field, level, updated * keep)

    def from_wide(field, level):
        return wide_ref[field * level_count + level]

    def to_mid(field, level, value):
        mid_ref[field * level_count + level] = value

    def from_mid(field, level):
        return mid_ref[field * level_count + level]

    def to_out(field, level, value):
        out_ref[0, field, level] = value[:row_count, :col_count]

    step(from_wide, to_mid)
    step(from_mid, to_out)


def dynamics(coeffs, row_terms, wide, field_count, level_count, row_count, col_count):
    planes, wide_rows, wide_cols = wide.shape
    return pl.pallas_call(
        stencil_kernel,
        out_shape=jax.ShapeDtypeStruct((1, field_count, level_count, row_count, col_count), jnp.float32),
        in_specs=[
            pl.BlockSpec(memory_space=pltpu.SMEM),
            pl.BlockSpec(memory_space=pltpu.VMEM),
            pl.BlockSpec(memory_space=pltpu.VMEM),
        ],
        out_specs=pl.BlockSpec(memory_space=pltpu.VMEM),
        scratch_shapes=[pltpu.VMEM((planes - 1, wide_rows, wide_cols), jnp.float32)],
        interpret=INTERPRET,
    )(coeffs, row_terms, wide)


def scatter_kernel(
    flag_ref, ground_ref, previous_ref, sea_ref, table_ref, pick_ref, tag_ref, out_ref, combo_ref, flat_ref
):
    tile_count = table_ref.shape[1]
    field_count, row_count, col_count = previous_ref.shape[1:]
    peer_count, chunk = out_ref.shape[:2]
    buffer_rows = peer_count * chunk
    ground = ground_ref[0, :, 0]
    previous = previous_ref[0]
    sea_float = sea_ref[0].astype(jnp.float32)
    ocean = (flag_ref[0] == 1).astype(jnp.float32)
    slip_east = ground[0] - previous[0]
    slip_north = ground[1] - previous[1]
    wind_speed = jnp.sqrt(slip_east * slip_east + slip_north * slip_north + gust_speed * gust_speed)
    bulk_flux = [
        drag_coeff * wind_speed * slip_east,
        drag_coeff * wind_speed * slip_north,
        heat_coeff * wind_speed * (previous[2] - ground[2]),
    ]
    exported = jnp.concatenate(
        [(ground[c] * ocean + bulk_flux[c] * (1.0 - ocean)) * sea_float for c in range(field_count)], 0
    )
    for tile in range(tile_count):
        weighted = jnp.dot(
            exported, table_ref[0, tile], precision=HIGHEST, preferred_element_type=jnp.float32
        )
        for c in range(field_count):
            combo_ref[c, tile * row_count : (tile + 1) * row_count, :] = weighted[
                c * row_count : (c + 1) * row_count
            ]
    chooser = (
        pick_ref[...] == lax.broadcasted_iota(jnp.int32, (buffer_rows, tile_count * row_count), 1)
    ).astype(jnp.float32)
    tag_rows = (
        lax.broadcasted_iota(jnp.int32, (buffer_rows, peer_count), 0)
        == lax.broadcasted_iota(jnp.int32, (buffer_rows, peer_count), 1) * chunk + (chunk - 1)
    ).astype(jnp.float32)
    tags = jnp.dot(tag_rows, tag_ref[...], precision=HIGHEST, preferred_element_type=jnp.float32)
    tag_width = tag_ref.shape[1]
    for c in range(field_count):
        picked = jnp.dot(chooser, combo_ref[c], precision=HIGHEST, preferred_element_type=jnp.float32)
        if c == 0:
            flat_ref[:, :tag_width] = picked[:, :tag_width] + tags
            flat_ref[:, tag_width:col_count] = picked[:, tag_width:]
        else:
            flat_ref[:, c * col_count : (c + 1) * col_count] = picked
    for peer in range(peer_count):
        out_ref[peer] = flat_ref[peer * chunk : (peer + 1) * chunk, :]


def scattered(flag, state, surface, sea_mask, remap_weights, pick, tags):
    field_count, row_count, col_count = surface.shape[1:]
    tile_count = remap_weights.shape[1]
    vmem = pl.BlockSpec(memory_space=pltpu.VMEM)
    return pl.pallas_call(
        scatter_kernel,
        out_shape=jax.ShapeDtypeStruct(
            (tags.shape[0], pick.shape[0] // tags.shape[0], field_count * col_count), jnp.float32
        ),
        in_specs=[
            pl.BlockSpec(memory_space=pltpu.SMEM),
            pl.BlockSpec((1, field_count, 1, row_count, col_count), lambda i: (0, 0, 0, 0, 0)),
            vmem,
            vmem,
            vmem,
            vmem,
            vmem,
        ],
        out_specs=vmem,
        grid=(1,),
        scratch_shapes=[
            pltpu.VMEM((field_count, tile_count * row_count, col_count), jnp.float32),
            pltpu.VMEM((pick.shape[0], field_count * col_count), jnp.float32),
        ],
        interpret=INTERPRET,
    )(flag, state, surface, sea_mask, remap_weights, pick, tags)


def gather_kernel(arrived_ref, out_ref):
    peer_count, tagged, width = arrived_ref.shape
    slot_count = tagged - 1
    field_count, row_count, col_count = out_ref.shape
    row_ids = lax.broadcasted_iota(jnp.int32, (row_count, slot_count), 0).astype(jnp.float32)

    def one_peer(peer, total):
        block = arrived_ref[peer]
        selector = (block[slot_count : slot_count + 1, :slot_count] == row_ids).astype(jnp.float32)
        return total + jnp.dot(
            selector, block[:slot_count, :], precision=HIGHEST, preferred_element_type=jnp.float32
        )

    total = lax.fori_loop(
        0, peer_count, one_peer, jnp.zeros((row_count, width), jnp.float32), unroll=peer_count <= 16
    )
    for field in range(field_count):
        out_ref[field] = total[:, field * col_count : (field + 1) * col_count]


def gathered(arrived, field_count, row_count, col_count):
    return pl.pallas_call(
        gather_kernel,
        out_shape=jax.ShapeDtypeStruct((field_count, row_count, col_count), jnp.float32),
        in_specs=[pl.BlockSpec(memory_space=pltpu.VMEM)],
        out_specs=pl.BlockSpec(memory_space=pltpu.VMEM),
        interpret=INTERPRET,
    )(arrived)


def surface_export(ground, previous, sea_float, ocean_side):
    slip_east = ground[0] - previous[0]
    slip_north = ground[1] - previous[1]
    wind_speed = jnp.sqrt(slip_east * slip_east + slip_north * slip_north + gust_speed * gust_speed)
    bulk_flux = jnp.stack(
        [
            drag_coeff * wind_speed * slip_east,
            drag_coeff * wind_speed * slip_north,
            heat_coeff * wind_speed * (previous[2] - ground[2]),
        ]
    )
    return jnp.where(ocean_side, ground, bulk_flux) * sea_float


def body(
    state,
    surface,
    sea_mask,
    coeffs,
    remap_weights,
    link_dest,
    link_src_row,
    link_dst_row,
    link_tile,
):
    fields = state[0]
    previous = surface[0]
    sea_float = sea_mask[0].astype(jnp.float32)
    level_coef = coeffs[0]
    tile_table = remap_weights[0]
    field_count, level_count, row_count, col_count = fields.shape
    tile_count = tile_table.shape[0]
    ocean_side = lax.axis_index("grp") == 1
    first_row = lax.axis_index("lat") * row_count
    total_rows = row_count * lax.axis_size("lat")
    peer_count = lax.axis_size("lat") * lax.axis_size("lon")
    width = field_count * col_count

    targets = link_dest[0, :, 0]
    link_count = targets.shape[0]
    slot_count = max(2, 2 * link_count // peer_count)
    chunk = slot_count + 1
    link_order = jnp.arange(link_count, dtype=jnp.int32)
    earlier_same = (targets[:, None] == targets[None, :]) & (
        link_order[None, :] < link_order[:, None]
    )
    link_rank = jnp.sum(earlier_same.astype(jnp.int32), axis=1)
    position = targets * chunk + link_rank
    buffer_ids = jnp.arange(peer_count * chunk, dtype=jnp.int32)
    in_slot = (position[None, :] == buffer_ids[:, None]).astype(jnp.int32)
    picked = link_tile[0] * row_count + link_src_row[0]
    slot_pick = jnp.sum(in_slot * (picked + 1)[None, :], axis=1) - 1
    slot_row = jnp.sum(in_slot * (link_dst_row[0] + 1)[None, :], axis=1) - 1
    slot_row = slot_row.reshape(peer_count, chunk)[:, :slot_count].astype(jnp.float32)
    tag_width = 128
    tags = jnp.pad(slot_row, ((0, 0), (0, tag_width - slot_count)))
    flag = lax.axis_index("grp").astype(jnp.int32).reshape(1)
    outgoing = scattered(
        flag, state, surface, sea_mask, remap_weights, slot_pick.reshape(-1, 1), tags
    )
    arrived = lax.all_to_all(outgoing, ("lat", "lon"), split_axis=0, concat_axis=0, tiled=True)
    arrived = arrived.reshape(peer_count, slot_count + 1, width)
    summed_here = gathered(arrived, field_count, row_count, col_count)
    imported = lax.ppermute(summed_here, "grp", [(0, 1), (1, 0)]) * sea_float

    gain = jnp.where(ocean_side, ocean_gain, air_gain)
    damping = jnp.where(ocean_side, 0.0, air_gain)
    ground = fields[:, 0] + sea_float * (gain * previous - damping * fields[:, 0])
    fields = jnp.concatenate([ground[:, None], fields[:, 1:]], 1)
    state_mask = jnp.where(ocean_side, sea_float, jnp.ones_like(sea_float))
    planes = jnp.concatenate(
        [fields.reshape(field_count * level_count, row_count, col_count), state_mask[None]], 0
    )
    wide_rows = -(-(row_count + 4 * SUBSTEPS) // 8) * 8
    wide_cols = -(-(col_count + 4 * SUBSTEPS) // 128) * 128
    wide = with_halo(planes, SUBSTEPS, wide_cols, wide_rows)
    local = jnp.arange(wide_rows, dtype=jnp.int32)
    row_index = first_row + jnp.where(local < wide_rows // 2 + row_count // 2, local, local - wide_rows)
    latitude = jnp.pi * (
        -1.0 / 3.0 + 2.0 / 3.0 * (row_index.astype(jnp.float32) + 0.5) / total_rows
    )
    coriolis = coriolis_scale * jnp.sin(latitude)
    inside = ((row_index >= 0) & (row_index < total_rows)).astype(jnp.float32)
    row_terms = jnp.broadcast_to(jnp.stack([coriolis, inside])[:, :, None], (2, wide_rows, wide_cols))
    fields = dynamics(coeffs, row_terms, wide, field_count, level_count, row_count, col_count)
    return (fields, imported[None])


def solution(mesh):
    placed = (
        P("grp", None, None, "lat", "lon"),
        P("grp", None, "lat", "lon"),
        P("grp", "lat", "lon"),
        P("grp", None, None),
        P("grp", None, None, None),
        P("grp", ("lat", "lon"), None),
        P("grp", ("lat", "lon")),
        P("grp", ("lat", "lon")),
        P("grp", ("lat", "lon")),
    )
    return jax.shard_map(
        body,
        mesh=mesh,
        in_specs=placed,
        out_specs=(P("grp", None, None, "lat", "lon"), P("grp", None, "lat", "lon")),
        check_vma=False,
    )
```

```python
import functools

import jax
import jax.numpy as jnp
from jax import lax
from jax.sharding import PartitionSpec as P
from jax.experimental import pallas as pl
from jax.experimental.pallas import tpu as pltpu

SUBSTEPS = 2


air_gain = 0.3
ocean_gain = 0.5
drag_coeff = 0.5
heat_coeff = 0.5
gust_speed = 0.5
coriolis_scale = 0.25

HIGHEST = lax.Precision.HIGHEST
INTERPRET = False


def shifted(part, axis, closed, forward):
    count = lax.axis_size(axis)
    ends = count if closed else count - 1
    if forward:
        route = [(i, (i + 1) % count) for i in range(ends)]
    else:
        route = [((i + 1) % count, i) for i in range(ends)]
    flat = lax.ppermute(part.reshape(-1), axis, route)
    return flat.reshape(part.shape)


def with_halo(cells, width, wide_cols, wide_rows):
    planes, rows, cols = cells.shape
    head = cells[:, :, :width]
    tail = cells[:, :, -width:]
    gap = jnp.zeros((planes, rows, wide_cols - cols - 2 * width), cells.dtype)
    cells = jnp.concatenate(
        [cells, shifted(head, "lon", True, False), gap, shifted(tail, "lon", True, True)], axis=2
    )
    head = cells[:, :width, :]
    tail = cells[:, rows - width : rows, :]
    gap = jnp.zeros((planes, wide_rows - rows - 2 * width, wide_cols), cells.dtype)
    return jnp.concatenate(
        [cells, shifted(head, "lat", False, False), gap, shifted(tail, "lat", False, True)], axis=1
    )


def stencil_kernel(coef_ref, row_ref, wide_ref, out_ref, mid_ref):
    field_count, level_count, row_count, col_count = out_ref.shape[1:]
    wide_rows, wide_cols = wide_ref.shape[1:]
    turning = row_ref[0]
    keep = wide_ref[field_count * level_count] * row_ref[1]

    def step(read, write):
        for field in range(field_count):
            for level in range(level_count):
                diffuse = coef_ref[0, 0, level]
                advect_east = coef_ref[0, 1, level]
                advect_north = coef_ref[0, 2, level]
                mixing = coef_ref[0, 3, level]
                center = read(field, level)
                north = pltpu.roll(center, wide_rows - 1, 0)
                south = pltpu.roll(center, 1, 0)
                east = pltpu.roll(center, wide_cols - 1, 1)
                west = pltpu.roll(center, 1, 1)
                above = read(field, min(level + 1, level_count - 1))
                below = read(field, max(level - 1, 0))
                laplace = north + south + east + west - 4.0 * center
                updated = (
                    center
                    + diffuse * laplace
                    - advect_east * (east - west)
                    - advect_north * (north - south)
                    + mixing * (above + below - 2.0 * center)
                )
                if field == 0:
                    updated = updated + turning * read(1, level)
                elif field == 1:
                    updated = updated + (-turning) * read(0, level)
                write(field, level, updated * keep)

    def from_wide(field, level):
        return wide_ref[field * level_count + level]

    def to_mid(field, level, value):
        mid_ref[field * level_count + level] = value

    def from_mid(field, level):
        return mid_ref[field * level_count + level]

    def to_out(field, level, value):
        out_ref[0, field, level] = value[:row_count, :col_count]

    step(from_wide, to_mid)
    step(from_mid, to_out)


def dynamics(coeffs, row_terms, wide, field_count, level_count, row_count, col_count):
    planes, wide_rows, wide_cols = wide.shape
    return pl.pallas_call(
        stencil_kernel,
        out_shape=jax.ShapeDtypeStruct((1, field_count, level_count, row_count, col_count), jnp.float32),
        in_specs=[
            pl.BlockSpec(memory_space=pltpu.SMEM),
            pl.BlockSpec(memory_space=pltpu.VMEM),
            pl.BlockSpec(memory_space=pltpu.VMEM),
        ],
        out_specs=pl.BlockSpec(memory_space=pltpu.VMEM),
        scratch_shapes=[pltpu.VMEM((planes - 1, wide_rows, wide_cols), jnp.float32)],
        interpret=INTERPRET,
    )(coeffs, row_terms, wide)


def export_kernel(flag_ref, ground_ref, previous_ref, sea_ref, link_ref, out_ref):
    field_count, row_count, col_count = previous_ref.shape[1:]
    link_fields, link_count = link_ref.shape
    ground = ground_ref[0, :, 0]
    previous = previous_ref[0]
    sea_float = sea_ref[0].astype(jnp.float32)
    ocean = (flag_ref[0] == 1).astype(jnp.float32)
    slip_east = ground[0] - previous[0]
    slip_north = ground[1] - previous[1]
    wind_speed = jnp.sqrt(slip_east * slip_east + slip_north * slip_north + gust_speed * gust_speed)
    bulk_flux = [
        drag_coeff * wind_speed * slip_east,
        drag_coeff * wind_speed * slip_north,
        heat_coeff * wind_speed * (previous[2] - ground[2]),
    ]
    for c in range(field_count):
        out_ref[c * row_count : (c + 1) * row_count, :] = (
            ground[c] * ocean + bulk_flux[c] * (1.0 - ocean)
        ) * sea_float
    base = field_count * row_count
    out_ref[base : base + 8, :] = jnp.zeros((8, col_count), jnp.float32)
    out_ref[base : base + link_fields, :link_count] = link_ref[...]


def exported_block(flag, state, surface, sea_mask, links):
    field_count, row_count, col_count = surface.shape[1:]
    vmem = pl.BlockSpec(memory_space=pltpu.VMEM)
    return pl.pallas_call(
        export_kernel,
        out_shape=jax.ShapeDtypeStruct((field_count * row_count + 8, col_count), jnp.float32),
        in_specs=[
            pl.BlockSpec(memory_space=pltpu.SMEM),
            pl.BlockSpec((1, field_count, 1, row_count, col_count), lambda i: (0, 0, 0, 0, 0)),
            vmem,
            vmem,
            vmem,
        ],
        out_specs=vmem,
        grid=(1,),
        interpret=INTERPRET,
    )(flag, state, surface, sea_mask, links)


def remap_kernel(link_count, lat_ref, gathered_ref, table_ref, out_ref, rows_ref, combo_ref):
    source_count = gathered_ref.shape[0]
    tile_count = table_ref.shape[1]
    owner_count, field_count, row_count, col_count = out_ref.shape
    base = field_count * row_count
    my_lat = lat_ref[0]
    for source in range(source_count):
        rows_ref[source * base : (source + 1) * base, :] = gathered_ref[source, :base, :]
    for tile in range(tile_count):
        weighted = jnp.dot(
            rows_ref[...], table_ref[0, tile], precision=HIGHEST, preferred_element_type=jnp.float32
        )
        for source in range(source_count):
            for c in range(field_count):
                first = (source * tile_count + tile) * row_count
                combo_ref[c, first : first + row_count, :] = weighted[
                    source * base + c * row_count : source * base + (c + 1) * row_count
                ]
    pick_count = source_count * tile_count * row_count
    into = jnp.zeros((owner_count * row_count, pick_count), jnp.float32)
    for source in range(source_count):
        table = gathered_ref[source, base : base + 4, :link_count].astype(jnp.int32)
        dest, src_row, dst_row, tile = table[0:1], table[1:2], table[2:3], table[3:4]
        low = my_lat * owner_count
        valid = (dest >= low) & (dest < low + owner_count)
        dest_col = (dest - low) * row_count + dst_row
        pick_col = (source * tile_count + tile) * row_count + src_row
        to_rows = (
            (lax.broadcasted_iota(jnp.int32, (owner_count * row_count, link_count), 0) == dest_col)
            & valid
        ).astype(jnp.bfloat16)
        from_rows = (
            lax.broadcasted_iota(jnp.int32, (pick_count, link_count), 0) == pick_col
        ).astype(jnp.bfloat16)
        into = into + lax.dot_general(
            to_rows, from_rows, (((1,), (1,)), ((), ())), preferred_element_type=jnp.float32
        )
    for c in range(field_count):
        summed = jnp.dot(into, combo_ref[c], precision=HIGHEST, preferred_element_type=jnp.float32)
        for owner in range(owner_count):
            out_ref[owner, c] = summed[owner * row_count : (owner + 1) * row_count]


def remapped(lat, gathered, remap_weights, owner_count, field_count, row_count, link_count):
    source_count, _, col_count = gathered.shape
    tile_count = remap_weights.shape[1]
    vmem = pl.BlockSpec(memory_space=pltpu.VMEM)
    return pl.pallas_call(
        functools.partial(remap_kernel, link_count),
        out_shape=jax.ShapeDtypeStruct((owner_count, field_count, row_count, col_count), jnp.float32),
        in_specs=[pl.BlockSpec(memory_space=pltpu.SMEM), vmem, vmem],
        out_specs=vmem,
        scratch_shapes=[
            pltpu.VMEM((source_count * field_count * row_count, col_count), jnp.float32),
            pltpu.VMEM(
                (field_count, source_count * tile_count * row_count, col_count), jnp.float32
            ),
        ],
        interpret=INTERPRET,
    )(lat, gathered, remap_weights)


def surface_export(ground, previous, sea_float, ocean_side):
    slip_east = ground[0] - previous[0]
    slip_north = ground[1] - previous[1]
    wind_speed = jnp.sqrt(slip_east * slip_east + slip_north * slip_north + gust_speed * gust_speed)
    bulk_flux = jnp.stack(
        [
            drag_coeff * wind_speed * slip_east,
            drag_coeff * wind_speed * slip_north,
            heat_coeff * wind_speed * (previous[2] - ground[2]),
        ]
    )
    return jnp.where(ocean_side, ground, bulk_flux) * sea_float


def body(
    state,
    surface,
    sea_mask,
    coeffs,
    remap_weights,
    link_dest,
    link_src_row,
    link_dst_row,
    link_tile,
):
    fields = state[0]
    previous = surface[0]
    sea_float = sea_mask[0].astype(jnp.float32)
    level_coef = coeffs[0]
    tile_table = remap_weights[0]
    field_count, level_count, row_count, col_count = fields.shape
    tile_count = tile_table.shape[0]
    ocean_side = lax.axis_index("grp") == 1
    first_row = lax.axis_index("lat") * row_count
    total_rows = row_count * lax.axis_size("lat")
    peer_count = lax.axis_size("lat") * lax.axis_size("lon")
    width = field_count * col_count

    links = jnp.stack(
        [link_dest[0, :, 0], link_src_row[0], link_dst_row[0], link_tile[0]]
    ).astype(jnp.float32)
    flag = lax.axis_index("grp").astype(jnp.int32).reshape(1)
    payload = exported_block(flag, state, surface, sea_mask, links)
    gathered = lax.all_gather(payload, "lat", axis=0, tiled=False)
    lat = lax.axis_index("lat").astype(jnp.int32).reshape(1)
    partial = remapped(
        lat, gathered, remap_weights, lax.axis_size("lon"), field_count, row_count, links.shape[1]
    )
    summed_here = lax.psum_scatter(partial, "lon", scatter_dimension=0, tiled=False)
    imported = lax.ppermute(summed_here, "grp", [(0, 1), (1, 0)]) * sea_float

    gain = jnp.where(ocean_side, ocean_gain, air_gain)
    damping = jnp.where(ocean_side, 0.0, air_gain)
    ground = fields[:, 0] + sea_float * (gain * previous - damping * fields[:, 0])
    fields = jnp.concatenate([ground[:, None], fields[:, 1:]], 1)
    state_mask = jnp.where(ocean_side, sea_float, jnp.ones_like(sea_float))
    planes = jnp.concatenate(
        [fields.reshape(field_count * level_count, row_count, col_count), state_mask[None]], 0
    )
    wide_rows = -(-(row_count + 4 * SUBSTEPS) // 8) * 8
    wide_cols = -(-(col_count + 4 * SUBSTEPS) // 128) * 128
    wide = with_halo(planes, SUBSTEPS, wide_cols, wide_rows)
    local = jnp.arange(wide_rows, dtype=jnp.int32)
    row_index = first_row + jnp.where(local < wide_rows // 2 + row_count // 2, local, local - wide_rows)
    latitude = jnp.pi * (
        -1.0 / 3.0 + 2.0 / 3.0 * (row_index.astype(jnp.float32) + 0.5) / total_rows
    )
    coriolis = coriolis_scale * jnp.sin(latitude)
    inside = ((row_index >= 0) & (row_index < total_rows)).astype(jnp.float32)
    row_terms = jnp.broadcast_to(jnp.stack([coriolis, inside])[:, :, None], (2, wide_rows, wide_cols))
    fields = dynamics(coeffs, row_terms, wide, field_count, level_count, row_count, col_count)
    return (fields, imported[None])


def solution(mesh):
    placed = (
        P("grp", None, None, "lat", "lon"),
        P("grp", None, "lat", "lon"),
        P("grp", "lat", "lon"),
        P("grp", None, None),
        P("grp", None, None, None),
        P("grp", ("lat", "lon"), None),
        P("grp", ("lat", "lon")),
        P("grp", ("lat", "lon")),
        P("grp", ("lat", "lon")),
    )
    return jax.shard_map(
        body,
        mesh=mesh,
        in_specs=placed,
        out_specs=(P("grp", None, None, "lat", "lon"), P("grp", None, "lat", "lon")),
        check_vma=False,
    )
```

```python
import functools

import jax
import jax.numpy as jnp
from jax import lax
from jax.sharding import PartitionSpec as P
from jax.experimental import pallas as pl
from jax.experimental.pallas import tpu as pltpu

SUBSTEPS = 2


air_gain = 0.3
ocean_gain = 0.5
drag_coeff = 0.5
heat_coeff = 0.5
gust_speed = 0.5
coriolis_scale = 0.25

HIGHEST = lax.Precision.HIGHEST
INTERPRET = False


def shifted(part, axis, closed, forward):
    count = lax.axis_size(axis)
    ends = count if closed else count - 1
    if forward:
        route = [(i, (i + 1) % count) for i in range(ends)]
    else:
        route = [((i + 1) % count, i) for i in range(ends)]
    flat = lax.ppermute(part.reshape(-1), axis, route)
    return flat.reshape(part.shape)


def with_halo(cells, width, wide_cols, wide_rows):
    planes, rows, cols = cells.shape
    head = cells[:, :, :width]
    tail = cells[:, :, -width:]
    gap = jnp.zeros((planes, rows, wide_cols - cols - 2 * width), cells.dtype)
    cells = jnp.concatenate(
        [cells, shifted(head, "lon", True, False), gap, shifted(tail, "lon", True, True)], axis=2
    )
    head = cells[:, :width, :]
    tail = cells[:, rows - width : rows, :]
    gap = jnp.zeros((planes, wide_rows - rows - 2 * width, wide_cols), cells.dtype)
    return jnp.concatenate(
        [cells, shifted(head, "lat", False, False), gap, shifted(tail, "lat", False, True)], axis=1
    )


def stencil_kernel(coef_ref, row_ref, wide_ref, out_ref, mid_ref):
    field_count, level_count, row_count, col_count = out_ref.shape[1:]
    wide_rows, wide_cols = wide_ref.shape[1:]
    turning = row_ref[0]
    keep = wide_ref[field_count * level_count] * row_ref[1]

    def step(read, write):
        for field in range(field_count):
            for level in range(level_count):
                diffuse = coef_ref[0, 0, level]
                advect_east = coef_ref[0, 1, level]
                advect_north = coef_ref[0, 2, level]
                mixing = coef_ref[0, 3, level]
                center = read(field, level)
                north = pltpu.roll(center, wide_rows - 1, 0)
                south = pltpu.roll(center, 1, 0)
                east = pltpu.roll(center, wide_cols - 1, 1)
                west = pltpu.roll(center, 1, 1)
                above = read(field, min(level + 1, level_count - 1))
                below = read(field, max(level - 1, 0))
                laplace = north + south + east + west - 4.0 * center
                updated = (
                    center
                    + diffuse * laplace
                    - advect_east * (east - west)
                    - advect_north * (north - south)
                    + mixing * (above + below - 2.0 * center)
                )
                if field == 0:
                    updated = updated + turning * read(1, level)
                elif field == 1:
                    updated = updated + (-turning) * read(0, level)
                write(field, level, updated * keep)

    def from_wide(field, level):
        return wide_ref[field * level_count + level]

    def to_mid(field, level, value):
        mid_ref[field * level_count + level] = value

    def from_mid(field, level):
        return mid_ref[field * level_count + level]

    def to_out(field, level, value):
        out_ref[0, field, level] = value[:row_count, :col_count]

    step(from_wide, to_mid)
    step(from_mid, to_out)


def dynamics(coeffs, row_terms, wide, field_count, level_count, row_count, col_count):
    planes, wide_rows, wide_cols = wide.shape
    return pl.pallas_call(
        stencil_kernel,
        out_shape=jax.ShapeDtypeStruct((1, field_count, level_count, row_count, col_count), jnp.float32),
        in_specs=[
            pl.BlockSpec(memory_space=pltpu.SMEM),
            pl.BlockSpec(memory_space=pltpu.VMEM),
            pl.BlockSpec(memory_space=pltpu.VMEM),
        ],
        out_specs=pl.BlockSpec(memory_space=pltpu.VMEM),
        scratch_shapes=[pltpu.VMEM((planes - 1, wide_rows, wide_cols), jnp.float32)],
        interpret=INTERPRET,
    )(coeffs, row_terms, wide)


def export_kernel(flag_ref, ground_ref, previous_ref, sea_ref, link_ref, out_ref):
    field_count, row_count, col_count = previous_ref.shape[1:]
    link_fields, link_count = link_ref.shape
    ground = ground_ref[0, :, 0]
    previous = previous_ref[0]
    sea_float = sea_ref[0].astype(jnp.float32)
    ocean = (flag_ref[0] == 1).astype(jnp.float32)
    slip_east = ground[0] - previous[0]
    slip_north = ground[1] - previous[1]
    wind_speed = jnp.sqrt(slip_east * slip_east + slip_north * slip_north + gust_speed * gust_speed)
    bulk_flux = [
        drag_coeff * wind_speed * slip_east,
        drag_coeff * wind_speed * slip_north,
        heat_coeff * wind_speed * (previous[2] - ground[2]),
    ]
    for c in range(field_count):
        out_ref[c * row_count : (c + 1) * row_count, :] = (
            ground[c] * ocean + bulk_flux[c] * (1.0 - ocean)
        ) * sea_float
    base = field_count * row_count
    out_ref[base : base + 8, :] = jnp.zeros((8, col_count), jnp.float32)
    out_ref[base : base + link_fields, :link_count] = link_ref[...]


def exported_block(flag, state, surface, sea_mask, links):
    field_count, row_count, col_count = surface.shape[1:]
    vmem = pl.BlockSpec(memory_space=pltpu.VMEM)
    return pl.pallas_call(
        export_kernel,
        out_shape=jax.ShapeDtypeStruct((field_count * row_count + 8, col_count), jnp.float32),
        in_specs=[
            pl.BlockSpec(memory_space=pltpu.SMEM),
            pl.BlockSpec((1, field_count, 1, row_count, col_count), lambda i: (0, 0, 0, 0, 0)),
            vmem,
            vmem,
            vmem,
        ],
        out_specs=vmem,
        grid=(1,),
        interpret=INTERPRET,
    )(flag, state, surface, sea_mask, links)


def remap_kernel(link_count, source_count, lat_ref, *refs):
    source_refs = refs[:source_count]
    table_ref, out_ref, rows_ref, combo_ref = refs[source_count:]
    tile_count = table_ref.shape[1]
    owner_count, field_count, row_count, col_count = out_ref.shape
    base = field_count * row_count
    my_lat = lat_ref[0]
    for source in range(source_count):
        rows_ref[source * base : (source + 1) * base, :] = source_refs[source][:base, :]
    for tile in range(tile_count):
        weighted = jnp.dot(
            rows_ref[...], table_ref[0, tile], precision=HIGHEST, preferred_element_type=jnp.float32
        )
        for source in range(source_count):
            for c in range(field_count):
                first = (source * tile_count + tile) * row_count
                combo_ref[c, first : first + row_count, :] = weighted[
                    source * base + c * row_count : source * base + (c + 1) * row_count
                ]
    pick_count = source_count * tile_count * row_count
    into = jnp.zeros((owner_count * row_count, pick_count), jnp.float32)
    for source in range(source_count):
        table = source_refs[source][base : base + 4, :link_count].astype(jnp.int32)
        dest, src_row, dst_row, tile = table[0:1], table[1:2], table[2:3], table[3:4]
        low = my_lat * owner_count
        valid = (dest >= low) & (dest < low + owner_count)
        dest_col = (dest - low) * row_count + dst_row
        pick_col = (source * tile_count + tile) * row_count + src_row
        to_rows = (
            (lax.broadcasted_iota(jnp.int32, (owner_count * row_count, link_count), 0) == dest_col)
            & valid
        ).astype(jnp.bfloat16)
        from_rows = (
            lax.broadcasted_iota(jnp.int32, (pick_count, link_count), 0) == pick_col
        ).astype(jnp.bfloat16)
        into = into + lax.dot_general(
            to_rows, from_rows, (((1,), (1,)), ((), ())), preferred_element_type=jnp.float32
        )
    for c in range(field_count):
        summed = jnp.dot(into, combo_ref[c], precision=HIGHEST, preferred_element_type=jnp.float32)
        for owner in range(owner_count):
            out_ref[owner, c] = summed[owner * row_count : (owner + 1) * row_count]


def remapped(lat, sources, remap_weights, owner_count, field_count, row_count, link_count):
    source_count = len(sources)
    col_count = sources[0].shape[1]
    tile_count = remap_weights.shape[1]
    vmem = pl.BlockSpec(memory_space=pltpu.VMEM)
    return pl.pallas_call(
        functools.partial(remap_kernel, link_count, source_count),
        out_shape=jax.ShapeDtypeStruct((owner_count, field_count, row_count, col_count), jnp.float32),
        in_specs=[pl.BlockSpec(memory_space=pltpu.SMEM)] + [vmem] * (source_count + 1),
        out_specs=vmem,
        scratch_shapes=[
            pltpu.VMEM((source_count * field_count * row_count, col_count), jnp.float32),
            pltpu.VMEM(
                (field_count, source_count * tile_count * row_count, col_count), jnp.float32
            ),
        ],
        interpret=INTERPRET,
    )(lat, *sources, remap_weights)


def surface_export(ground, previous, sea_float, ocean_side):
    slip_east = ground[0] - previous[0]
    slip_north = ground[1] - previous[1]
    wind_speed = jnp.sqrt(slip_east * slip_east + slip_north * slip_north + gust_speed * gust_speed)
    bulk_flux = jnp.stack(
        [
            drag_coeff * wind_speed * slip_east,
            drag_coeff * wind_speed * slip_north,
            heat_coeff * wind_speed * (previous[2] - ground[2]),
        ]
    )
    return jnp.where(ocean_side, ground, bulk_flux) * sea_float


def body(
    state,
    surface,
    sea_mask,
    coeffs,
    remap_weights,
    link_dest,
    link_src_row,
    link_dst_row,
    link_tile,
):
    fields = state[0]
    previous = surface[0]
    sea_float = sea_mask[0].astype(jnp.float32)
    level_coef = coeffs[0]
    tile_table = remap_weights[0]
    field_count, level_count, row_count, col_count = fields.shape
    tile_count = tile_table.shape[0]
    ocean_side = lax.axis_index("grp") == 1
    first_row = lax.axis_index("lat") * row_count
    total_rows = row_count * lax.axis_size("lat")
    peer_count = lax.axis_size("lat") * lax.axis_size("lon")
    width = field_count * col_count

    links = jnp.stack(
        [link_dest[0, :, 0], link_src_row[0], link_dst_row[0], link_tile[0]]
    ).astype(jnp.float32)
    flag = lax.axis_index("grp").astype(jnp.int32).reshape(1)
    payload = exported_block(flag, state, surface, sea_mask, links)
    lat_count = lax.axis_size("lat")
    lon_count = lax.axis_size("lon")
    sources = [payload] + [
        lax.ppermute(payload, "lat", [(i, (i + shift) % lat_count) for i in range(lat_count)])
        for shift in range(1, lat_count)
    ]
    lat = lax.axis_index("lat").astype(jnp.int32).reshape(1)
    partial = remapped(lat, sources, remap_weights, lon_count, field_count, row_count, links.shape[1])
    pieces = []
    for shift in range(lon_count):
        route = [
            (g * lon_count + j, (1 - g) * lon_count + (j + shift) % lon_count)
            for g in range(2)
            for j in range(lon_count)
        ]
        owner_lon = (lax.axis_index("lon") + shift) % lon_count
        pieces.append(lax.ppermute(partial[owner_lon], ("grp", "lon"), route))
    imported = functools.reduce(jnp.add, pieces) * sea_float

    gain = jnp.where(ocean_side, ocean_gain, air_gain)
    damping = jnp.where(ocean_side, 0.0, air_gain)
    ground = fields[:, 0] + sea_float * (gain * previous - damping * fields[:, 0])
    fields = jnp.concatenate([ground[:, None], fields[:, 1:]], 1)
    state_mask = jnp.where(ocean_side, sea_float, jnp.ones_like(sea_float))
    planes = jnp.concatenate(
        [fields.reshape(field_count * level_count, row_count, col_count), state_mask[None]], 0
    )
    wide_rows = -(-(row_count + 4 * SUBSTEPS) // 8) * 8
    wide_cols = -(-(col_count + 4 * SUBSTEPS) // 128) * 128
    wide = with_halo(planes, SUBSTEPS, wide_cols, wide_rows)
    local = jnp.arange(wide_rows, dtype=jnp.int32)
    row_index = first_row + jnp.where(local < wide_rows // 2 + row_count // 2, local, local - wide_rows)
    latitude = jnp.pi * (
        -1.0 / 3.0 + 2.0 / 3.0 * (row_index.astype(jnp.float32) + 0.5) / total_rows
    )
    coriolis = coriolis_scale * jnp.sin(latitude)
    inside = ((row_index >= 0) & (row_index < total_rows)).astype(jnp.float32)
    row_terms = jnp.broadcast_to(jnp.stack([coriolis, inside])[:, :, None], (2, wide_rows, wide_cols))
    fields = dynamics(coeffs, row_terms, wide, field_count, level_count, row_count, col_count)
    return (fields, imported[None])


def solution(mesh):
    placed = (
        P("grp", None, None, "lat", "lon"),
        P("grp", None, "lat", "lon"),
        P("grp", "lat", "lon"),
        P("grp", None, None),
        P("grp", None, None, None),
        P("grp", ("lat", "lon"), None),
        P("grp", ("lat", "lon")),
        P("grp", ("lat", "lon")),
        P("grp", ("lat", "lon")),
    )
    return jax.shard_map(
        body,
        mesh=mesh,
        in_specs=placed,
        out_specs=(P("grp", None, None, "lat", "lon"), P("grp", None, "lat", "lon")),
        check_vma=False,
    )
```

```python
import functools

import jax
import jax.numpy as jnp
from jax import lax
from jax.sharding import PartitionSpec as P
from jax.experimental import pallas as pl
from jax.experimental.pallas import tpu as pltpu

SUBSTEPS = 2


air_gain = 0.3
ocean_gain = 0.5
drag_coeff = 0.5
heat_coeff = 0.5
gust_speed = 0.5
coriolis_scale = 0.25

HIGHEST = lax.Precision.HIGHEST
INTERPRET = False


def shifted(part, axis, closed, forward):
    count = lax.axis_size(axis)
    ends = count if closed else count - 1
    if forward:
        route = [(i, (i + 1) % count) for i in range(ends)]
    else:
        route = [((i + 1) % count, i) for i in range(ends)]
    flat = lax.ppermute(part.reshape(-1), axis, route)
    return flat.reshape(part.shape)


def with_halo(cells, width, wide_cols, wide_rows):
    planes, rows, cols = cells.shape
    head = cells[:, :, :width]
    tail = cells[:, :, -width:]
    gap = jnp.zeros((planes, rows, wide_cols - cols - 2 * width), cells.dtype)
    cells = jnp.concatenate(
        [cells, shifted(head, "lon", True, False), gap, shifted(tail, "lon", True, True)], axis=2
    )
    head = cells[:, :width, :]
    tail = cells[:, rows - width : rows, :]
    gap = jnp.zeros((planes, wide_rows - rows - 2 * width, wide_cols), cells.dtype)
    return jnp.concatenate(
        [cells, shifted(head, "lat", False, False), gap, shifted(tail, "lat", False, True)], axis=1
    )


def stencil_kernel(coef_ref, row_ref, wide_ref, out_ref, mid_ref):
    field_count, level_count, row_count, col_count = out_ref.shape[1:]
    wide_rows, wide_cols = wide_ref.shape[1:]
    turning_wide = jnp.broadcast_to(row_ref[0], (wide_rows, wide_cols))
    keep_wide = wide_ref[field_count * level_count] * jnp.broadcast_to(row_ref[1], (wide_rows, wide_cols))

    def step(read, write, rows, cols):
        turning = turning_wide[:rows, :cols]
        keep = keep_wide[:rows, :cols]
        for field in range(field_count):
            for level in range(level_count):
                diffuse = coef_ref[0, 0, level]
                advect_east = coef_ref[0, 1, level]
                advect_north = coef_ref[0, 2, level]
                mixing = coef_ref[0, 3, level]
                whole = read(field, level)
                north = pltpu.roll(whole, wide_rows - 1, 0)[:rows, :cols]
                south = pltpu.roll(whole, 1, 0)[:rows, :cols]
                east = pltpu.roll(whole, wide_cols - 1, 1)[:rows, :cols]
                west = pltpu.roll(whole, 1, 1)[:rows, :cols]
                center = whole[:rows, :cols]
                above = read(field, min(level + 1, level_count - 1))[:rows, :cols]
                below = read(field, max(level - 1, 0))[:rows, :cols]
                laplace = north + south + east + west - 4.0 * center
                updated = (
                    center
                    + diffuse * laplace
                    - advect_east * (east - west)
                    - advect_north * (north - south)
                    + mixing * (above + below - 2.0 * center)
                )
                if field == 0:
                    updated = updated + turning * read(1, level)[:rows, :cols]
                elif field == 1:
                    updated = updated + (-turning) * read(0, level)[:rows, :cols]
                write(field, level, updated * keep)

    def from_wide(field, level):
        return wide_ref[field * level_count + level]

    def to_mid(field, level, value):
        mid_ref[field * level_count + level] = value

    def from_mid(field, level):
        return mid_ref[field * level_count + level]

    def to_out(field, level, value):
        out_ref[0, field, level] = value

    step(from_wide, to_mid, wide_rows, wide_cols)
    step(from_mid, to_out, row_count, col_count)


def dynamics(coeffs, row_terms, wide, field_count, level_count, row_count, col_count):
    planes, wide_rows, wide_cols = wide.shape
    return pl.pallas_call(
        stencil_kernel,
        out_shape=jax.ShapeDtypeStruct((1, field_count, level_count, row_count, col_count), jnp.float32),
        in_specs=[
            pl.BlockSpec(memory_space=pltpu.SMEM),
            pl.BlockSpec(memory_space=pltpu.VMEM),
            pl.BlockSpec(memory_space=pltpu.VMEM),
        ],
        out_specs=pl.BlockSpec(memory_space=pltpu.VMEM),
        scratch_shapes=[pltpu.VMEM((planes - 1, wide_rows, wide_cols), jnp.float32)],
        interpret=INTERPRET,
    )(coeffs, row_terms, wide)


def export_kernel(flag_ref, ground_ref, previous_ref, sea_ref, link_ref, out_ref):
    field_count, row_count, col_count = previous_ref.shape[1:]
    link_fields, link_count = link_ref.shape
    ground = ground_ref[0, :, 0]
    previous = previous_ref[0]
    sea_float = sea_ref[0].astype(jnp.float32)
    ocean = (flag_ref[0] == 1).astype(jnp.float32)
    slip_east = ground[0] - previous[0]
    slip_north = ground[1] - previous[1]
    wind_speed = jnp.sqrt(slip_east * slip_east + slip_north * slip_north + gust_speed * gust_speed)
    bulk_flux = [
        drag_coeff * wind_speed * slip_east,
        drag_coeff * wind_speed * slip_north,
        heat_coeff * wind_speed * (previous[2] - ground[2]),
    ]
    for c in range(field_count):
        out_ref[c * row_count : (c + 1) * row_count, :] = (
            ground[c] * ocean + bulk_flux[c] * (1.0 - ocean)
        ) * sea_float
    base = field_count * row_count
    out_ref[base : base + 8, :] = jnp.zeros((8, col_count), jnp.float32)
    out_ref[base : base + link_fields, :link_count] = link_ref[...]


def exported_block(flag, state, surface, sea_mask, links):
    field_count, row_count, col_count = surface.shape[1:]
    vmem = pl.BlockSpec(memory_space=pltpu.VMEM)
    return pl.pallas_call(
        export_kernel,
        out_shape=jax.ShapeDtypeStruct((field_count * row_count + 8, col_count), jnp.float32),
        in_specs=[
            pl.BlockSpec(memory_space=pltpu.SMEM),
            pl.BlockSpec((1, field_count, 1, row_count, col_count), lambda i: (0, 0, 0, 0, 0)),
            vmem,
            vmem,
            vmem,
        ],
        out_specs=vmem,
        grid=(1,),
        interpret=INTERPRET,
    )(flag, state, surface, sea_mask, links)


def remap_kernel(link_count, source_count, place_ref, *refs):
    source_refs = refs[:source_count]
    table_ref, out_ref, rows_ref, combo_ref = refs[source_count:]
    tile_count = table_ref.shape[1]
    owner_count, field_count, row_count, col_count = out_ref.shape
    base = field_count * row_count
    my_lat = place_ref[0]
    my_lon = place_ref[1]
    for source in range(source_count):
        rows_ref[source * base : (source + 1) * base, :] = source_refs[source][:base, :]
    for tile in range(tile_count):
        weighted = jnp.dot(
            rows_ref[...], table_ref[0, tile], precision=HIGHEST, preferred_element_type=jnp.float32
        )
        for source in range(source_count):
            for c in range(field_count):
                first = (source * tile_count + tile) * row_count
                combo_ref[c, first : first + row_count, :] = weighted[
                    source * base + c * row_count : source * base + (c + 1) * row_count
                ]
    pick_count = source_count * tile_count * row_count
    into = jnp.zeros((owner_count * row_count, pick_count), jnp.float32)
    for source in range(source_count):
        table = source_refs[source][base : base + 4, :link_count].astype(jnp.int32)
        dest, src_row, dst_row, tile = table[0:1], table[1:2], table[2:3], table[3:4]
        low = my_lat * owner_count
        valid = (dest >= low) & (dest < low + owner_count)
        shift = dest - low - my_lon
        shift = jnp.where(shift < 0, shift + owner_count, shift)
        dest_col = shift * row_count + dst_row
        pick_col = (source * tile_count + tile) * row_count + src_row
        to_rows = (
            (lax.broadcasted_iota(jnp.int32, (owner_count * row_count, link_count), 0) == dest_col)
            & valid
        ).astype(jnp.bfloat16)
        from_rows = (
            lax.broadcasted_iota(jnp.int32, (pick_count, link_count), 0) == pick_col
        ).astype(jnp.bfloat16)
        into = into + lax.dot_general(
            to_rows, from_rows, (((1,), (1,)), ((), ())), preferred_element_type=jnp.float32
        )
    for c in range(field_count):
        summed = jnp.dot(into, combo_ref[c], precision=HIGHEST, preferred_element_type=jnp.float32)
        for owner in range(owner_count):
            out_ref[owner, c] = summed[owner * row_count : (owner + 1) * row_count]


def remapped(lat, sources, remap_weights, owner_count, field_count, row_count, link_count):
    source_count = len(sources)
    col_count = sources[0].shape[1]
    tile_count = remap_weights.shape[1]
    vmem = pl.BlockSpec(memory_space=pltpu.VMEM)
    return pl.pallas_call(
        functools.partial(remap_kernel, link_count, source_count),
        out_shape=jax.ShapeDtypeStruct((owner_count, field_count, row_count, col_count), jnp.float32),
        in_specs=[pl.BlockSpec(memory_space=pltpu.SMEM)] + [vmem] * (source_count + 1),
        out_specs=vmem,
        scratch_shapes=[
            pltpu.VMEM((source_count * field_count * row_count, col_count), jnp.float32),
            pltpu.VMEM(
                (field_count, source_count * tile_count * row_count, col_count), jnp.float32
            ),
        ],
        interpret=INTERPRET,
    )(lat, *sources, remap_weights)


def surface_export(ground, previous, sea_float, ocean_side):
    slip_east = ground[0] - previous[0]
    slip_north = ground[1] - previous[1]
    wind_speed = jnp.sqrt(slip_east * slip_east + slip_north * slip_north + gust_speed * gust_speed)
    bulk_flux = jnp.stack(
        [
            drag_coeff * wind_speed * slip_east,
            drag_coeff * wind_speed * slip_north,
            heat_coeff * wind_speed * (previous[2] - ground[2]),
        ]
    )
    return jnp.where(ocean_side, ground, bulk_flux) * sea_float


def body(
    state,
    surface,
    sea_mask,
    coeffs,
    remap_weights,
    link_dest,
    link_src_row,
    link_dst_row,
    link_tile,
):
    fields = state[0]
    previous = surface[0]
    sea_float = sea_mask[0].astype(jnp.float32)
    level_coef = coeffs[0]
    tile_table = remap_weights[0]
    field_count, level_count, row_count, col_count = fields.shape
    tile_count = tile_table.shape[0]
    ocean_side = lax.axis_index("grp") == 1
    first_row = lax.axis_index("lat") * row_count
    total_rows = row_count * lax.axis_size("lat")
    peer_count = lax.axis_size("lat") * lax.axis_size("lon")
    width = field_count * col_count

    links = jnp.stack(
        [link_dest[0, :, 0], link_src_row[0], link_dst_row[0], link_tile[0]]
    ).astype(jnp.float32)
    flag = lax.axis_index("grp").astype(jnp.int32).reshape(1)
    payload = exported_block(flag, state, surface, sea_mask, links)
    lat_count = lax.axis_size("lat")
    lon_count = lax.axis_size("lon")
    sources = [payload] + [
        lax.ppermute(payload, "lat", [(i, (i + shift) % lat_count) for i in range(lat_count)])
        for shift in range(1, lat_count)
    ]
    place = jnp.stack([lax.axis_index("lat"), lax.axis_index("lon")]).astype(jnp.int32)
    partial = remapped(place, sources, remap_weights, lon_count, field_count, row_count, links.shape[1])
    pieces = []
    for shift in range(lon_count):
        route = [
            (g * lon_count + j, (1 - g) * lon_count + (j + shift) % lon_count)
            for g in range(2)
            for j in range(lon_count)
        ]
        pieces.append(lax.ppermute(partial[shift], ("grp", "lon"), route))
    imported = functools.reduce(jnp.add, pieces) * sea_float

    gain = jnp.where(ocean_side, ocean_gain, air_gain)
    damping = jnp.where(ocean_side, 0.0, air_gain)
    ground = fields[:, 0] + sea_float * (gain * previous - damping * fields[:, 0])
    fields = jnp.concatenate([ground[:, None], fields[:, 1:]], 1)
    state_mask = jnp.where(ocean_side, sea_float, jnp.ones_like(sea_float))
    planes = jnp.concatenate(
        [fields.reshape(field_count * level_count, row_count, col_count), state_mask[None]], 0
    )
    wide_rows = -(-(row_count + 4 * SUBSTEPS) // 8) * 8
    wide_cols = -(-(col_count + 4 * SUBSTEPS) // 128) * 128
    wide = with_halo(planes, SUBSTEPS, wide_cols, wide_rows)
    local = jnp.arange(wide_rows, dtype=jnp.int32)
    row_index = first_row + jnp.where(local < wide_rows // 2 + row_count // 2, local, local - wide_rows)
    latitude = jnp.pi * (
        -1.0 / 3.0 + 2.0 / 3.0 * (row_index.astype(jnp.float32) + 0.5) / total_rows
    )
    coriolis = coriolis_scale * jnp.sin(latitude)
    inside = ((row_index >= 0) & (row_index < total_rows)).astype(jnp.float32)
    row_terms = jnp.stack([coriolis, inside])[:, :, None]
    fields = dynamics(coeffs, row_terms, wide, field_count, level_count, row_count, col_count)
    return (fields, imported[None])


def solution(mesh):
    placed = (
        P("grp", None, None, "lat", "lon"),
        P("grp", None, "lat", "lon"),
        P("grp", "lat", "lon"),
        P("grp", None, None),
        P("grp", None, None, None),
        P("grp", ("lat", "lon"), None),
        P("grp", ("lat", "lon")),
        P("grp", ("lat", "lon")),
        P("grp", ("lat", "lon")),
    )
    return jax.shard_map(
        body,
        mesh=mesh,
        in_specs=placed,
        out_specs=(P("grp", None, None, "lat", "lon"), P("grp", None, "lat", "lon")),
        check_vma=False,
    )
```

```python
import functools

import jax
import jax.numpy as jnp
from jax import lax
from jax.sharding import PartitionSpec as P
from jax.experimental import pallas as pl
from jax.experimental.pallas import tpu as pltpu

SUBSTEPS = 2


air_gain = 0.3
ocean_gain = 0.5
drag_coeff = 0.5
heat_coeff = 0.5
gust_speed = 0.5
coriolis_scale = 0.25

HIGHEST = lax.Precision.HIGHEST
INTERPRET = False


def shifted(part, axis, closed, forward):
    count = lax.axis_size(axis)
    ends = count if closed else count - 1
    if forward:
        route = [(i, (i + 1) % count) for i in range(ends)]
    else:
        route = [((i + 1) % count, i) for i in range(ends)]
    flat = lax.ppermute(part.reshape(-1), axis, route)
    return flat.reshape(part.shape)


def with_halo(cells, width, wide_cols, wide_rows):
    planes, rows, cols = cells.shape
    head = cells[:, :, :width]
    tail = cells[:, :, -width:]
    gap = jnp.zeros((planes, rows, wide_cols - cols - 2 * width), cells.dtype)
    cells = jnp.concatenate(
        [cells, shifted(head, "lon", True, False), gap, shifted(tail, "lon", True, True)], axis=2
    )
    head = cells[:, :width, :]
    tail = cells[:, rows - width : rows, :]
    gap = jnp.zeros((planes, wide_rows - rows - 2 * width, wide_cols), cells.dtype)
    return jnp.concatenate(
        [cells, shifted(head, "lat", False, False), gap, shifted(tail, "lat", False, True)], axis=1
    )


def stencil_kernel(coef_ref, row_ref, wide_ref, out_ref, mid_ref):
    field_count, level_count, row_count, col_count = out_ref.shape[1:]
    wide_rows, wide_cols = wide_ref.shape[1:]
    turning_wide = jnp.broadcast_to(row_ref[0], (wide_rows, wide_cols))
    keep_wide = wide_ref[field_count * level_count] * jnp.broadcast_to(row_ref[1], (wide_rows, wide_cols))

    def step(read, write, rows, cols):
        turning = turning_wide[:rows, :cols]
        keep = keep_wide[:rows, :cols]
        for field in range(field_count):
            for level in range(level_count):
                diffuse = coef_ref[0, 0, level]
                advect_east = coef_ref[0, 1, level]
                advect_north = coef_ref[0, 2, level]
                mixing = coef_ref[0, 3, level]
                whole = read(field, level)
                north = pltpu.roll(whole, wide_rows - 1, 0)[:rows, :cols]
                south = pltpu.roll(whole, 1, 0)[:rows, :cols]
                east = pltpu.roll(whole, wide_cols - 1, 1)[:rows, :cols]
                west = pltpu.roll(whole, 1, 1)[:rows, :cols]
                center = whole[:rows, :cols]
                above = read(field, min(level + 1, level_count - 1))[:rows, :cols]
                below = read(field, max(level - 1, 0))[:rows, :cols]
                laplace = north + south + east + west - 4.0 * center
                updated = (
                    center
                    + diffuse * laplace
                    - advect_east * (east - west)
                    - advect_north * (north - south)
                    + mixing * (above + below - 2.0 * center)
                )
                if field == 0:
                    updated = updated + turning * read(1, level)[:rows, :cols]
                elif field == 1:
                    updated = updated + (-turning) * read(0, level)[:rows, :cols]
                write(field, level, updated * keep)

    def from_wide(field, level):
        return wide_ref[field * level_count + level]

    def to_mid(field, level, value):
        mid_ref[field * level_count + level] = value

    def from_mid(field, level):
        return mid_ref[field * level_count + level]

    def to_out(field, level, value):
        out_ref[0, field, level] = value

    step(from_wide, to_mid, wide_rows, wide_cols)
    step(from_mid, to_out, row_count, col_count)


def dynamics(coeffs, row_terms, wide, field_count, level_count, row_count, col_count):
    planes, wide_rows, wide_cols = wide.shape
    return pl.pallas_call(
        stencil_kernel,
        out_shape=jax.ShapeDtypeStruct((1, field_count, level_count, row_count, col_count), jnp.float32),
        in_specs=[
            pl.BlockSpec(memory_space=pltpu.SMEM),
            pl.BlockSpec(memory_space=pltpu.VMEM),
            pl.BlockSpec(memory_space=pltpu.VMEM),
        ],
        out_specs=pl.BlockSpec(memory_space=pltpu.VMEM),
        scratch_shapes=[pltpu.VMEM((planes - 1, wide_rows, wide_cols), jnp.float32)],
        interpret=INTERPRET,
    )(coeffs, row_terms, wide)


def export_kernel(flag_ref, ground_ref, previous_ref, sea_ref, link_ref, out_ref):
    field_count, row_count, col_count = previous_ref.shape[1:]
    link_fields, link_count = link_ref.shape
    ground = ground_ref[0, :, 0]
    previous = previous_ref[0]
    sea_float = sea_ref[0].astype(jnp.float32)
    ocean = (flag_ref[0] == 1).astype(jnp.float32)
    slip_east = ground[0] - previous[0]
    slip_north = ground[1] - previous[1]
    wind_speed = jnp.sqrt(slip_east * slip_east + slip_north * slip_north + gust_speed * gust_speed)
    bulk_flux = [
        drag_coeff * wind_speed * slip_east,
        drag_coeff * wind_speed * slip_north,
        heat_coeff * wind_speed * (previous[2] - ground[2]),
    ]
    for c in range(field_count):
        out_ref[c * row_count : (c + 1) * row_count, :] = (
            ground[c] * ocean + bulk_flux[c] * (1.0 - ocean)
        ) * sea_float
    base = field_count * row_count
    out_ref[base : base + 8, :] = jnp.zeros((8, col_count), jnp.float32)
    out_ref[base : base + link_fields, :link_count] = link_ref[...]


def exported_block(flag, state, surface, sea_mask, links):
    field_count, row_count, col_count = surface.shape[1:]
    vmem = pl.BlockSpec(memory_space=pltpu.VMEM)
    return pl.pallas_call(
        export_kernel,
        out_shape=jax.ShapeDtypeStruct((field_count * row_count + 8, col_count), jnp.float32),
        in_specs=[
            pl.BlockSpec(memory_space=pltpu.SMEM),
            pl.BlockSpec((1, field_count, 1, row_count, col_count), lambda i: (0, 0, 0, 0, 0)),
            vmem,
            vmem,
            vmem,
        ],
        out_specs=vmem,
        grid=(1,),
        interpret=INTERPRET,
    )(flag, state, surface, sea_mask, links)


def remap_kernel(link_count, source_count, place_ref, *refs):
    source_refs = refs[:source_count]
    table_ref, out_ref, rows_ref, combo_ref = refs[source_count:]
    tile_count = table_ref.shape[1]
    owner_count, field_count, row_count, col_count = out_ref.shape
    base = field_count * row_count
    my_lat = place_ref[0]
    my_lon = place_ref[1]
    for source in range(source_count):
        rows_ref[source * base : (source + 1) * base, :] = source_refs[source][:base, :]
    for tile in range(tile_count):
        weighted = jnp.dot(
            rows_ref[...], table_ref[0, tile], precision=HIGHEST, preferred_element_type=jnp.float32
        )
        for source in range(source_count):
            for c in range(field_count):
                first = (source * tile_count + tile) * row_count
                combo_ref[c, first : first + row_count, :] = weighted[
                    source * base + c * row_count : source * base + (c + 1) * row_count
                ]
    pick_count = source_count * tile_count * row_count
    into = jnp.zeros((owner_count * row_count, pick_count), jnp.float32)
    for source in range(source_count):
        table = source_refs[source][base : base + 4, :link_count].astype(jnp.int32)
        dest, src_row, dst_row, tile = table[0:1], table[1:2], table[2:3], table[3:4]
        low = my_lat * owner_count
        valid = (dest >= low) & (dest < low + owner_count)
        shift = dest - low - my_lon
        shift = jnp.where(shift < 0, shift + owner_count, shift)
        dest_col = shift * row_count + dst_row
        pick_col = (source * tile_count + tile) * row_count + src_row
        to_rows = (
            (lax.broadcasted_iota(jnp.int32, (owner_count * row_count, link_count), 0) == dest_col)
            & valid
        ).astype(jnp.bfloat16)
        from_rows = (
            lax.broadcasted_iota(jnp.int32, (pick_count, link_count), 0) == pick_col
        ).astype(jnp.bfloat16)
        into = into + lax.dot_general(
            to_rows, from_rows, (((1,), (1,)), ((), ())), preferred_element_type=jnp.float32
        )
    for c in range(field_count):
        summed = jnp.dot(into, combo_ref[c], precision=HIGHEST, preferred_element_type=jnp.float32)
        for owner in range(owner_count):
            out_ref[owner, c] = summed[owner * row_count : (owner + 1) * row_count]


def remapped(lat, sources, remap_weights, owner_count, field_count, row_count, link_count):
    source_count = len(sources)
    col_count = sources[0].shape[1]
    tile_count = remap_weights.shape[1]
    vmem = pl.BlockSpec(memory_space=pltpu.VMEM)
    return pl.pallas_call(
        functools.partial(remap_kernel, link_count, source_count),
        out_shape=jax.ShapeDtypeStruct((owner_count, field_count, row_count, col_count), jnp.float32),
        in_specs=[pl.BlockSpec(memory_space=pltpu.SMEM)] + [vmem] * (source_count + 1),
        out_specs=vmem,
        scratch_shapes=[
            pltpu.VMEM((source_count * field_count * row_count, col_count), jnp.float32),
            pltpu.VMEM(
                (field_count, source_count * tile_count * row_count, col_count), jnp.float32
            ),
        ],
        interpret=INTERPRET,
    )(lat, *sources, remap_weights)


def surface_export(ground, previous, sea_float, ocean_side):
    slip_east = ground[0] - previous[0]
    slip_north = ground[1] - previous[1]
    wind_speed = jnp.sqrt(slip_east * slip_east + slip_north * slip_north + gust_speed * gust_speed)
    bulk_flux = jnp.stack(
        [
            drag_coeff * wind_speed * slip_east,
            drag_coeff * wind_speed * slip_north,
            heat_coeff * wind_speed * (previous[2] - ground[2]),
        ]
    )
    return jnp.where(ocean_side, ground, bulk_flux) * sea_float


def body(
    state,
    surface,
    sea_mask,
    coeffs,
    remap_weights,
    link_dest,
    link_src_row,
    link_dst_row,
    link_tile,
):
    fields = state[0]
    previous = surface[0]
    sea_float = sea_mask[0].astype(jnp.float32)
    level_coef = coeffs[0]
    tile_table = remap_weights[0]
    field_count, level_count, row_count, col_count = fields.shape
    tile_count = tile_table.shape[0]
    ocean_side = lax.axis_index("grp") == 1
    first_row = lax.axis_index("lat") * row_count
    total_rows = row_count * lax.axis_size("lat")
    peer_count = lax.axis_size("lat") * lax.axis_size("lon")
    width = field_count * col_count

    links = jnp.stack(
        [link_dest[0, :, 0], link_src_row[0], link_dst_row[0], link_tile[0]]
    ).astype(jnp.float32)
    flag = lax.axis_index("grp").astype(jnp.int32).reshape(1)
    payload = exported_block(flag, state, surface, sea_mask, links)
    lat_count = lax.axis_size("lat")
    lon_count = lax.axis_size("lon")
    copies = jnp.broadcast_to(payload[None], (lat_count,) + payload.shape)
    gathered = lax.all_to_all(copies, "lat", split_axis=0, concat_axis=0, tiled=True)
    sources = [gathered[i] for i in range(lat_count)]
    place = jnp.stack([lax.axis_index("lat"), lax.axis_index("lon")]).astype(jnp.int32)
    partial = remapped(place, sources, remap_weights, lon_count, field_count, row_count, links.shape[1])
    pieces = []
    for shift in range(lon_count):
        route = [
            (g * lon_count + j, (1 - g) * lon_count + (j + shift) % lon_count)
            for g in range(2)
            for j in range(lon_count)
        ]
        pieces.append(lax.ppermute(partial[shift], ("grp", "lon"), route))
    imported = functools.reduce(jnp.add, pieces) * sea_float

    gain = jnp.where(ocean_side, ocean_gain, air_gain)
    damping = jnp.where(ocean_side, 0.0, air_gain)
    ground = fields[:, 0] + sea_float * (gain * previous - damping * fields[:, 0])
    fields = jnp.concatenate([ground[:, None], fields[:, 1:]], 1)
    state_mask = jnp.where(ocean_side, sea_float, jnp.ones_like(sea_float))
    planes = jnp.concatenate(
        [fields.reshape(field_count * level_count, row_count, col_count), state_mask[None]], 0
    )
    wide_rows = -(-(row_count + 4 * SUBSTEPS) // 8) * 8
    wide_cols = -(-(col_count + 4 * SUBSTEPS) // 128) * 128
    wide = with_halo(planes, SUBSTEPS, wide_cols, wide_rows)
    local = jnp.arange(wide_rows, dtype=jnp.int32)
    row_index = first_row + jnp.where(local < wide_rows // 2 + row_count // 2, local, local - wide_rows)
    latitude = jnp.pi * (
        -1.0 / 3.0 + 2.0 / 3.0 * (row_index.astype(jnp.float32) + 0.5) / total_rows
    )
    coriolis = coriolis_scale * jnp.sin(latitude)
    inside = ((row_index >= 0) & (row_index < total_rows)).astype(jnp.float32)
    row_terms = jnp.stack([coriolis, inside])[:, :, None]
    fields = dynamics(coeffs, row_terms, wide, field_count, level_count, row_count, col_count)
    return (fields, imported[None])


def solution(mesh):
    placed = (
        P("grp", None, None, "lat", "lon"),
        P("grp", None, "lat", "lon"),
        P("grp", "lat", "lon"),
        P("grp", None, None),
        P("grp", None, None, None),
        P("grp", ("lat", "lon"), None),
        P("grp", ("lat", "lon")),
        P("grp", ("lat", "lon")),
        P("grp", ("lat", "lon")),
    )
    return jax.shard_map(
        body,
        mesh=mesh,
        in_specs=placed,
        out_specs=(P("grp", None, None, "lat", "lon"), P("grp", None, "lat", "lon")),
        check_vma=False,
    )
```

```python
import functools

import jax
import jax.numpy as jnp
from jax import lax
from jax.sharding import PartitionSpec as P
from jax.experimental import pallas as pl
from jax.experimental.pallas import tpu as pltpu

SUBSTEPS = 2


air_gain = 0.3
ocean_gain = 0.5
drag_coeff = 0.5
heat_coeff = 0.5
gust_speed = 0.5
coriolis_scale = 0.25

HIGHEST = lax.Precision.HIGHEST
INTERPRET = False


def shifted(part, axis, closed, forward):
    count = lax.axis_size(axis)
    ends = count if closed else count - 1
    if forward:
        route = [(i, (i + 1) % count) for i in range(ends)]
    else:
        route = [((i + 1) % count, i) for i in range(ends)]
    flat = lax.ppermute(part.reshape(-1), axis, route)
    return flat.reshape(part.shape)


def with_halo(cells, width, wide_cols, wide_rows):
    planes, rows, cols = cells.shape
    head = cells[:, :, :width]
    tail = cells[:, :, -width:]
    gap = jnp.zeros((planes, rows, wide_cols - cols - 2 * width), cells.dtype)
    cells = jnp.concatenate(
        [cells, shifted(head, "lon", True, False), gap, shifted(tail, "lon", True, True)], axis=2
    )
    head = cells[:, :width, :]
    tail = cells[:, rows - width : rows, :]
    gap = jnp.zeros((planes, wide_rows - rows - 2 * width, wide_cols), cells.dtype)
    return jnp.concatenate(
        [cells, shifted(head, "lat", False, False), gap, shifted(tail, "lat", False, True)], axis=1
    )


def stencil_kernel(coef_ref, wide_ref, out_ref, mid_ref):
    field_count, level_count, row_count, col_count = out_ref.shape[1:]
    wide_rows, wide_cols = wide_ref.shape[1:]
    turning_wide = wide_ref[field_count * level_count + 1]
    keep_wide = wide_ref[field_count * level_count] * wide_ref[field_count * level_count + 2]

    def step(read, write, rows, cols):
        turning = turning_wide[:rows, :cols]
        keep = keep_wide[:rows, :cols]
        for field in range(field_count):
            for level in range(level_count):
                diffuse = coef_ref[0, 0, level]
                advect_east = coef_ref[0, 1, level]
                advect_north = coef_ref[0, 2, level]
                mixing = coef_ref[0, 3, level]
                whole = read(field, level)
                north = pltpu.roll(whole, wide_rows - 1, 0)[:rows, :cols]
                south = pltpu.roll(whole, 1, 0)[:rows, :cols]
                east = pltpu.roll(whole, wide_cols - 1, 1)[:rows, :cols]
                west = pltpu.roll(whole, 1, 1)[:rows, :cols]
                center = whole[:rows, :cols]
                above = read(field, min(level + 1, level_count - 1))[:rows, :cols]
                below = read(field, max(level - 1, 0))[:rows, :cols]
                laplace = north + south + east + west - 4.0 * center
                updated = (
                    center
                    + diffuse * laplace
                    - advect_east * (east - west)
                    - advect_north * (north - south)
                    + mixing * (above + below - 2.0 * center)
                )
                if field == 0:
                    updated = updated + turning * read(1, level)[:rows, :cols]
                elif field == 1:
                    updated = updated + (-turning) * read(0, level)[:rows, :cols]
                write(field, level, updated * keep)

    def from_wide(field, level):
        return wide_ref[field * level_count + level]

    def to_mid(field, level, value):
        mid_ref[field * level_count + level] = value

    def from_mid(field, level):
        return mid_ref[field * level_count + level]

    def to_out(field, level, value):
        out_ref[0, field, level] = value

    step(from_wide, to_mid, wide_rows, wide_cols)
    step(from_mid, to_out, row_count, col_count)


def dynamics(coeffs, wide, field_count, level_count, row_count, col_count):
    planes, wide_rows, wide_cols = wide.shape
    return pl.pallas_call(
        stencil_kernel,
        out_shape=jax.ShapeDtypeStruct((1, field_count, level_count, row_count, col_count), jnp.float32),
        in_specs=[
            pl.BlockSpec(memory_space=pltpu.SMEM),
            pl.BlockSpec(memory_space=pltpu.VMEM),
        ],
        out_specs=pl.BlockSpec(memory_space=pltpu.VMEM),
        scratch_shapes=[pltpu.VMEM((planes - 3, wide_rows, wide_cols), jnp.float32)],
        interpret=INTERPRET,
    )(coeffs, wide)


def export_kernel(flag_ref, ground_ref, previous_ref, sea_ref, link_ref, out_ref):
    field_count, row_count, col_count = previous_ref.shape[1:]
    link_fields, link_count = link_ref.shape
    ground = ground_ref[0, :, 0]
    previous = previous_ref[0]
    sea_float = sea_ref[0].astype(jnp.float32)
    ocean = (flag_ref[0] == 1).astype(jnp.float32)
    slip_east = ground[0] - previous[0]
    slip_north = ground[1] - previous[1]
    wind_speed = jnp.sqrt(slip_east * slip_east + slip_north * slip_north + gust_speed * gust_speed)
    bulk_flux = [
        drag_coeff * wind_speed * slip_east,
        drag_coeff * wind_speed * slip_north,
        heat_coeff * wind_speed * (previous[2] - ground[2]),
    ]
    for c in range(field_count):
        out_ref[c * row_count : (c + 1) * row_count, :] = (
            ground[c] * ocean + bulk_flux[c] * (1.0 - ocean)
        ) * sea_float
    base = field_count * row_count
    out_ref[base : base + 8, :] = jnp.zeros((8, col_count), jnp.float32)
    out_ref[base : base + link_fields, :link_count] = link_ref[...]


def exported_block(flag, state, surface, sea_mask, links):
    field_count, row_count, col_count = surface.shape[1:]
    vmem = pl.BlockSpec(memory_space=pltpu.VMEM)
    return pl.pallas_call(
        export_kernel,
        out_shape=jax.ShapeDtypeStruct((field_count * row_count + 8, col_count), jnp.float32),
        in_specs=[
            pl.BlockSpec(memory_space=pltpu.SMEM),
            pl.BlockSpec((1, field_count, 1, row_count, col_count), lambda i: (0, 0, 0, 0, 0)),
            vmem,
            vmem,
            vmem,
        ],
        out_specs=vmem,
        grid=(1,),
        interpret=INTERPRET,
    )(flag, state, surface, sea_mask, links)


def remap_kernel(link_count, source_count, place_ref, *refs):
    source_refs = refs[:source_count]
    table_ref = refs[source_count]
    tile_count = table_ref.shape[1]
    out_refs = refs[source_count + 1 : -4]
    rows_ref, combo_ref, weight_ref, copy_sems = refs[-4:]
    owner_count = len(out_refs)
    field_count, row_count, col_count = out_refs[0].shape
    copies = [
        pltpu.make_async_copy(table_ref.at[0, tile], weight_ref.at[tile], copy_sems.at[tile])
        for tile in range(tile_count)
    ]
    for copy in copies:
        copy.start()
    base = field_count * row_count
    my_lat = place_ref[0]
    my_lon = place_ref[1]
    for source in range(source_count):
        rows_ref[source * base : (source + 1) * base, :] = source_refs[source][:base, :]
    for tile in range(tile_count):
        copies[tile].wait()
        weighted = jnp.dot(
            rows_ref[...], weight_ref[tile], precision=HIGHEST, preferred_element_type=jnp.float32
        )
        for source in range(source_count):
            for c in range(field_count):
                first = (source * tile_count + tile) * row_count
                combo_ref[c, first : first + row_count, :] = weighted[
                    source * base + c * row_count : source * base + (c + 1) * row_count
                ]
    pick_count = source_count * tile_count * row_count
    into = jnp.zeros((owner_count * row_count, pick_count), jnp.float32)
    for source in range(source_count):
        table = source_refs[source][base : base + 4, :link_count].astype(jnp.int32)
        dest, src_row, dst_row, tile = table[0:1], table[1:2], table[2:3], table[3:4]
        low = my_lat * owner_count
        valid = (dest >= low) & (dest < low + owner_count)
        shift = dest - low - my_lon
        shift = jnp.where(shift < 0, shift + owner_count, shift)
        dest_col = shift * row_count + dst_row
        pick_col = (source * tile_count + tile) * row_count + src_row
        to_rows = (
            (lax.broadcasted_iota(jnp.int32, (owner_count * row_count, link_count), 0) == dest_col)
            & valid
        ).astype(jnp.bfloat16)
        from_rows = (
            lax.broadcasted_iota(jnp.int32, (pick_count, link_count), 0) == pick_col
        ).astype(jnp.bfloat16)
        into = into + lax.dot_general(
            to_rows, from_rows, (((1,), (1,)), ((), ())), preferred_element_type=jnp.float32
        )
    for c in range(field_count):
        summed = jnp.dot(into, combo_ref[c], precision=HIGHEST, preferred_element_type=jnp.float32)
        for owner in range(owner_count):
            out_refs[owner][c] = summed[owner * row_count : (owner + 1) * row_count]


def remapped(lat, sources, remap_weights, owner_count, field_count, row_count, link_count):
    source_count = len(sources)
    col_count = sources[0].shape[1]
    tile_count = remap_weights.shape[1]
    vmem = pl.BlockSpec(memory_space=pltpu.VMEM)
    return pl.pallas_call(
        functools.partial(remap_kernel, link_count, source_count),
        out_shape=[
            jax.ShapeDtypeStruct((field_count, row_count, col_count), jnp.float32)
            for owner in range(owner_count)
        ],
        in_specs=[pl.BlockSpec(memory_space=pltpu.SMEM)]
        + [vmem] * source_count
        + [pl.BlockSpec(memory_space=pl.ANY)],
        out_specs=[vmem] * owner_count,
        scratch_shapes=[
            pltpu.VMEM((source_count * field_count * row_count, col_count), jnp.float32),
            pltpu.VMEM(
                (field_count, source_count * tile_count * row_count, col_count), jnp.float32
            ),
            pltpu.VMEM(remap_weights.shape[1:], jnp.float32),
            pltpu.SemaphoreType.DMA((tile_count,)),
        ],
        interpret=INTERPRET,
    )(lat, *sources, remap_weights)


def surface_export(ground, previous, sea_float, ocean_side):
    slip_east = ground[0] - previous[0]
    slip_north = ground[1] - previous[1]
    wind_speed = jnp.sqrt(slip_east * slip_east + slip_north * slip_north + gust_speed * gust_speed)
    bulk_flux = jnp.stack(
        [
            drag_coeff * wind_speed * slip_east,
            drag_coeff * wind_speed * slip_north,
            heat_coeff * wind_speed * (previous[2] - ground[2]),
        ]
    )
    return jnp.where(ocean_side, ground, bulk_flux) * sea_float


def body(
    state,
    surface,
    sea_mask,
    coeffs,
    remap_weights,
    link_dest,
    link_src_row,
    link_dst_row,
    link_tile,
):
    fields = state[0]
    previous = surface[0]
    sea_float = sea_mask[0].astype(jnp.float32)
    level_coef = coeffs[0]
    tile_table = remap_weights[0]
    field_count, level_count, row_count, col_count = fields.shape
    tile_count = tile_table.shape[0]
    ocean_side = lax.axis_index("grp") == 1
    first_row = lax.axis_index("lat") * row_count
    total_rows = row_count * lax.axis_size("lat")
    peer_count = lax.axis_size("lat") * lax.axis_size("lon")
    width = field_count * col_count

    links = jnp.stack(
        [link_dest[0, :, 0], link_src_row[0], link_dst_row[0], link_tile[0]]
    ).astype(jnp.float32)
    flag = lax.axis_index("grp").astype(jnp.int32).reshape(1)
    payload = exported_block(flag, state, surface, sea_mask, links)
    lat_count = lax.axis_size("lat")
    lon_count = lax.axis_size("lon")
    sources = [payload] + [
        lax.ppermute(payload, "lat", [(i, (i + shift) % lat_count) for i in range(lat_count)])
        for shift in range(1, lat_count)
    ]
    place = jnp.stack([lax.axis_index("lat"), lax.axis_index("lon")]).astype(jnp.int32)
    partial = remapped(place, sources, remap_weights, lon_count, field_count, row_count, links.shape[1])
    pieces = []
    for shift in range(lon_count):
        route = [
            (g * lon_count + j, (1 - g) * lon_count + (j + shift) % lon_count)
            for g in range(2)
            for j in range(lon_count)
        ]
        pieces.append(lax.ppermute(partial[shift], ("grp", "lon"), route))
    imported = functools.reduce(jnp.add, pieces) * sea_float

    gain = jnp.where(ocean_side, ocean_gain, air_gain)
    damping = jnp.where(ocean_side, 0.0, air_gain)
    ground = fields[:, 0] + sea_float * (gain * previous - damping * fields[:, 0])
    fields = jnp.concatenate([ground[:, None], fields[:, 1:]], 1)
    state_mask = jnp.where(ocean_side, sea_float, jnp.ones_like(sea_float))
    planes = jnp.concatenate(
        [fields.reshape(field_count * level_count, row_count, col_count), state_mask[None]], 0
    )
    wide_rows = -(-(row_count + 4 * SUBSTEPS) // 8) * 8
    wide_cols = -(-(col_count + 4 * SUBSTEPS) // 128) * 128
    wide = with_halo(planes, SUBSTEPS, wide_cols, wide_rows)
    local = jnp.arange(wide_rows, dtype=jnp.int32)
    row_index = first_row + jnp.where(local < wide_rows // 2 + row_count // 2, local, local - wide_rows)
    latitude = jnp.pi * (
        -1.0 / 3.0 + 2.0 / 3.0 * (row_index.astype(jnp.float32) + 0.5) / total_rows
    )
    coriolis = coriolis_scale * jnp.sin(latitude)
    inside = ((row_index >= 0) & (row_index < total_rows)).astype(jnp.float32)
    row_terms = jnp.broadcast_to(jnp.stack([coriolis, inside])[:, :, None], (2, wide_rows, wide_cols))
    wide = jnp.concatenate([wide, row_terms], 0)
    fields = dynamics(coeffs, wide, field_count, level_count, row_count, col_count)
    return (fields, imported[None])


def solution(mesh):
    placed = (
        P("grp", None, None, "lat", "lon"),
        P("grp", None, "lat", "lon"),
        P("grp", "lat", "lon"),
        P("grp", None, None),
        P("grp", None, None, None),
        P("grp", ("lat", "lon"), None),
        P("grp", ("lat", "lon")),
        P("grp", ("lat", "lon")),
        P("grp", ("lat", "lon")),
    )
    return jax.shard_map(
        body,
        mesh=mesh,
        in_specs=placed,
        out_specs=(P("grp", None, None, "lat", "lon"), P("grp", None, "lat", "lon")),
        check_vma=False,
    )
```

```python
import functools

import jax
import jax.numpy as jnp
from jax import lax
from jax.sharding import PartitionSpec as P
from jax.experimental import pallas as pl
from jax.experimental.pallas import tpu as pltpu

SUBSTEPS = 2


air_gain = 0.3
ocean_gain = 0.5
drag_coeff = 0.5
heat_coeff = 0.5
gust_speed = 0.5
coriolis_scale = 0.25

HIGHEST = lax.Precision.HIGHEST
INTERPRET = False


def shifted(part, axis, closed, forward):
    count = lax.axis_size(axis)
    ends = count if closed else count - 1
    if forward:
        route = [(i, (i + 1) % count) for i in range(ends)]
    else:
        route = [((i + 1) % count, i) for i in range(ends)]
    flat = lax.ppermute(part.reshape(-1), axis, route)
    return flat.reshape(part.shape)


def with_halo(cells, width, wide_cols, wide_rows):
    planes, rows, cols = cells.shape
    head = cells[:, :, :width]
    tail = cells[:, :, -width:]
    gap = jnp.zeros((planes, rows, wide_cols - cols - 2 * width), cells.dtype)
    cells = jnp.concatenate(
        [cells, shifted(head, "lon", True, False), gap, shifted(tail, "lon", True, True)], axis=2
    )
    head = cells[:, :width, :]
    tail = cells[:, rows - width : rows, :]
    gap = jnp.zeros((planes, wide_rows - rows - 2 * width, wide_cols), cells.dtype)
    return jnp.concatenate(
        [cells, shifted(head, "lat", False, False), gap, shifted(tail, "lat", False, True)], axis=1
    )


def stencil_kernel(coef_ref, row_ref, wide_ref, out_ref, mid_ref):
    field_count, level_count, row_count, col_count = out_ref.shape[1:]
    wide_rows, wide_cols = wide_ref.shape[1:]
    turning_wide = jnp.broadcast_to(row_ref[0], (wide_rows, wide_cols))
    keep_wide = wide_ref[field_count * level_count] * jnp.broadcast_to(row_ref[1], (wide_rows, wide_cols))

    def step(read, write, rows, cols):
        turning = turning_wide[:rows, :cols]
        keep = keep_wide[:rows, :cols]
        for field in range(field_count):
            for level in range(level_count):
                diffuse = coef_ref[0, 0, level]
                advect_east = coef_ref[0, 1, level]
                advect_north = coef_ref[0, 2, level]
                mixing = coef_ref[0, 3, level]
                own_weight = 1.0 - 4.0 * diffuse - 2.0 * mixing
                north_weight = diffuse - advect_north
                south_weight = diffuse + advect_north
                east_weight = diffuse - advect_east
                west_weight = diffuse + advect_east
                whole = read(field, level)
                north = pltpu.roll(whole, wide_rows - 1, 0)[:rows, :cols]
                south = pltpu.roll(whole, 1, 0)[:rows, :cols]
                east = pltpu.roll(whole, wide_cols - 1, 1)[:rows, :cols]
                west = pltpu.roll(whole, 1, 1)[:rows, :cols]
                center = whole[:rows, :cols]
                above = read(field, min(level + 1, level_count - 1))[:rows, :cols]
                below = read(field, max(level - 1, 0))[:rows, :cols]
                updated = (
                    own_weight * center
                    + north_weight * north
                    + south_weight * south
                    + east_weight * east
                    + west_weight * west
                    + mixing * (above + below)
                )
                if field == 0:
                    updated = updated + turning * read(1, level)[:rows, :cols]
                elif field == 1:
                    updated = updated + (-turning) * read(0, level)[:rows, :cols]
                write(field, level, updated * keep)

    def from_wide(field, level):
        return wide_ref[field * level_count + level]

    def to_mid(field, level, value):
        mid_ref[field * level_count + level] = value

    def from_mid(field, level):
        return mid_ref[field * level_count + level]

    def to_out(field, level, value):
        out_ref[0, field, level] = value

    step(from_wide, to_mid, wide_rows, wide_cols)
    step(from_mid, to_out, row_count, col_count)


def dynamics(coeffs, row_terms, wide, field_count, level_count, row_count, col_count):
    planes, wide_rows, wide_cols = wide.shape
    return pl.pallas_call(
        stencil_kernel,
        out_shape=jax.ShapeDtypeStruct((1, field_count, level_count, row_count, col_count), jnp.float32),
        in_specs=[
            pl.BlockSpec(memory_space=pltpu.SMEM),
            pl.BlockSpec(memory_space=pltpu.VMEM),
            pl.BlockSpec(memory_space=pltpu.VMEM),
        ],
        out_specs=pl.BlockSpec(memory_space=pltpu.VMEM),
        scratch_shapes=[pltpu.VMEM((planes - 1, wide_rows, wide_cols), jnp.float32)],
        interpret=INTERPRET,
    )(coeffs, row_terms, wide)


def export_kernel(flag_ref, ground_ref, previous_ref, sea_ref, link_ref, out_ref):
    field_count, row_count, col_count = previous_ref.shape[1:]
    link_fields, link_count = link_ref.shape
    ground = ground_ref[0, :, 0]
    previous = previous_ref[0]
    sea_float = sea_ref[0].astype(jnp.float32)
    ocean = (flag_ref[0] == 1).astype(jnp.float32)
    slip_east = ground[0] - previous[0]
    slip_north = ground[1] - previous[1]
    wind_speed = jnp.sqrt(slip_east * slip_east + slip_north * slip_north + gust_speed * gust_speed)
    bulk_flux = [
        drag_coeff * wind_speed * slip_east,
        drag_coeff * wind_speed * slip_north,
        heat_coeff * wind_speed * (previous[2] - ground[2]),
    ]
    for c in range(field_count):
        out_ref[c * row_count : (c + 1) * row_count, :] = (
            ground[c] * ocean + bulk_flux[c] * (1.0 - ocean)
        ) * sea_float
    base = field_count * row_count
    out_ref[base : base + 8, :] = jnp.zeros((8, col_count), jnp.float32)
    out_ref[base : base + link_fields, :link_count] = link_ref[...]


def exported_block(flag, state, surface, sea_mask, links):
    field_count, row_count, col_count = surface.shape[1:]
    vmem = pl.BlockSpec(memory_space=pltpu.VMEM)
    return pl.pallas_call(
        export_kernel,
        out_shape=jax.ShapeDtypeStruct((field_count * row_count + 8, col_count), jnp.float32),
        in_specs=[
            pl.BlockSpec(memory_space=pltpu.SMEM),
            pl.BlockSpec((1, field_count, 1, row_count, col_count), lambda i: (0, 0, 0, 0, 0)),
            vmem,
            vmem,
            vmem,
        ],
        out_specs=vmem,
        grid=(1,),
        interpret=INTERPRET,
    )(flag, state, surface, sea_mask, links)


def remap_kernel(link_count, source_count, place_ref, *refs):
    source_refs = refs[:source_count]
    table_ref = refs[source_count]
    tile_count = table_ref.shape[1]
    out_refs = refs[source_count + 1 : -2]
    rows_ref, combo_ref = refs[-2:]
    owner_count = len(out_refs)
    field_count, row_count, col_count = out_refs[0].shape
    base = field_count * row_count
    my_lat = place_ref[0]
    my_lon = place_ref[1]
    for source in range(source_count):
        rows_ref[source * base : (source + 1) * base, :] = source_refs[source][:base, :]
    for tile in range(tile_count):
        weighted = jnp.dot(
            rows_ref[...], table_ref[0, tile], precision=HIGHEST, preferred_element_type=jnp.float32
        )
        for source in range(source_count):
            for c in range(field_count):
                first = (source * tile_count + tile) * row_count
                combo_ref[c, first : first + row_count, :] = weighted[
                    source * base + c * row_count : source * base + (c + 1) * row_count
                ]
    pick_count = source_count * tile_count * row_count
    into = jnp.zeros((owner_count * row_count, pick_count), jnp.float32)
    for source in range(source_count):
        table = source_refs[source][base : base + 4, :link_count].astype(jnp.int32)
        dest, src_row, dst_row, tile = table[0:1], table[1:2], table[2:3], table[3:4]
        low = my_lat * owner_count
        valid = (dest >= low) & (dest < low + owner_count)
        shift = dest - low - my_lon
        shift = jnp.where(shift < 0, shift + owner_count, shift)
        dest_col = shift * row_count + dst_row
        pick_col = (source * tile_count + tile) * row_count + src_row
        to_rows = (
            (lax.broadcasted_iota(jnp.int32, (owner_count * row_count, link_count), 0) == dest_col)
            & valid
        ).astype(jnp.bfloat16)
        from_rows = (
            lax.broadcasted_iota(jnp.int32, (pick_count, link_count), 0) == pick_col
        ).astype(jnp.bfloat16)
        into = into + lax.dot_general(
            to_rows, from_rows, (((1,), (1,)), ((), ())), preferred_element_type=jnp.float32
        )
    for c in range(field_count):
        summed = jnp.dot(into, combo_ref[c], precision=HIGHEST, preferred_element_type=jnp.float32)
        for owner in range(owner_count):
            out_refs[owner][c] = summed[owner * row_count : (owner + 1) * row_count]


def remapped(lat, sources, remap_weights, owner_count, field_count, row_count, link_count):
    source_count = len(sources)
    col_count = sources[0].shape[1]
    tile_count = remap_weights.shape[1]
    vmem = pl.BlockSpec(memory_space=pltpu.VMEM)
    return pl.pallas_call(
        functools.partial(remap_kernel, link_count, source_count),
        out_shape=[
            jax.ShapeDtypeStruct((field_count, row_count, col_count), jnp.float32)
            for owner in range(owner_count)
        ],
        in_specs=[pl.BlockSpec(memory_space=pltpu.SMEM)] + [vmem] * (source_count + 1),
        out_specs=[vmem] * owner_count,
        scratch_shapes=[
            pltpu.VMEM((source_count * field_count * row_count, col_count), jnp.float32),
            pltpu.VMEM(
                (field_count, source_count * tile_count * row_count, col_count), jnp.float32
            ),
        ],
        interpret=INTERPRET,
    )(lat, *sources, remap_weights)


def surface_export(ground, previous, sea_float, ocean_side):
    slip_east = ground[0] - previous[0]
    slip_north = ground[1] - previous[1]
    wind_speed = jnp.sqrt(slip_east * slip_east + slip_north * slip_north + gust_speed * gust_speed)
    bulk_flux = jnp.stack(
        [
            drag_coeff * wind_speed * slip_east,
            drag_coeff * wind_speed * slip_north,
            heat_coeff * wind_speed * (previous[2] - ground[2]),
        ]
    )
    return jnp.where(ocean_side, ground, bulk_flux) * sea_float


def body(
    state,
    surface,
    sea_mask,
    coeffs,
    remap_weights,
    link_dest,
    link_src_row,
    link_dst_row,
    link_tile,
):
    fields = state[0]
    previous = surface[0]
    sea_float = sea_mask[0].astype(jnp.float32)
    level_coef = coeffs[0]
    tile_table = remap_weights[0]
    field_count, level_count, row_count, col_count = fields.shape
    tile_count = tile_table.shape[0]
    ocean_side = lax.axis_index("grp") == 1
    first_row = lax.axis_index("lat") * row_count
    total_rows = row_count * lax.axis_size("lat")
    peer_count = lax.axis_size("lat") * lax.axis_size("lon")
    width = field_count * col_count

    links = jnp.stack(
        [link_dest[0, :, 0], link_src_row[0], link_dst_row[0], link_tile[0]]
    ).astype(jnp.float32)
    flag = lax.axis_index("grp").astype(jnp.int32).reshape(1)
    payload = exported_block(flag, state, surface, sea_mask, links)
    lat_count = lax.axis_size("lat")
    lon_count = lax.axis_size("lon")
    sources = [payload] + [
        lax.ppermute(payload, "lat", [(i, (i + shift) % lat_count) for i in range(lat_count)])
        for shift in range(1, lat_count)
    ]
    place = jnp.stack([lax.axis_index("lat"), lax.axis_index("lon")]).astype(jnp.int32)
    partial = remapped(place, sources, remap_weights, lon_count, field_count, row_count, links.shape[1])
    pieces = []
    for shift in range(lon_count):
        route = [
            (g * lon_count + j, (1 - g) * lon_count + (j + shift) % lon_count)
            for g in range(2)
            for j in range(lon_count)
        ]
        pieces.append(lax.ppermute(partial[shift], ("grp", "lon"), route))
    imported = functools.reduce(jnp.add, pieces) * sea_float

    gain = jnp.where(ocean_side, ocean_gain, air_gain)
    damping = jnp.where(ocean_side, 0.0, air_gain)
    ground = fields[:, 0] + sea_float * (gain * previous - damping * fields[:, 0])
    fields = jnp.concatenate([ground[:, None], fields[:, 1:]], 1)
    state_mask = jnp.where(ocean_side, sea_float, jnp.ones_like(sea_float))
    planes = jnp.concatenate(
        [fields.reshape(field_count * level_count, row_count, col_count), state_mask[None]], 0
    )
    wide_rows = -(-(row_count + 4 * SUBSTEPS) // 8) * 8
    wide_cols = -(-(col_count + 4 * SUBSTEPS) // 128) * 128
    wide = with_halo(planes, SUBSTEPS, wide_cols, wide_rows)
    local = jnp.arange(wide_rows, dtype=jnp.int32)
    row_index = first_row + jnp.where(local < wide_rows // 2 + row_count // 2, local, local - wide_rows)
    latitude = jnp.pi * (
        -1.0 / 3.0 + 2.0 / 3.0 * (row_index.astype(jnp.float32) + 0.5) / total_rows
    )
    coriolis = coriolis_scale * jnp.sin(latitude)
    inside = ((row_index >= 0) & (row_index < total_rows)).astype(jnp.float32)
    row_terms = jnp.stack([coriolis, inside])[:, :, None]
    fields = dynamics(coeffs, row_terms, wide, field_count, level_count, row_count, col_count)
    return (fields, imported[None])


def solution(mesh):
    placed = (
        P("grp", None, None, "lat", "lon"),
        P("grp", None, "lat", "lon"),
        P("grp", "lat", "lon"),
        P("grp", None, None),
        P("grp", None, None, None),
        P("grp", ("lat", "lon"), None),
        P("grp", ("lat", "lon")),
        P("grp", ("lat", "lon")),
        P("grp", ("lat", "lon")),
    )
    return jax.shard_map(
        body,
        mesh=mesh,
        in_specs=placed,
        out_specs=(P("grp", None, None, "lat", "lon"), P("grp", None, "lat", "lon")),
        check_vma=False,
    )
```

```python
import functools

import jax
import jax.numpy as jnp
from jax import lax
from jax.sharding import PartitionSpec as P
from jax.experimental import pallas as pl
from jax.experimental.pallas import tpu as pltpu

SUBSTEPS = 2


air_gain = 0.3
ocean_gain = 0.5
drag_coeff = 0.5
heat_coeff = 0.5
gust_speed = 0.5
coriolis_scale = 0.25

HIGHEST = lax.Precision.HIGHEST
INTERPRET = False


def shifted(part, axis, closed, forward):
    count = lax.axis_size(axis)
    ends = count if closed else count - 1
    if forward:
        route = [(i, (i + 1) % count) for i in range(ends)]
    else:
        route = [((i + 1) % count, i) for i in range(ends)]
    flat = lax.ppermute(part.reshape(-1), axis, route)
    return flat.reshape(part.shape)


def with_halo(cells, width, wide_cols, wide_rows):
    planes, rows, cols = cells.shape
    head = cells[:, :, :width]
    tail = cells[:, :, -width:]
    gap = jnp.zeros((planes, rows, wide_cols - cols - 2 * width), cells.dtype)
    cells = jnp.concatenate(
        [cells, shifted(head, "lon", True, False), gap, shifted(tail, "lon", True, True)], axis=2
    )
    head = cells[:, :width, :]
    tail = cells[:, rows - width : rows, :]
    gap = jnp.zeros((planes, wide_rows - rows - 2 * width, wide_cols), cells.dtype)
    return jnp.concatenate(
        [cells, shifted(head, "lat", False, False), gap, shifted(tail, "lat", False, True)], axis=1
    )


def stencil_kernel(coef_ref, row_ref, wide_ref, out_ref, mid_ref):
    field_count, level_count, row_count, col_count = out_ref.shape[1:]
    wide_rows, wide_cols = wide_ref.shape[1:]
    turning_wide = jnp.broadcast_to(row_ref[0], (wide_rows, wide_cols))
    keep_wide = wide_ref[field_count * level_count] * jnp.broadcast_to(row_ref[1], (wide_rows, wide_cols))

    def step(read, write, rows, cols):
        turning = turning_wide[:rows, :cols]
        keep = keep_wide[:rows, :cols]
        for field in range(field_count):
            for level in range(level_count):
                diffuse = coef_ref[0, 0, level]
                advect_east = coef_ref[0, 1, level]
                advect_north = coef_ref[0, 2, level]
                mixing = coef_ref[0, 3, level]
                own_weight = 1.0 - 4.0 * diffuse - 2.0 * mixing
                north_weight = diffuse - advect_north
                south_weight = diffuse + advect_north
                east_weight = diffuse - advect_east
                west_weight = diffuse + advect_east
                whole = read(field, level)
                north = pltpu.roll(whole, wide_rows - 1, 0)[:rows, :cols]
                south = pltpu.roll(whole, 1, 0)[:rows, :cols]
                east = pltpu.roll(whole, wide_cols - 1, 1)[:rows, :cols]
                west = pltpu.roll(whole, 1, 1)[:rows, :cols]
                center = whole[:rows, :cols]
                above = read(field, min(level + 1, level_count - 1))[:rows, :cols]
                below = read(field, max(level - 1, 0))[:rows, :cols]
                updated = (
                    own_weight * center
                    + north_weight * north
                    + south_weight * south
                    + east_weight * east
                    + west_weight * west
                    + mixing * (above + below)
                )
                if field == 0:
                    updated = updated + turning * read(1, level)[:rows, :cols]
                elif field == 1:
                    updated = updated + (-turning) * read(0, level)[:rows, :cols]
                write(field, level, updated * keep)

    def from_wide(field, level):
        return wide_ref[field * level_count + level]

    def to_mid(field, level, value):
        mid_ref[field * level_count + level] = value

    def from_mid(field, level):
        return mid_ref[field * level_count + level]

    def to_out(field, level, value):
        out_ref[0, field, level] = value

    step(from_wide, to_mid, wide_rows, wide_cols)
    step(from_mid, to_out, row_count, col_count)


def dynamics(coeffs, row_terms, wide, field_count, level_count, row_count, col_count):
    planes, wide_rows, wide_cols = wide.shape
    return pl.pallas_call(
        stencil_kernel,
        out_shape=jax.ShapeDtypeStruct((1, field_count, level_count, row_count, col_count), jnp.float32),
        in_specs=[
            pl.BlockSpec(memory_space=pltpu.SMEM),
            pl.BlockSpec(memory_space=pltpu.VMEM),
            pl.BlockSpec(memory_space=pltpu.VMEM),
        ],
        out_specs=pl.BlockSpec(memory_space=pltpu.VMEM),
        scratch_shapes=[pltpu.VMEM((planes - 1, wide_rows, wide_cols), jnp.float32)],
        interpret=INTERPRET,
    )(coeffs, row_terms, wide)


def export_kernel(flag_ref, ground_ref, previous_ref, sea_ref, link_ref, out_ref):
    field_count, row_count, col_count = previous_ref.shape[1:]
    link_fields, link_count = link_ref.shape
    ground = ground_ref[0, :, 0]
    previous = previous_ref[0]
    sea_float = sea_ref[0].astype(jnp.float32)
    ocean = (flag_ref[0] == 1).astype(jnp.float32)
    slip_east = ground[0] - previous[0]
    slip_north = ground[1] - previous[1]
    wind_speed = jnp.sqrt(slip_east * slip_east + slip_north * slip_north + gust_speed * gust_speed)
    bulk_flux = [
        drag_coeff * wind_speed * slip_east,
        drag_coeff * wind_speed * slip_north,
        heat_coeff * wind_speed * (previous[2] - ground[2]),
    ]
    for c in range(field_count):
        out_ref[c * row_count : (c + 1) * row_count, :] = (
            ground[c] * ocean + bulk_flux[c] * (1.0 - ocean)
        ) * sea_float
    base = field_count * row_count
    out_ref[base : base + 8, :] = jnp.zeros((8, col_count), jnp.float32)
    out_ref[base : base + link_fields, :link_count] = link_ref[...]


def exported_block(flag, state, surface, sea_mask, links):
    field_count, row_count, col_count = surface.shape[1:]
    vmem = pl.BlockSpec(memory_space=pltpu.VMEM)
    return pl.pallas_call(
        export_kernel,
        out_shape=jax.ShapeDtypeStruct((field_count * row_count + 8, col_count), jnp.float32),
        in_specs=[
            pl.BlockSpec(memory_space=pltpu.SMEM),
            pl.BlockSpec((1, field_count, 1, row_count, col_count), lambda i: (0, 0, 0, 0, 0)),
            vmem,
            vmem,
            vmem,
        ],
        out_specs=vmem,
        grid=(1,),
        interpret=INTERPRET,
    )(flag, state, surface, sea_mask, links)


def remap_kernel(link_count, source_count, place_ref, *refs):
    source_refs = refs[:source_count]
    table_ref = refs[source_count]
    tile_count = table_ref.shape[1]
    out_refs = refs[source_count + 1 : -2]
    rows_ref, combo_ref = refs[-2:]
    owner_count = len(out_refs)
    field_count, row_count, col_count = out_refs[0].shape
    base = field_count * row_count
    my_lat = place_ref[0]
    my_lon = place_ref[1]
    for source in range(source_count):
        rows_ref[source * base : (source + 1) * base, :] = source_refs[source][:base, :]
    for tile in range(tile_count):
        weighted = jnp.dot(
            rows_ref[...], table_ref[0, tile], precision=lax.Precision.HIGH, preferred_element_type=jnp.float32
        )
        for source in range(source_count):
            for c in range(field_count):
                first = (source * tile_count + tile) * row_count
                combo_ref[c, first : first + row_count, :] = weighted[
                    source * base + c * row_count : source * base + (c + 1) * row_count
                ]
    pick_count = source_count * tile_count * row_count
    into = jnp.zeros((owner_count * row_count, pick_count), jnp.float32)
    for source in range(source_count):
        table = source_refs[source][base : base + 4, :link_count].astype(jnp.int32)
        dest, src_row, dst_row, tile = table[0:1], table[1:2], table[2:3], table[3:4]
        low = my_lat * owner_count
        valid = (dest >= low) & (dest < low + owner_count)
        shift = dest - low - my_lon
        shift = jnp.where(shift < 0, shift + owner_count, shift)
        dest_col = shift * row_count + dst_row
        pick_col = (source * tile_count + tile) * row_count + src_row
        to_rows = (
            (lax.broadcasted_iota(jnp.int32, (owner_count * row_count, link_count), 0) == dest_col)
            & valid
        ).astype(jnp.bfloat16)
        from_rows = (
            lax.broadcasted_iota(jnp.int32, (pick_count, link_count), 0) == pick_col
        ).astype(jnp.bfloat16)
        into = into + lax.dot_general(
            to_rows, from_rows, (((1,), (1,)), ((), ())), preferred_element_type=jnp.float32
        )
    for c in range(field_count):
        summed = jnp.dot(into, combo_ref[c], precision=lax.Precision.HIGH, preferred_element_type=jnp.float32)
        for owner in range(owner_count):
            out_refs[owner][c] = summed[owner * row_count : (owner + 1) * row_count]


def remapped(lat, sources, remap_weights, owner_count, field_count, row_count, link_count):
    source_count = len(sources)
    col_count = sources[0].shape[1]
    tile_count = remap_weights.shape[1]
    vmem = pl.BlockSpec(memory_space=pltpu.VMEM)
    return pl.pallas_call(
        functools.partial(remap_kernel, link_count, source_count),
        out_shape=[
            jax.ShapeDtypeStruct((field_count, row_count, col_count), jnp.float32)
            for owner in range(owner_count)
        ],
        in_specs=[pl.BlockSpec(memory_space=pltpu.SMEM)] + [vmem] * (source_count + 1),
        out_specs=[vmem] * owner_count,
        scratch_shapes=[
            pltpu.VMEM((source_count * field_count * row_count, col_count), jnp.float32),
            pltpu.VMEM(
                (field_count, source_count * tile_count * row_count, col_count), jnp.float32
            ),
        ],
        interpret=INTERPRET,
    )(lat, *sources, remap_weights)


def surface_export(ground, previous, sea_float, ocean_side):
    slip_east = ground[0] - previous[0]
    slip_north = ground[1] - previous[1]
    wind_speed = jnp.sqrt(slip_east * slip_east + slip_north * slip_north + gust_speed * gust_speed)
    bulk_flux = jnp.stack(
        [
            drag_coeff * wind_speed * slip_east,
            drag_coeff * wind_speed * slip_north,
            heat_coeff * wind_speed * (previous[2] - ground[2]),
        ]
    )
    return jnp.where(ocean_side, ground, bulk_flux) * sea_float


def body(
    state,
    surface,
    sea_mask,
    coeffs,
    remap_weights,
    link_dest,
    link_src_row,
    link_dst_row,
    link_tile,
):
    fields = state[0]
    previous = surface[0]
    sea_float = sea_mask[0].astype(jnp.float32)
    level_coef = coeffs[0]
    tile_table = remap_weights[0]
    field_count, level_count, row_count, col_count = fields.shape
    tile_count = tile_table.shape[0]
    ocean_side = lax.axis_index("grp") == 1
    first_row = lax.axis_index("lat") * row_count
    total_rows = row_count * lax.axis_size("lat")
    peer_count = lax.axis_size("lat") * lax.axis_size("lon")
    width = field_count * col_count

    links = jnp.stack(
        [link_dest[0, :, 0], link_src_row[0], link_dst_row[0], link_tile[0]]
    ).astype(jnp.float32)
    flag = lax.axis_index("grp").astype(jnp.int32).reshape(1)
    payload = exported_block(flag, state, surface, sea_mask, links)
    lat_count = lax.axis_size("lat")
    lon_count = lax.axis_size("lon")
    sources = [payload] + [
        lax.ppermute(payload, "lat", [(i, (i + shift) % lat_count) for i in range(lat_count)])
        for shift in range(1, lat_count)
    ]
    place = jnp.stack([lax.axis_index("lat"), lax.axis_index("lon")]).astype(jnp.int32)
    partial = remapped(place, sources, remap_weights, lon_count, field_count, row_count, links.shape[1])
    pieces = []
    for shift in range(lon_count):
        route = [
            (g * lon_count + j, (1 - g) * lon_count + (j + shift) % lon_count)
            for g in range(2)
            for j in range(lon_count)
        ]
        pieces.append(lax.ppermute(partial[shift], ("grp", "lon"), route))
    imported = functools.reduce(jnp.add, pieces) * sea_float

    gain = jnp.where(ocean_side, ocean_gain, air_gain)
    damping = jnp.where(ocean_side, 0.0, air_gain)
    ground = fields[:, 0] + sea_float * (gain * previous - damping * fields[:, 0])
    fields = jnp.concatenate([ground[:, None], fields[:, 1:]], 1)
    state_mask = jnp.where(ocean_side, sea_float, jnp.ones_like(sea_float))
    planes = jnp.concatenate(
        [fields.reshape(field_count * level_count, row_count, col_count), state_mask[None]], 0
    )
    wide_rows = -(-(row_count + 4 * SUBSTEPS) // 8) * 8
    wide_cols = -(-(col_count + 4 * SUBSTEPS) // 128) * 128
    wide = with_halo(planes, SUBSTEPS, wide_cols, wide_rows)
    local = jnp.arange(wide_rows, dtype=jnp.int32)
    row_index = first_row + jnp.where(local < wide_rows // 2 + row_count // 2, local, local - wide_rows)
    latitude = jnp.pi * (
        -1.0 / 3.0 + 2.0 / 3.0 * (row_index.astype(jnp.float32) + 0.5) / total_rows
    )
    coriolis = coriolis_scale * jnp.sin(latitude)
    inside = ((row_index >= 0) & (row_index < total_rows)).astype(jnp.float32)
    row_terms = jnp.stack([coriolis, inside])[:, :, None]
    fields = dynamics(coeffs, row_terms, wide, field_count, level_count, row_count, col_count)
    return (fields, imported[None])


def solution(mesh):
    placed = (
        P("grp", None, None, "lat", "lon"),
        P("grp", None, "lat", "lon"),
        P("grp", "lat", "lon"),
        P("grp", None, None),
        P("grp", None, None, None),
        P("grp", ("lat", "lon"), None),
        P("grp", ("lat", "lon")),
        P("grp", ("lat", "lon")),
        P("grp", ("lat", "lon")),
    )
    return jax.shard_map(
        body,
        mesh=mesh,
        in_specs=placed,
        out_specs=(P("grp", None, None, "lat", "lon"), P("grp", None, "lat", "lon")),
        check_vma=False,
    )
```

```python
import functools

import jax
import jax.numpy as jnp
from jax import lax
from jax.sharding import PartitionSpec as P
from jax.experimental import pallas as pl
from jax.experimental.pallas import tpu as pltpu

SUBSTEPS = 2


air_gain = 0.3
ocean_gain = 0.5
drag_coeff = 0.5
heat_coeff = 0.5
gust_speed = 0.5
coriolis_scale = 0.25

HIGHEST = lax.Precision.HIGHEST
INTERPRET = False


def shifted(part, axis, closed, forward):
    count = lax.axis_size(axis)
    ends = count if closed else count - 1
    if forward:
        route = [(i, (i + 1) % count) for i in range(ends)]
    else:
        route = [((i + 1) % count, i) for i in range(ends)]
    flat = lax.ppermute(part.reshape(-1), axis, route)
    return flat.reshape(part.shape)


def stencil_kernel(coef_ref, row_ref, wide_ref, out_ref, mid_ref):
    field_count, level_count, row_count, col_count = out_ref.shape[1:]
    wide_rows, wide_cols = wide_ref.shape[1:]
    turning_wide = jnp.broadcast_to(row_ref[0], (wide_rows, wide_cols))
    keep_wide = wide_ref[field_count * level_count] * jnp.broadcast_to(row_ref[1], (wide_rows, wide_cols))

    def step(read, write, rows, cols):
        turning = turning_wide[:rows, :cols]
        keep = keep_wide[:rows, :cols]
        for field in range(field_count):
            for level in range(level_count):
                diffuse = coef_ref[0, 0, level]
                advect_east = coef_ref[0, 1, level]
                advect_north = coef_ref[0, 2, level]
                mixing = coef_ref[0, 3, level]
                own_weight = 1.0 - 4.0 * diffuse - 2.0 * mixing
                north_weight = diffuse - advect_north
                south_weight = diffuse + advect_north
                east_weight = diffuse - advect_east
                west_weight = diffuse + advect_east
                whole = read(field, level)
                north = pltpu.roll(whole, wide_rows - 1, 0)[:rows, :cols]
                south = pltpu.roll(whole, 1, 0)[:rows, :cols]
                east = pltpu.roll(whole, wide_cols - 1, 1)[:rows, :cols]
                west = pltpu.roll(whole, 1, 1)[:rows, :cols]
                center = whole[:rows, :cols]
                above = read(field, min(level + 1, level_count - 1))[:rows, :cols]
                below = read(field, max(level - 1, 0))[:rows, :cols]
                updated = (
                    own_weight * center
                    + north_weight * north
                    + south_weight * south
                    + east_weight * east
                    + west_weight * west
                    + mixing * (above + below)
                )
                if field == 0:
                    updated = updated + turning * read(1, level)[:rows, :cols]
                elif field == 1:
                    updated = updated + (-turning) * read(0, level)[:rows, :cols]
                write(field, level, updated * keep)

    def from_wide(field, level):
        return wide_ref[field * level_count + level]

    def to_mid(field, level, value):
        mid_ref[field * level_count + level] = value

    def from_mid(field, level):
        return mid_ref[field * level_count + level]

    def to_out(field, level, value):
        out_ref[0, field, level] = value

    step(from_wide, to_mid, wide_rows, wide_cols)
    step(from_mid, to_out, row_count, col_count)


def dynamics(coeffs, row_terms, wide, field_count, level_count, row_count, col_count):
    planes, wide_rows, wide_cols = wide.shape
    return pl.pallas_call(
        stencil_kernel,
        out_shape=jax.ShapeDtypeStruct((1, field_count, level_count, row_count, col_count), jnp.float32),
        in_specs=[
            pl.BlockSpec(memory_space=pltpu.SMEM),
            pl.BlockSpec(memory_space=pltpu.VMEM),
            pl.BlockSpec(memory_space=pltpu.VMEM),
        ],
        out_specs=pl.BlockSpec(memory_space=pltpu.VMEM),
        scratch_shapes=[pltpu.VMEM((planes - 1, wide_rows, wide_cols), jnp.float32)],
        interpret=INTERPRET,
    )(coeffs, row_terms, wide)


def export_kernel(flag_ref, ground_ref, previous_ref, sea_ref, link_ref, out_ref):
    field_count, row_count, col_count = previous_ref.shape[1:]
    link_fields, link_count = link_ref.shape
    ground = ground_ref[0, :, 0]
    previous = previous_ref[0]
    sea_float = sea_ref[0].astype(jnp.float32)
    ocean = (flag_ref[0] == 1).astype(jnp.float32)
    slip_east = ground[0] - previous[0]
    slip_north = ground[1] - previous[1]
    wind_speed = jnp.sqrt(slip_east * slip_east + slip_north * slip_north + gust_speed * gust_speed)
    bulk_flux = [
        drag_coeff * wind_speed * slip_east,
        drag_coeff * wind_speed * slip_north,
        heat_coeff * wind_speed * (previous[2] - ground[2]),
    ]
    for c in range(field_count):
        out_ref[c * row_count : (c + 1) * row_count, :] = (
            ground[c] * ocean + bulk_flux[c] * (1.0 - ocean)
        ) * sea_float
    base = field_count * row_count
    out_ref[base : base + 8, :] = jnp.zeros((8, col_count), jnp.float32)
    out_ref[base : base + link_fields, :link_count] = link_ref[...]


def exported_block(flag, state, surface, sea_mask, links):
    field_count, row_count, col_count = surface.shape[1:]
    vmem = pl.BlockSpec(memory_space=pltpu.VMEM)
    return pl.pallas_call(
        export_kernel,
        out_shape=jax.ShapeDtypeStruct((field_count * row_count + 8, col_count), jnp.float32),
        in_specs=[
            pl.BlockSpec(memory_space=pltpu.SMEM),
            pl.BlockSpec((1, field_count, 1, row_count, col_count), lambda i: (0, 0, 0, 0, 0)),
            vmem,
            vmem,
            vmem,
        ],
        out_specs=vmem,
        grid=(1,),
        interpret=INTERPRET,
    )(flag, state, surface, sea_mask, links)


def remap_kernel(link_count, source_count, place_ref, *refs):
    source_refs = refs[:source_count]
    table_ref = refs[source_count]
    tile_count = table_ref.shape[1]
    out_refs = refs[source_count + 1 : -2]
    rows_ref, combo_ref = refs[-2:]
    owner_count = len(out_refs)
    field_count, row_count, col_count = out_refs[0].shape
    base = field_count * row_count
    my_lat = place_ref[0]
    my_lon = place_ref[1]
    for source in range(source_count):
        rows_ref[source * base : (source + 1) * base, :] = source_refs[source][:base, :]
    for tile in range(tile_count):
        weighted = jnp.dot(
            rows_ref[...], table_ref[0, tile], precision=lax.Precision.HIGH, preferred_element_type=jnp.float32
        )
        for source in range(source_count):
            for c in range(field_count):
                first = (source * tile_count + tile) * row_count
                combo_ref[c, first : first + row_count, :] = weighted[
                    source * base + c * row_count : source * base + (c + 1) * row_count
                ]
    pick_count = source_count * tile_count * row_count
    into = jnp.zeros((owner_count * row_count, pick_count), jnp.float32)
    for source in range(source_count):
        table = source_refs[source][base : base + 4, :link_count].astype(jnp.int32)
        dest, src_row, dst_row, tile = table[0:1], table[1:2], table[2:3], table[3:4]
        low = my_lat * owner_count
        valid = (dest >= low) & (dest < low + owner_count)
        shift = dest - low - my_lon
        shift = jnp.where(shift < 0, shift + owner_count, shift)
        dest_col = shift * row_count + dst_row
        pick_col = (source * tile_count + tile) * row_count + src_row
        to_rows = (
            (lax.broadcasted_iota(jnp.int32, (owner_count * row_count, link_count), 0) == dest_col)
            & valid
        ).astype(jnp.bfloat16)
        from_rows = (
            lax.broadcasted_iota(jnp.int32, (pick_count, link_count), 0) == pick_col
        ).astype(jnp.bfloat16)
        into = into + lax.dot_general(
            to_rows, from_rows, (((1,), (1,)), ((), ())), preferred_element_type=jnp.float32
        )
    for c in range(field_count):
        summed = jnp.dot(into, combo_ref[c], precision=lax.Precision.HIGH, preferred_element_type=jnp.float32)
        for owner in range(owner_count):
            out_refs[owner][c] = summed[owner * row_count : (owner + 1) * row_count]


def remapped(lat, sources, remap_weights, owner_count, field_count, row_count, link_count):
    source_count = len(sources)
    col_count = sources[0].shape[1]
    tile_count = remap_weights.shape[1]
    vmem = pl.BlockSpec(memory_space=pltpu.VMEM)
    return pl.pallas_call(
        functools.partial(remap_kernel, link_count, source_count),
        out_shape=[
            jax.ShapeDtypeStruct((field_count, row_count, col_count), jnp.float32)
            for owner in range(owner_count)
        ],
        in_specs=[pl.BlockSpec(memory_space=pltpu.SMEM)] + [vmem] * (source_count + 1),
        out_specs=[vmem] * owner_count,
        scratch_shapes=[
            pltpu.VMEM((source_count * field_count * row_count, col_count), jnp.float32),
            pltpu.VMEM(
                (field_count, source_count * tile_count * row_count, col_count), jnp.float32
            ),
        ],
        interpret=INTERPRET,
    )(lat, *sources, remap_weights)


def surface_export(ground, previous, sea_float, ocean_side):
    slip_east = ground[0] - previous[0]
    slip_north = ground[1] - previous[1]
    wind_speed = jnp.sqrt(slip_east * slip_east + slip_north * slip_north + gust_speed * gust_speed)
    bulk_flux = jnp.stack(
        [
            drag_coeff * wind_speed * slip_east,
            drag_coeff * wind_speed * slip_north,
            heat_coeff * wind_speed * (previous[2] - ground[2]),
        ]
    )
    return jnp.where(ocean_side, ground, bulk_flux) * sea_float


def body(
    state,
    surface,
    sea_mask,
    coeffs,
    remap_weights,
    link_dest,
    link_src_row,
    link_dst_row,
    link_tile,
):
    fields = state[0]
    previous = surface[0]
    sea_float = sea_mask[0].astype(jnp.float32)
    level_coef = coeffs[0]
    tile_table = remap_weights[0]
    field_count, level_count, row_count, col_count = fields.shape
    tile_count = tile_table.shape[0]
    ocean_side = lax.axis_index("grp") == 1
    first_row = lax.axis_index("lat") * row_count
    total_rows = row_count * lax.axis_size("lat")

    links = jnp.stack(
        [link_dest[0, :, 0], link_src_row[0], link_dst_row[0], link_tile[0]]
    ).astype(jnp.float32)
    flag = lax.axis_index("grp").astype(jnp.int32).reshape(1)
    payload = exported_block(flag, state, surface, sea_mask, links)
    lat_count = lax.axis_size("lat")
    lon_count = lax.axis_size("lon")
    gain = jnp.where(ocean_side, ocean_gain, air_gain)
    damping = jnp.where(ocean_side, 0.0, air_gain)
    ground = fields[:, 0] + sea_float * (gain * previous - damping * fields[:, 0])
    fields = jnp.concatenate([ground[:, None], fields[:, 1:]], 1)
    state_mask = jnp.where(ocean_side, sea_float, jnp.ones_like(sea_float))
    planes = jnp.concatenate(
        [fields.reshape(field_count * level_count, row_count, col_count), state_mask[None]], 0
    )
    plane_count = planes.shape[0]
    width = SUBSTEPS
    edge_rows = plane_count * width
    edge_pad = -(-edge_rows // 8) * 8 - edge_rows
    head = planes[:, :width, :].reshape(edge_rows, col_count)
    tail = planes[:, row_count - width :, :].reshape(edge_rows, col_count)
    gap_rows = jnp.zeros((edge_pad, col_count), jnp.float32)
    base = payload.shape[0]
    sources = [payload]
    south = north = None
    for shift in range(1, lat_count):
        parts = [payload]
        if shift == 1:
            parts += [tail, gap_rows]
        if shift == lat_count - 1:
            parts += [head, gap_rows]
        sent = jnp.concatenate(parts, 0) if len(parts) > 1 else payload
        got = lax.ppermute(sent, "lat", [(i, (i + shift) % lat_count) for i in range(lat_count)])
        sources.append(got)
        if shift == 1:
            south = got[base : base + edge_rows]
        if shift == lat_count - 1:
            start = base + (edge_rows + edge_pad if shift == 1 else 0)
            north = got[start : start + edge_rows]
    my_lat = lax.axis_index("lat")
    south = south.reshape(plane_count, width, col_count) * (my_lat > 0).astype(jnp.float32)
    north = north.reshape(plane_count, width, col_count) * (my_lat < lat_count - 1).astype(jnp.float32)
    place = jnp.stack([lax.axis_index("lat"), lax.axis_index("lon")]).astype(jnp.int32)
    partial = remapped(place, sources, remap_weights, lon_count, field_count, row_count, links.shape[1])
    pieces = []
    for shift in range(lon_count):
        route = [
            (g * lon_count + j, (1 - g) * lon_count + (j + shift) % lon_count)
            for g in range(2)
            for j in range(lon_count)
        ]
        pieces.append(lax.ppermute(partial[shift], ("grp", "lon"), route))
    imported = functools.reduce(jnp.add, pieces) * sea_float

    wide_rows = -(-(row_count + 4 * SUBSTEPS) // 8) * 8
    wide_cols = -(-(col_count + 4 * SUBSTEPS) // 128) * 128
    row_gap = jnp.zeros((plane_count, wide_rows - row_count - 2 * width, col_count), jnp.float32)
    stacked = jnp.concatenate([planes, north, row_gap, south], 1)
    col_gap = jnp.zeros((plane_count, wide_rows, wide_cols - col_count - 2 * width), jnp.float32)
    wide = jnp.concatenate(
        [
            stacked,
            shifted(stacked[:, :, :width], "lon", True, False),
            col_gap,
            shifted(stacked[:, :, col_count - width :], "lon", True, True),
        ],
        2,
    )
    local = jnp.arange(wide_rows, dtype=jnp.int32)
    row_index = first_row + jnp.where(local < wide_rows // 2 + row_count // 2, local, local - wide_rows)
    latitude = jnp.pi * (
        -1.0 / 3.0 + 2.0 / 3.0 * (row_index.astype(jnp.float32) + 0.5) / total_rows
    )
    coriolis = coriolis_scale * jnp.sin(latitude)
    inside = ((row_index >= 0) & (row_index < total_rows)).astype(jnp.float32)
    row_terms = jnp.stack([coriolis, inside])[:, :, None]
    fields = dynamics(coeffs, row_terms, wide, field_count, level_count, row_count, col_count)
    return (fields, imported[None])


def solution(mesh):
    placed = (
        P("grp", None, None, "lat", "lon"),
        P("grp", None, "lat", "lon"),
        P("grp", "lat", "lon"),
        P("grp", None, None),
        P("grp", None, None, None),
        P("grp", ("lat", "lon"), None),
        P("grp", ("lat", "lon")),
        P("grp", ("lat", "lon")),
        P("grp", ("lat", "lon")),
    )
    return jax.shard_map(
        body,
        mesh=mesh,
        in_specs=placed,
        out_specs=(P("grp", None, None, "lat", "lon"), P("grp", None, "lat", "lon")),
        check_vma=False,
    )
```

```python
import functools

import jax
import jax.numpy as jnp
from jax import lax
from jax.sharding import PartitionSpec as P
from jax.experimental import pallas as pl
from jax.experimental.pallas import tpu as pltpu

SUBSTEPS = 2


air_gain = 0.3
ocean_gain = 0.5
drag_coeff = 0.5
heat_coeff = 0.5
gust_speed = 0.5
coriolis_scale = 0.25

HIGHEST = lax.Precision.HIGHEST
INTERPRET = False


def shifted(part, axis, closed, forward):
    count = lax.axis_size(axis)
    ends = count if closed else count - 1
    if forward:
        route = [(i, (i + 1) % count) for i in range(ends)]
    else:
        route = [((i + 1) % count, i) for i in range(ends)]
    flat = lax.ppermute(part.reshape(-1), axis, route)
    return flat.reshape(part.shape)


def stencil_kernel(total_rows, coef_ref, place_ref, wide_ref, out_ref, mid_ref):
    field_count, level_count, row_count, col_count = out_ref.shape[1:]
    wide_rows, wide_cols = wide_ref.shape[1:]
    local = lax.broadcasted_iota(jnp.int32, (wide_rows, wide_cols), 0)
    row_index = place_ref[1] * row_count + jnp.where(
        local < wide_rows // 2 + row_count // 2, local, local - wide_rows
    )
    latitude = jnp.pi * (
        -1.0 / 3.0 + 2.0 / 3.0 * (row_index.astype(jnp.float32) + 0.5) / total_rows
    )
    turning_wide = coriolis_scale * jnp.sin(latitude)
    inside = ((row_index >= 0) & (row_index < total_rows)).astype(jnp.float32)
    keep_wide = wide_ref[field_count * level_count] * inside

    def step(read, write, rows, cols):
        turning = turning_wide[:rows, :cols]
        keep = keep_wide[:rows, :cols]
        for field in range(field_count):
            for level in range(level_count):
                diffuse = coef_ref[0, 0, level]
                advect_east = coef_ref[0, 1, level]
                advect_north = coef_ref[0, 2, level]
                mixing = coef_ref[0, 3, level]
                own_weight = 1.0 - 4.0 * diffuse - 2.0 * mixing
                north_weight = diffuse - advect_north
                south_weight = diffuse + advect_north
                east_weight = diffuse - advect_east
                west_weight = diffuse + advect_east
                whole = read(field, level)
                north = pltpu.roll(whole, wide_rows - 1, 0)[:rows, :cols]
                south = pltpu.roll(whole, 1, 0)[:rows, :cols]
                east = pltpu.roll(whole, wide_cols - 1, 1)[:rows, :cols]
                west = pltpu.roll(whole, 1, 1)[:rows, :cols]
                center = whole[:rows, :cols]
                above = read(field, min(level + 1, level_count - 1))[:rows, :cols]
                below = read(field, max(level - 1, 0))[:rows, :cols]
                updated = (
                    own_weight * center
                    + north_weight * north
                    + south_weight * south
                    + east_weight * east
                    + west_weight * west
                    + mixing * (above + below)
                )
                if field == 0:
                    updated = updated + turning * read(1, level)[:rows, :cols]
                elif field == 1:
                    updated = updated + (-turning) * read(0, level)[:rows, :cols]
                write(field, level, updated * keep)

    def from_wide(field, level):
        return wide_ref[field * level_count + level]

    def to_mid(field, level, value):
        mid_ref[field * level_count + level] = value

    def from_mid(field, level):
        return mid_ref[field * level_count + level]

    def to_out(field, level, value):
        out_ref[0, field, level] = value

    step(from_wide, to_mid, wide_rows, wide_cols)
    step(from_mid, to_out, row_count, col_count)


def dynamics(coeffs, place, wide, field_count, level_count, row_count, col_count, total_rows):
    planes, wide_rows, wide_cols = wide.shape
    return pl.pallas_call(
        functools.partial(stencil_kernel, total_rows),
        out_shape=jax.ShapeDtypeStruct((1, field_count, level_count, row_count, col_count), jnp.float32),
        in_specs=[
            pl.BlockSpec(memory_space=pltpu.SMEM),
            pl.BlockSpec(memory_space=pltpu.SMEM),
            pl.BlockSpec(memory_space=pltpu.VMEM),
        ],
        out_specs=pl.BlockSpec(memory_space=pltpu.VMEM),
        scratch_shapes=[pltpu.VMEM((planes - 1, wide_rows, wide_cols), jnp.float32)],
        interpret=INTERPRET,
    )(coeffs, place, wide)


def export_kernel(flag_ref, ground_ref, previous_ref, sea_ref, link_ref, out_ref):
    field_count, row_count, col_count = previous_ref.shape[1:]
    link_fields, link_count = link_ref.shape
    ground = ground_ref[0, :, 0]
    previous = previous_ref[0]
    sea_float = sea_ref[0].astype(jnp.float32)
    ocean = (flag_ref[0] == 1).astype(jnp.float32)
    slip_east = ground[0] - previous[0]
    slip_north = ground[1] - previous[1]
    wind_speed = jnp.sqrt(slip_east * slip_east + slip_north * slip_north + gust_speed * gust_speed)
    bulk_flux = [
        drag_coeff * wind_speed * slip_east,
        drag_coeff * wind_speed * slip_north,
        heat_coeff * wind_speed * (previous[2] - ground[2]),
    ]
    for c in range(field_count):
        out_ref[c * row_count : (c + 1) * row_count, :] = (
            ground[c] * ocean + bulk_flux[c] * (1.0 - ocean)
        ) * sea_float
    base = field_count * row_count
    out_ref[base : base + 8, :] = jnp.zeros((8, col_count), jnp.float32)
    out_ref[base : base + link_fields, :link_count] = link_ref[...]


def exported_block(flag, state, surface, sea_mask, links):
    field_count, row_count, col_count = surface.shape[1:]
    vmem = pl.BlockSpec(memory_space=pltpu.VMEM)
    return pl.pallas_call(
        export_kernel,
        out_shape=jax.ShapeDtypeStruct((field_count * row_count + 8, col_count), jnp.float32),
        in_specs=[
            pl.BlockSpec(memory_space=pltpu.SMEM),
            pl.BlockSpec((1, field_count, 1, row_count, col_count), lambda i: (0, 0, 0, 0, 0)),
            vmem,
            vmem,
            vmem,
        ],
        out_specs=vmem,
        grid=(1,),
        interpret=INTERPRET,
    )(flag, state, surface, sea_mask, links)


def remap_kernel(link_count, source_count, place_ref, *refs):
    source_refs = refs[:source_count]
    table_ref = refs[source_count]
    tile_count = table_ref.shape[1]
    out_refs = refs[source_count + 1 : -2]
    rows_ref, combo_ref = refs[-2:]
    owner_count = len(out_refs)
    field_count, row_count, col_count = out_refs[0].shape
    base = field_count * row_count
    my_lat = place_ref[1]
    my_lon = place_ref[2]
    for source in range(source_count):
        rows_ref[source * base : (source + 1) * base, :] = source_refs[source][:base, :]
    for tile in range(tile_count):
        weighted = jnp.dot(
            rows_ref[...], table_ref[0, tile], precision=lax.Precision.HIGH, preferred_element_type=jnp.float32
        )
        for source in range(source_count):
            for c in range(field_count):
                first = (source * tile_count + tile) * row_count
                combo_ref[c, first : first + row_count, :] = weighted[
                    source * base + c * row_count : source * base + (c + 1) * row_count
                ]
    pick_count = source_count * tile_count * row_count
    into = jnp.zeros((owner_count * row_count, pick_count), jnp.float32)
    for source in range(source_count):
        table = source_refs[source][base : base + 4, :link_count].astype(jnp.int32)
        dest, src_row, dst_row, tile = table[0:1], table[1:2], table[2:3], table[3:4]
        low = my_lat * owner_count
        valid = (dest >= low) & (dest < low + owner_count)
        shift = dest - low - my_lon
        shift = jnp.where(shift < 0, shift + owner_count, shift)
        dest_col = shift * row_count + dst_row
        pick_col = (source * tile_count + tile) * row_count + src_row
        to_rows = (
            (lax.broadcasted_iota(jnp.int32, (owner_count * row_count, link_count), 0) == dest_col)
            & valid
        ).astype(jnp.bfloat16)
        from_rows = (
            lax.broadcasted_iota(jnp.int32, (pick_count, link_count), 0) == pick_col
        ).astype(jnp.bfloat16)
        into = into + lax.dot_general(
            to_rows, from_rows, (((1,), (1,)), ((), ())), preferred_element_type=jnp.float32
        )
    for c in range(field_count):
        summed = jnp.dot(into, combo_ref[c], precision=lax.Precision.HIGH, preferred_element_type=jnp.float32)
        for owner in range(owner_count):
            out_refs[owner][c] = summed[owner * row_count : (owner + 1) * row_count]


def remapped(lat, sources, remap_weights, owner_count, field_count, row_count, link_count):
    source_count = len(sources)
    col_count = sources[0].shape[1]
    tile_count = remap_weights.shape[1]
    vmem = pl.BlockSpec(memory_space=pltpu.VMEM)
    return pl.pallas_call(
        functools.partial(remap_kernel, link_count, source_count),
        out_shape=[
            jax.ShapeDtypeStruct((field_count, row_count, col_count), jnp.float32)
            for owner in range(owner_count)
        ],
        in_specs=[pl.BlockSpec(memory_space=pltpu.SMEM)] + [vmem] * (source_count + 1),
        out_specs=[vmem] * owner_count,
        scratch_shapes=[
            pltpu.VMEM((source_count * field_count * row_count, col_count), jnp.float32),
            pltpu.VMEM(
                (field_count, source_count * tile_count * row_count, col_count), jnp.float32
            ),
        ],
        interpret=INTERPRET,
    )(lat, *sources, remap_weights)


def surface_export(ground, previous, sea_float, ocean_side):
    slip_east = ground[0] - previous[0]
    slip_north = ground[1] - previous[1]
    wind_speed = jnp.sqrt(slip_east * slip_east + slip_north * slip_north + gust_speed * gust_speed)
    bulk_flux = jnp.stack(
        [
            drag_coeff * wind_speed * slip_east,
            drag_coeff * wind_speed * slip_north,
            heat_coeff * wind_speed * (previous[2] - ground[2]),
        ]
    )
    return jnp.where(ocean_side, ground, bulk_flux) * sea_float


def body(
    state,
    surface,
    sea_mask,
    coeffs,
    remap_weights,
    link_dest,
    link_src_row,
    link_dst_row,
    link_tile,
):
    fields = state[0]
    previous = surface[0]
    sea_float = sea_mask[0].astype(jnp.float32)
    level_coef = coeffs[0]
    tile_table = remap_weights[0]
    field_count, level_count, row_count, col_count = fields.shape
    tile_count = tile_table.shape[0]
    ocean_side = lax.axis_index("grp") == 1
    first_row = lax.axis_index("lat") * row_count
    total_rows = row_count * lax.axis_size("lat")

    links = jnp.stack(
        [link_dest[0, :, 0], link_src_row[0], link_dst_row[0], link_tile[0]]
    ).astype(jnp.float32)
    place = jnp.stack([lax.axis_index(axis) for axis in ("grp", "lat", "lon")]).astype(jnp.int32)
    payload = exported_block(place, state, surface, sea_mask, links)
    lat_count = lax.axis_size("lat")
    lon_count = lax.axis_size("lon")
    gain = jnp.where(ocean_side, ocean_gain, air_gain)
    damping = jnp.where(ocean_side, 0.0, air_gain)
    ground = fields[:, 0] + sea_float * (gain * previous - damping * fields[:, 0])
    fields = jnp.concatenate([ground[:, None], fields[:, 1:]], 1)
    state_mask = jnp.where(ocean_side, sea_float, jnp.ones_like(sea_float))
    planes = jnp.concatenate(
        [fields.reshape(field_count * level_count, row_count, col_count), state_mask[None]], 0
    )
    plane_count = planes.shape[0]
    width = SUBSTEPS
    edge_rows = plane_count * width
    edge_pad = -(-edge_rows // 8) * 8 - edge_rows
    head = planes[:, :width, :].reshape(edge_rows, col_count)
    tail = planes[:, row_count - width :, :].reshape(edge_rows, col_count)
    gap_rows = jnp.zeros((edge_pad, col_count), jnp.float32)
    base = payload.shape[0]
    sources = [payload]
    south = north = None
    for shift in range(1, lat_count):
        parts = [payload]
        if shift == 1:
            parts += [tail, gap_rows]
        if shift == lat_count - 1:
            parts += [head, gap_rows]
        sent = jnp.concatenate(parts, 0) if len(parts) > 1 else payload
        got = lax.ppermute(sent, "lat", [(i, (i + shift) % lat_count) for i in range(lat_count)])
        sources.append(got)
        if shift == 1:
            south = got[base : base + edge_rows]
        if shift == lat_count - 1:
            start = base + (edge_rows + edge_pad if shift == 1 else 0)
            north = got[start : start + edge_rows]
    my_lat = lax.axis_index("lat")
    south = south.reshape(plane_count, width, col_count) * (my_lat > 0).astype(jnp.float32)
    north = north.reshape(plane_count, width, col_count) * (my_lat < lat_count - 1).astype(jnp.float32)
    partial = remapped(place, sources, remap_weights, lon_count, field_count, row_count, links.shape[1])
    pieces = []
    for shift in range(lon_count):
        route = [
            (g * lon_count + j, (1 - g) * lon_count + (j + shift) % lon_count)
            for g in range(2)
            for j in range(lon_count)
        ]
        pieces.append(lax.ppermute(partial[shift], ("grp", "lon"), route))
    imported = functools.reduce(jnp.add, pieces) * sea_float

    wide_rows = -(-(row_count + 4 * SUBSTEPS) // 8) * 8
    wide_cols = -(-(col_count + 4 * SUBSTEPS) // 128) * 128
    row_gap = jnp.zeros((plane_count, wide_rows - row_count - 2 * width, col_count), jnp.float32)
    stacked = jnp.concatenate([planes, north, row_gap, south], 1)
    col_gap = jnp.zeros((plane_count, wide_rows, wide_cols - col_count - 2 * width), jnp.float32)
    wide = jnp.concatenate(
        [
            stacked,
            shifted(stacked[:, :, :width], "lon", True, False),
            col_gap,
            shifted(stacked[:, :, col_count - width :], "lon", True, True),
        ],
        2,
    )
    fields = dynamics(
        coeffs, place, wide, field_count, level_count, row_count, col_count, total_rows
    )
    return (fields, imported[None])


def solution(mesh):
    placed = (
        P("grp", None, None, "lat", "lon"),
        P("grp", None, "lat", "lon"),
        P("grp", "lat", "lon"),
        P("grp", None, None),
        P("grp", None, None, None),
        P("grp", ("lat", "lon"), None),
        P("grp", ("lat", "lon")),
        P("grp", ("lat", "lon")),
        P("grp", ("lat", "lon")),
    )
    return jax.shard_map(
        body,
        mesh=mesh,
        in_specs=placed,
        out_specs=(P("grp", None, None, "lat", "lon"), P("grp", None, "lat", "lon")),
        check_vma=False,
    )
```

```python
import functools

import jax
import jax.numpy as jnp
from jax import lax
from jax.sharding import PartitionSpec as P
from jax.experimental import pallas as pl
from jax.experimental.pallas import tpu as pltpu

SUBSTEPS = 2


air_gain = 0.3
ocean_gain = 0.5
drag_coeff = 0.5
heat_coeff = 0.5
gust_speed = 0.5
coriolis_scale = 0.25

HIGHEST = lax.Precision.HIGHEST
INTERPRET = False


def shifted(part, axis, closed, forward):
    count = lax.axis_size(axis)
    ends = count if closed else count - 1
    if forward:
        route = [(i, (i + 1) % count) for i in range(ends)]
    else:
        route = [((i + 1) % count, i) for i in range(ends)]
    flat = lax.ppermute(part.reshape(-1), axis, route)
    return flat.reshape(part.shape)


def stencil_kernel(total_rows, coef_ref, place_ref, wide_ref, out_ref, mid_ref):
    field_count, level_count, row_count, col_count = out_ref.shape[1:]
    wide_rows, wide_cols = wide_ref.shape[1:]
    local = lax.broadcasted_iota(jnp.int32, (wide_rows, wide_cols), 0)
    row_index = place_ref[1] * row_count + jnp.where(
        local < wide_rows // 2 + row_count // 2, local, local - wide_rows
    )
    latitude = jnp.pi * (
        -1.0 / 3.0 + 2.0 / 3.0 * (row_index.astype(jnp.float32) + 0.5) / total_rows
    )
    turning_wide = coriolis_scale * jnp.sin(latitude)
    inside = ((row_index >= 0) & (row_index < total_rows)).astype(jnp.float32)
    keep_wide = wide_ref[field_count * level_count] * inside

    def step(read, write, rows, cols):
        turning = turning_wide[:rows, :cols]
        keep = keep_wide[:rows, :cols]
        for field in range(field_count):
            for level in range(level_count):
                diffuse = coef_ref[0, 0, level]
                advect_east = coef_ref[0, 1, level]
                advect_north = coef_ref[0, 2, level]
                mixing = coef_ref[0, 3, level]
                own_weight = 1.0 - 4.0 * diffuse - 2.0 * mixing
                north_weight = diffuse - advect_north
                south_weight = diffuse + advect_north
                east_weight = diffuse - advect_east
                west_weight = diffuse + advect_east
                whole = read(field, level)
                north = pltpu.roll(whole, wide_rows - 1, 0)[:rows, :cols]
                south = pltpu.roll(whole, 1, 0)[:rows, :cols]
                east = pltpu.roll(whole, wide_cols - 1, 1)[:rows, :cols]
                west = pltpu.roll(whole, 1, 1)[:rows, :cols]
                center = whole[:rows, :cols]
                above = read(field, min(level + 1, level_count - 1))[:rows, :cols]
                below = read(field, max(level - 1, 0))[:rows, :cols]
                updated = (
                    own_weight * center
                    + north_weight * north
                    + south_weight * south
                    + east_weight * east
                    + west_weight * west
                    + mixing * (above + below)
                )
                if field == 0:
                    updated = updated + turning * read(1, level)[:rows, :cols]
                elif field == 1:
                    updated = updated + (-turning) * read(0, level)[:rows, :cols]
                write(field, level, updated * keep)

    def from_wide(field, level):
        return wide_ref[field * level_count + level]

    def to_mid(field, level, value):
        mid_ref[field * level_count + level] = value

    def from_mid(field, level):
        return mid_ref[field * level_count + level]

    def to_out(field, level, value):
        out_ref[0, field, level] = value

    step(from_wide, to_mid, wide_rows, wide_cols)
    step(from_mid, to_out, row_count, col_count)


def dynamics(coeffs, place, wide, field_count, level_count, row_count, col_count, total_rows):
    planes, wide_rows, wide_cols = wide.shape
    return pl.pallas_call(
        functools.partial(stencil_kernel, total_rows),
        out_shape=jax.ShapeDtypeStruct((1, field_count, level_count, row_count, col_count), jnp.float32),
        in_specs=[
            pl.BlockSpec(memory_space=pltpu.SMEM),
            pl.BlockSpec(memory_space=pltpu.SMEM),
            pl.BlockSpec(memory_space=pltpu.VMEM),
        ],
        out_specs=pl.BlockSpec(memory_space=pltpu.VMEM),
        scratch_shapes=[pltpu.VMEM((planes - 1, wide_rows, wide_cols), jnp.float32)],
        interpret=INTERPRET,
    )(coeffs, place, wide)


def export_kernel(
    flag_ref, ground_ref, head_ref, tail_ref, previous_ref, sea_ref, link_ref, mid_ref, up_ref, down_ref
):
    field_count, row_count, col_count = previous_ref.shape[1:]
    level_count = head_ref.shape[2]
    link_fields, link_count = link_ref.shape
    ground = ground_ref[0, :, 0]
    previous = previous_ref[0]
    sea_float = sea_ref[0].astype(jnp.float32)
    ocean = (flag_ref[0] == 1).astype(jnp.float32)
    slip_east = ground[0] - previous[0]
    slip_north = ground[1] - previous[1]
    wind_speed = jnp.sqrt(slip_east * slip_east + slip_north * slip_north + gust_speed * gust_speed)
    bulk_flux = [
        drag_coeff * wind_speed * slip_east,
        drag_coeff * wind_speed * slip_north,
        heat_coeff * wind_speed * (previous[2] - ground[2]),
    ]
    base = field_count * row_count
    for out_ref in (mid_ref, up_ref, down_ref):
        for c in range(field_count):
            out_ref[c * row_count : (c + 1) * row_count, :] = (
                ground[c] * ocean + bulk_flux[c] * (1.0 - ocean)
            ) * sea_float
        out_ref[base : base + 8, :] = jnp.zeros((8, col_count), jnp.float32)
        out_ref[base : base + link_fields, :link_count] = link_ref[...]
    gain = air_gain + (ocean_gain - air_gain) * ocean
    damping = air_gain * (1.0 - ocean)
    width = SUBSTEPS
    per_tile = 8 // width
    row_ids = lax.broadcasted_iota(jnp.int32, (8, col_count), 0)
    for edge_ref, out_ref, first in ((tail_ref, up_ref, 8 - width), (head_ref, down_ref, 0)):
        edge_prev = previous_ref[0, :, pl.ds(row_count - 8 if first else 0, 8), :]
        edge_sea = sea_ref[0, pl.ds(row_count - 8 if first else 0, 8), :].astype(jnp.float32)
        planes = []
        for c in range(field_count):
            for level in range(level_count):
                value = edge_ref[0, c, level]
                if level == 0:
                    value = value + edge_sea * (gain * edge_prev[c] - damping * value)
                planes.append(value)
        planes.append(edge_sea * ocean + (1.0 - ocean))
        tile_count = -(-len(planes) // per_tile)
        for tile in range(tile_count):
            packed = jnp.zeros((8, col_count), jnp.float32)
            for slot in range(per_tile):
                plane = tile * per_tile + slot
                if plane >= len(planes):
                    break
                offset = slot * width
                moved = pltpu.roll(planes[plane], (offset - first) % 8, 0)
                packed = jnp.where((row_ids >= offset) & (row_ids < offset + width), moved, packed)
            out_ref[base + 8 * (tile + 1) : base + 8 * (tile + 2), :] = packed


def exported_block(flag, state, surface, sea_mask, links, edge_rows):
    field_count, row_count, col_count = surface.shape[1:]
    level_count = state.shape[2]
    vmem = pl.BlockSpec(memory_space=pltpu.VMEM)
    base = field_count * row_count + 8
    wide_rows = base + -(-edge_rows // 8) * 8
    last = row_count // 8 - 1
    return pl.pallas_call(
        export_kernel,
        out_shape=[
            jax.ShapeDtypeStruct((base, col_count), jnp.float32),
            jax.ShapeDtypeStruct((wide_rows, col_count), jnp.float32),
            jax.ShapeDtypeStruct((wide_rows, col_count), jnp.float32),
        ],
        in_specs=[
            pl.BlockSpec(memory_space=pltpu.SMEM),
            pl.BlockSpec((1, field_count, 1, row_count, col_count), lambda i: (0, 0, 0, 0, 0)),
            pl.BlockSpec((1, field_count, level_count, 8, col_count), lambda i: (0, 0, 0, 0, 0)),
            pl.BlockSpec((1, field_count, level_count, 8, col_count), lambda i: (0, 0, 0, last, 0)),
            vmem,
            vmem,
            vmem,
        ],
        out_specs=[vmem, vmem, vmem],
        grid=(1,),
        interpret=INTERPRET,
    )(flag, state, state, state, surface, sea_mask, links)


def remap_kernel(link_count, source_count, place_ref, *refs):
    source_refs = refs[:source_count]
    table_ref = refs[source_count]
    tile_count = table_ref.shape[1]
    out_refs = refs[source_count + 1 : -2]
    rows_ref, combo_ref = refs[-2:]
    owner_count = len(out_refs)
    field_count, row_count, col_count = out_refs[0].shape
    base = field_count * row_count
    my_lat = place_ref[1]
    my_lon = place_ref[2]
    for source in range(source_count):
        rows_ref[source * base : (source + 1) * base, :] = source_refs[source][:base, :]
    for tile in range(tile_count):
        weighted = jnp.dot(
            rows_ref[...], table_ref[0, tile], precision=lax.Precision.HIGH, preferred_element_type=jnp.float32
        )
        for source in range(source_count):
            for c in range(field_count):
                first = (source * tile_count + tile) * row_count
                combo_ref[c, first : first + row_count, :] = weighted[
                    source * base + c * row_count : source * base + (c + 1) * row_count
                ]
    pick_count = source_count * tile_count * row_count
    into = jnp.zeros((owner_count * row_count, pick_count), jnp.float32)
    for source in range(source_count):
        table = source_refs[source][base : base + 4, :link_count].astype(jnp.int32)
        dest, src_row, dst_row, tile = table[0:1], table[1:2], table[2:3], table[3:4]
        low = my_lat * owner_count
        valid = (dest >= low) & (dest < low + owner_count)
        shift = dest - low - my_lon
        shift = jnp.where(shift < 0, shift + owner_count, shift)
        dest_col = shift * row_count + dst_row
        pick_col = (source * tile_count + tile) * row_count + src_row
        to_rows = (
            (lax.broadcasted_iota(jnp.int32, (owner_count * row_count, link_count), 0) == dest_col)
            & valid
        ).astype(jnp.bfloat16)
        from_rows = (
            lax.broadcasted_iota(jnp.int32, (pick_count, link_count), 0) == pick_col
        ).astype(jnp.bfloat16)
        into = into + lax.dot_general(
            to_rows, from_rows, (((1,), (1,)), ((), ())), preferred_element_type=jnp.float32
        )
    for c in range(field_count):
        summed = jnp.dot(into, combo_ref[c], precision=lax.Precision.HIGH, preferred_element_type=jnp.float32)
        for owner in range(owner_count):
            out_refs[owner][c] = summed[owner * row_count : (owner + 1) * row_count]


def remapped(lat, sources, remap_weights, owner_count, field_count, row_count, link_count):
    source_count = len(sources)
    col_count = sources[0].shape[1]
    tile_count = remap_weights.shape[1]
    vmem = pl.BlockSpec(memory_space=pltpu.VMEM)
    return pl.pallas_call(
        functools.partial(remap_kernel, link_count, source_count),
        out_shape=[
            jax.ShapeDtypeStruct((field_count, row_count, col_count), jnp.float32)
            for owner in range(owner_count)
        ],
        in_specs=[pl.BlockSpec(memory_space=pltpu.SMEM)] + [vmem] * (source_count + 1),
        out_specs=[vmem] * owner_count,
        scratch_shapes=[
            pltpu.VMEM((source_count * field_count * row_count, col_count), jnp.float32),
            pltpu.VMEM(
                (field_count, source_count * tile_count * row_count, col_count), jnp.float32
            ),
        ],
        interpret=INTERPRET,
    )(lat, *sources, remap_weights)


def surface_export(ground, previous, sea_float, ocean_side):
    slip_east = ground[0] - previous[0]
    slip_north = ground[1] - previous[1]
    wind_speed = jnp.sqrt(slip_east * slip_east + slip_north * slip_north + gust_speed * gust_speed)
    bulk_flux = jnp.stack(
        [
            drag_coeff * wind_speed * slip_east,
            drag_coeff * wind_speed * slip_north,
            heat_coeff * wind_speed * (previous[2] - ground[2]),
        ]
    )
    return jnp.where(ocean_side, ground, bulk_flux) * sea_float


def body(
    state,
    surface,
    sea_mask,
    coeffs,
    remap_weights,
    link_dest,
    link_src_row,
    link_dst_row,
    link_tile,
):
    fields = state[0]
    previous = surface[0]
    sea_float = sea_mask[0].astype(jnp.float32)
    level_coef = coeffs[0]
    tile_table = remap_weights[0]
    field_count, level_count, row_count, col_count = fields.shape
    tile_count = tile_table.shape[0]
    ocean_side = lax.axis_index("grp") == 1
    first_row = lax.axis_index("lat") * row_count
    total_rows = row_count * lax.axis_size("lat")

    links = jnp.stack(
        [link_dest[0, :, 0], link_src_row[0], link_dst_row[0], link_tile[0]]
    ).astype(jnp.float32)
    place = jnp.stack([lax.axis_index(axis) for axis in ("grp", "lat", "lon")]).astype(jnp.int32)
    lat_count = lax.axis_size("lat")
    lon_count = lax.axis_size("lon")
    plane_count = field_count * level_count + 1
    width = SUBSTEPS
    edge_rows = plane_count * width
    payload, upward, downward = exported_block(place, state, surface, sea_mask, links, edge_rows)
    base = payload.shape[0]
    gain = jnp.where(ocean_side, ocean_gain, air_gain)
    damping = jnp.where(ocean_side, 0.0, air_gain)
    ground = fields[:, 0] + sea_float * (gain * previous - damping * fields[:, 0])
    fields = jnp.concatenate([ground[:, None], fields[:, 1:]], 1)
    state_mask = jnp.where(ocean_side, sea_float, jnp.ones_like(sea_float))
    planes = jnp.concatenate(
        [fields.reshape(field_count * level_count, row_count, col_count), state_mask[None]], 0
    )
    sources = [payload]
    for shift in range(1, lat_count):
        sent = upward if shift == 1 else downward if shift == lat_count - 1 else payload
        got = lax.ppermute(sent, "lat", [(i, (i + shift) % lat_count) for i in range(lat_count)])
        sources.append(got)
        if shift == 1:
            south = got[base : base + edge_rows]
        if shift == lat_count - 1:
            north = got[base : base + edge_rows]
    my_lat = lax.axis_index("lat")
    south = south.reshape(plane_count, width, col_count) * (my_lat > 0).astype(jnp.float32)
    north = north.reshape(plane_count, width, col_count) * (my_lat < lat_count - 1).astype(jnp.float32)
    partial = remapped(place, sources, remap_weights, lon_count, field_count, row_count, links.shape[1])
    pieces = []
    for shift in range(lon_count):
        route = [
            (g * lon_count + j, (1 - g) * lon_count + (j + shift) % lon_count)
            for g in range(2)
            for j in range(lon_count)
        ]
        pieces.append(lax.ppermute(partial[shift], ("grp", "lon"), route))
    imported = functools.reduce(jnp.add, pieces) * sea_float

    wide_rows = -(-(row_count + 4 * SUBSTEPS) // 8) * 8
    wide_cols = -(-(col_count + 4 * SUBSTEPS) // 128) * 128
    row_gap = jnp.zeros((plane_count, wide_rows - row_count - 2 * width, col_count), jnp.float32)
    stacked = jnp.concatenate([planes, north, row_gap, south], 1)
    col_gap = jnp.zeros((plane_count, wide_rows, wide_cols - col_count - 2 * width), jnp.float32)
    wide = jnp.concatenate(
        [
            stacked,
            shifted(stacked[:, :, :width], "lon", True, False),
            col_gap,
            shifted(stacked[:, :, col_count - width :], "lon", True, True),
        ],
        2,
    )
    fields = dynamics(
        coeffs, place, wide, field_count, level_count, row_count, col_count, total_rows
    )
    return (fields, imported[None])


def solution(mesh):
    placed = (
        P("grp", None, None, "lat", "lon"),
        P("grp", None, "lat", "lon"),
        P("grp", "lat", "lon"),
        P("grp", None, None),
        P("grp", None, None, None),
        P("grp", ("lat", "lon"), None),
        P("grp", ("lat", "lon")),
        P("grp", ("lat", "lon")),
        P("grp", ("lat", "lon")),
    )
    return jax.shard_map(
        body,
        mesh=mesh,
        in_specs=placed,
        out_specs=(P("grp", None, None, "lat", "lon"), P("grp", None, "lat", "lon")),
        check_vma=False,
    )
```

```python
import functools

import jax
import jax.numpy as jnp
from jax import lax
from jax.sharding import PartitionSpec as P
from jax.experimental import pallas as pl
from jax.experimental.pallas import tpu as pltpu

SUBSTEPS = 2


air_gain = 0.3
ocean_gain = 0.5
drag_coeff = 0.5
heat_coeff = 0.5
gust_speed = 0.5
coriolis_scale = 0.25

HIGHEST = lax.Precision.HIGHEST
INTERPRET = False


def shifted(part, axis, closed, forward):
    count = lax.axis_size(axis)
    ends = count if closed else count - 1
    if forward:
        route = [(i, (i + 1) % count) for i in range(ends)]
    else:
        route = [((i + 1) % count, i) for i in range(ends)]
    flat = lax.ppermute(part.reshape(-1), axis, route)
    return flat.reshape(part.shape)


def stencil_kernel(total_rows, coef_ref, place_ref, wide_ref, out_ref, mid_ref):
    field_count, level_count, row_count, col_count = out_ref.shape[1:]
    wide_rows, wide_cols = wide_ref.shape[1:]
    local = lax.broadcasted_iota(jnp.int32, (wide_rows, wide_cols), 0)
    row_index = place_ref[1] * row_count + jnp.where(
        local < wide_rows // 2 + row_count // 2, local, local - wide_rows
    )
    latitude = jnp.pi * (
        -1.0 / 3.0 + 2.0 / 3.0 * (row_index.astype(jnp.float32) + 0.5) / total_rows
    )
    turning_wide = coriolis_scale * jnp.sin(latitude)
    inside = ((row_index >= 0) & (row_index < total_rows)).astype(jnp.float32)
    keep_wide = wide_ref[field_count * level_count] * inside

    def step(read, write, rows, cols):
        turning = turning_wide[:rows, :cols]
        keep = keep_wide[:rows, :cols]
        for field in range(field_count):
            for level in range(level_count):
                diffuse = coef_ref[0, 0, level]
                advect_east = coef_ref[0, 1, level]
                advect_north = coef_ref[0, 2, level]
                mixing = coef_ref[0, 3, level]
                own_weight = 1.0 - 4.0 * diffuse - 2.0 * mixing
                north_weight = diffuse - advect_north
                south_weight = diffuse + advect_north
                east_weight = diffuse - advect_east
                west_weight = diffuse + advect_east
                whole = read(field, level)
                north = pltpu.roll(whole, wide_rows - 1, 0)[:rows, :cols]
                south = pltpu.roll(whole, 1, 0)[:rows, :cols]
                east = pltpu.roll(whole, wide_cols - 1, 1)[:rows, :cols]
                west = pltpu.roll(whole, 1, 1)[:rows, :cols]
                center = whole[:rows, :cols]
                above = read(field, min(level + 1, level_count - 1))[:rows, :cols]
                below = read(field, max(level - 1, 0))[:rows, :cols]
                updated = (
                    own_weight * center
                    + north_weight * north
                    + south_weight * south
                    + east_weight * east
                    + west_weight * west
                    + mixing * (above + below)
                )
                if field == 0:
                    updated = updated + turning * read(1, level)[:rows, :cols]
                elif field == 1:
                    updated = updated + (-turning) * read(0, level)[:rows, :cols]
                write(field, level, updated * keep)

    def from_wide(field, level):
        return wide_ref[field * level_count + level]

    def to_mid(field, level, value):
        mid_ref[field * level_count + level] = value

    def from_mid(field, level):
        return mid_ref[field * level_count + level]

    def to_out(field, level, value):
        out_ref[0, field, level] = value

    step(from_wide, to_mid, wide_rows, wide_cols)
    step(from_mid, to_out, row_count, col_count)


def dynamics(coeffs, place, wide, field_count, level_count, row_count, col_count, total_rows):
    planes, wide_rows, wide_cols = wide.shape
    return pl.pallas_call(
        functools.partial(stencil_kernel, total_rows),
        out_shape=jax.ShapeDtypeStruct((1, field_count, level_count, row_count, col_count), jnp.float32),
        in_specs=[
            pl.BlockSpec(memory_space=pltpu.SMEM),
            pl.BlockSpec(memory_space=pltpu.SMEM),
            pl.BlockSpec(memory_space=pltpu.VMEM),
        ],
        out_specs=pl.BlockSpec(memory_space=pltpu.VMEM),
        scratch_shapes=[pltpu.VMEM((planes - 1, wide_rows, wide_cols), jnp.float32)],
        interpret=INTERPRET,
    )(coeffs, place, wide)


def export_kernel(
    flag_ref, ground_ref, head_ref, tail_ref, previous_ref, sea_ref, link_ref, mid_ref, up_ref, down_ref
):
    field_count, row_count, col_count = previous_ref.shape[1:]
    level_count = head_ref.shape[2]
    link_fields, link_count = link_ref.shape
    ground = ground_ref[0, :, 0]
    previous = previous_ref[0]
    sea_float = sea_ref[0].astype(jnp.float32)
    ocean = (flag_ref[0] == 1).astype(jnp.float32)
    slip_east = ground[0] - previous[0]
    slip_north = ground[1] - previous[1]
    wind_speed = jnp.sqrt(slip_east * slip_east + slip_north * slip_north + gust_speed * gust_speed)
    bulk_flux = [
        drag_coeff * wind_speed * slip_east,
        drag_coeff * wind_speed * slip_north,
        heat_coeff * wind_speed * (previous[2] - ground[2]),
    ]
    base = field_count * row_count
    for out_ref in (mid_ref, up_ref, down_ref):
        for c in range(field_count):
            out_ref[c * row_count : (c + 1) * row_count, :] = (
                ground[c] * ocean + bulk_flux[c] * (1.0 - ocean)
            ) * sea_float
        out_ref[base : base + 8, :] = jnp.zeros((8, col_count), jnp.float32)
        out_ref[base : base + link_fields, :link_count] = link_ref[...]
    gain = air_gain + (ocean_gain - air_gain) * ocean
    damping = air_gain * (1.0 - ocean)
    width = SUBSTEPS
    per_tile = 8 // width
    row_ids = lax.broadcasted_iota(jnp.int32, (8, col_count), 0)
    for edge_ref, out_ref, first in ((tail_ref, up_ref, 8 - width), (head_ref, down_ref, 0)):
        edge_prev = previous_ref[0, :, pl.ds(row_count - 8 if first else 0, 8), :]
        edge_sea = sea_ref[0, pl.ds(row_count - 8 if first else 0, 8), :].astype(jnp.float32)
        planes = []
        for c in range(field_count):
            for level in range(level_count):
                value = edge_ref[0, c, level]
                if level == 0:
                    value = value + edge_sea * (gain * edge_prev[c] - damping * value)
                planes.append(value)
        planes.append(edge_sea * ocean + (1.0 - ocean))
        tile_count = -(-len(planes) // per_tile)
        for tile in range(tile_count):
            packed = jnp.zeros((8, col_count), jnp.float32)
            for slot in range(per_tile):
                plane = tile * per_tile + slot
                if plane >= len(planes):
                    break
                offset = slot * width
                moved = pltpu.roll(planes[plane], (offset - first) % 8, 0)
                packed = jnp.where((row_ids >= offset) & (row_ids < offset + width), moved, packed)
            out_ref[base + 8 * (tile + 1) : base + 8 * (tile + 2), :] = packed


def exported_block(flag, state, surface, sea_mask, links, edge_rows):
    field_count, row_count, col_count = surface.shape[1:]
    level_count = state.shape[2]
    vmem = pl.BlockSpec(memory_space=pltpu.VMEM)
    base = field_count * row_count + 8
    wide_rows = base + -(-edge_rows // 8) * 8
    last = row_count // 8 - 1
    return pl.pallas_call(
        export_kernel,
        out_shape=[
            jax.ShapeDtypeStruct((base, col_count), jnp.float32),
            jax.ShapeDtypeStruct((wide_rows, col_count), jnp.float32),
            jax.ShapeDtypeStruct((wide_rows, col_count), jnp.float32),
        ],
        in_specs=[
            pl.BlockSpec(memory_space=pltpu.SMEM),
            pl.BlockSpec((1, field_count, 1, row_count, col_count), lambda i: (0, 0, 0, 0, 0)),
            pl.BlockSpec((1, field_count, level_count, 8, col_count), lambda i: (0, 0, 0, 0, 0)),
            pl.BlockSpec((1, field_count, level_count, 8, col_count), lambda i: (0, 0, 0, last, 0)),
            vmem,
            vmem,
            vmem,
        ],
        out_specs=[vmem, vmem, vmem],
        grid=(1,),
        interpret=INTERPRET,
    )(flag, state, state, state, surface, sea_mask, links)


def own_kernel(payload_ref, table_ref, out_ref):
    tile_count = table_ref.shape[1]
    field_count, picks, col_count = out_ref.shape
    row_count = picks // tile_count
    base = field_count * row_count
    for tile in range(tile_count):
        weighted = jnp.dot(
            payload_ref[:base, :], table_ref[0, tile], precision=lax.Precision.HIGH,
            preferred_element_type=jnp.float32,
        )
        for c in range(field_count):
            out_ref[c, tile * row_count : (tile + 1) * row_count, :] = weighted[
                c * row_count : (c + 1) * row_count
            ]


def own_products(payload, remap_weights, field_count, row_count):
    tile_count = remap_weights.shape[1]
    col_count = payload.shape[1]
    vmem = pl.BlockSpec(memory_space=pltpu.VMEM)
    return pl.pallas_call(
        own_kernel,
        out_shape=jax.ShapeDtypeStruct((field_count, tile_count * row_count, col_count), jnp.float32),
        in_specs=[vmem, vmem],
        out_specs=vmem,
        interpret=INTERPRET,
    )(payload, remap_weights)


def remap_kernel(link_count, source_count, place_ref, own_ref, *refs):
    source_refs = refs[:source_count]
    table_ref = refs[source_count]
    tile_count = table_ref.shape[1]
    out_refs = refs[source_count + 1 : -2]
    rows_ref, combo_ref = refs[-2:]
    owner_count = len(out_refs)
    field_count, row_count, col_count = out_refs[0].shape
    base = field_count * row_count
    my_lat = place_ref[1]
    my_lon = place_ref[2]
    for source in range(1, source_count):
        rows_ref[(source - 1) * base : source * base, :] = source_refs[source][:base, :]
    for tile in range(tile_count):
        weighted = jnp.dot(
            rows_ref[...], table_ref[0, tile], precision=lax.Precision.HIGH, preferred_element_type=jnp.float32
        )
        for source in range(1, source_count):
            for c in range(field_count):
                first = ((source - 1) * tile_count + tile) * row_count
                combo_ref[c, first : first + row_count, :] = weighted[
                    (source - 1) * base + c * row_count : (source - 1) * base + (c + 1) * row_count
                ]
    pick_count = source_count * tile_count * row_count
    into = jnp.zeros((owner_count * row_count, pick_count), jnp.float32)
    for source in range(source_count):
        table = source_refs[source][base : base + 4, :link_count].astype(jnp.int32)
        dest, src_row, dst_row, tile = table[0:1], table[1:2], table[2:3], table[3:4]
        low = my_lat * owner_count
        valid = (dest >= low) & (dest < low + owner_count)
        shift = dest - low - my_lon
        shift = jnp.where(shift < 0, shift + owner_count, shift)
        dest_col = shift * row_count + dst_row
        pick_col = (source * tile_count + tile) * row_count + src_row
        to_rows = (
            (lax.broadcasted_iota(jnp.int32, (owner_count * row_count, link_count), 0) == dest_col)
            & valid
        ).astype(jnp.bfloat16)
        from_rows = (
            lax.broadcasted_iota(jnp.int32, (pick_count, link_count), 0) == pick_col
        ).astype(jnp.bfloat16)
        into = into + lax.dot_general(
            to_rows, from_rows, (((1,), (1,)), ((), ())), preferred_element_type=jnp.float32
        )
    for c in range(field_count):
        own_picks = tile_count * row_count
        summed = jnp.dot(
            into[:, :own_picks], own_ref[c], precision=lax.Precision.HIGH,
            preferred_element_type=jnp.float32,
        ) + jnp.dot(
            into[:, own_picks:], combo_ref[c], precision=lax.Precision.HIGH,
            preferred_element_type=jnp.float32,
        )
        for owner in range(owner_count):
            out_refs[owner][c] = summed[owner * row_count : (owner + 1) * row_count]


def remapped(lat, own, sources, remap_weights, owner_count, field_count, row_count, link_count):
    source_count = len(sources)
    col_count = sources[0].shape[1]
    tile_count = remap_weights.shape[1]
    vmem = pl.BlockSpec(memory_space=pltpu.VMEM)
    return pl.pallas_call(
        functools.partial(remap_kernel, link_count, source_count),
        out_shape=[
            jax.ShapeDtypeStruct((field_count, row_count, col_count), jnp.float32)
            for owner in range(owner_count)
        ],
        in_specs=[pl.BlockSpec(memory_space=pltpu.SMEM)] + [vmem] * (source_count + 2),
        out_specs=[vmem] * owner_count,
        scratch_shapes=[
            pltpu.VMEM(((source_count - 1) * field_count * row_count, col_count), jnp.float32),
            pltpu.VMEM(
                (field_count, (source_count - 1) * tile_count * row_count, col_count), jnp.float32
            ),
        ],
        interpret=INTERPRET,
    )(lat, own, *sources, remap_weights)


def surface_export(ground, previous, sea_float, ocean_side):
    slip_east = ground[0] - previous[0]
    slip_north = ground[1] - previous[1]
    wind_speed = jnp.sqrt(slip_east * slip_east + slip_north * slip_north + gust_speed * gust_speed)
    bulk_flux = jnp.stack(
        [
            drag_coeff * wind_speed * slip_east,
            drag_coeff * wind_speed * slip_north,
            heat_coeff * wind_speed * (previous[2] - ground[2]),
        ]
    )
    return jnp.where(ocean_side, ground, bulk_flux) * sea_float


def body(
    state,
    surface,
    sea_mask,
    coeffs,
    remap_weights,
    link_dest,
    link_src_row,
    link_dst_row,
    link_tile,
):
    fields = state[0]
    previous = surface[0]
    sea_float = sea_mask[0].astype(jnp.float32)
    level_coef = coeffs[0]
    tile_table = remap_weights[0]
    field_count, level_count, row_count, col_count = fields.shape
    tile_count = tile_table.shape[0]
    ocean_side = lax.axis_index("grp") == 1
    first_row = lax.axis_index("lat") * row_count
    total_rows = row_count * lax.axis_size("lat")

    links = jnp.stack(
        [link_dest[0, :, 0], link_src_row[0], link_dst_row[0], link_tile[0]]
    ).astype(jnp.float32)
    place = jnp.stack([lax.axis_index(axis) for axis in ("grp", "lat", "lon")]).astype(jnp.int32)
    lat_count = lax.axis_size("lat")
    lon_count = lax.axis_size("lon")
    plane_count = field_count * level_count + 1
    width = SUBSTEPS
    edge_rows = plane_count * width
    payload, upward, downward = exported_block(place, state, surface, sea_mask, links, edge_rows)
    base = payload.shape[0]
    gain = jnp.where(ocean_side, ocean_gain, air_gain)
    damping = jnp.where(ocean_side, 0.0, air_gain)
    ground = fields[:, 0] + sea_float * (gain * previous - damping * fields[:, 0])
    fields = jnp.concatenate([ground[:, None], fields[:, 1:]], 1)
    state_mask = jnp.where(ocean_side, sea_float, jnp.ones_like(sea_float))
    planes = jnp.concatenate(
        [fields.reshape(field_count * level_count, row_count, col_count), state_mask[None]], 0
    )
    sources = [payload]
    for shift in range(1, lat_count):
        sent = upward if shift == 1 else downward if shift == lat_count - 1 else payload
        got = lax.ppermute(sent, "lat", [(i, (i + shift) % lat_count) for i in range(lat_count)])
        sources.append(got)
        if shift == 1:
            south = got[base : base + edge_rows]
        if shift == lat_count - 1:
            north = got[base : base + edge_rows]
    my_lat = lax.axis_index("lat")
    south = south.reshape(plane_count, width, col_count) * (my_lat > 0).astype(jnp.float32)
    north = north.reshape(plane_count, width, col_count) * (my_lat < lat_count - 1).astype(jnp.float32)
    own = own_products(payload, remap_weights, field_count, row_count)
    partial = remapped(place, own, sources, remap_weights, lon_count, field_count, row_count, links.shape[1])
    pieces = []
    for shift in range(lon_count):
        route = [
            (g * lon_count + j, (1 - g) * lon_count + (j + shift) % lon_count)
            for g in range(2)
            for j in range(lon_count)
        ]
        pieces.append(lax.ppermute(partial[shift], ("grp", "lon"), route))
    imported = functools.reduce(jnp.add, pieces) * sea_float

    wide_rows = -(-(row_count + 4 * SUBSTEPS) // 8) * 8
    wide_cols = -(-(col_count + 4 * SUBSTEPS) // 128) * 128
    row_gap = jnp.zeros((plane_count, wide_rows - row_count - 2 * width, col_count), jnp.float32)
    stacked = jnp.concatenate([planes, north, row_gap, south], 1)
    col_gap = jnp.zeros((plane_count, wide_rows, wide_cols - col_count - 2 * width), jnp.float32)
    wide = jnp.concatenate(
        [
            stacked,
            shifted(stacked[:, :, :width], "lon", True, False),
            col_gap,
            shifted(stacked[:, :, col_count - width :], "lon", True, True),
        ],
        2,
    )
    fields = dynamics(
        coeffs, place, wide, field_count, level_count, row_count, col_count, total_rows
    )
    return (fields, imported[None])


def solution(mesh):
    placed = (
        P("grp", None, None, "lat", "lon"),
        P("grp", None, "lat", "lon"),
        P("grp", "lat", "lon"),
        P("grp", None, None),
        P("grp", None, None, None),
        P("grp", ("lat", "lon"), None),
        P("grp", ("lat", "lon")),
        P("grp", ("lat", "lon")),
        P("grp", ("lat", "lon")),
    )
    return jax.shard_map(
        body,
        mesh=mesh,
        in_specs=placed,
        out_specs=(P("grp", None, None, "lat", "lon"), P("grp", None, "lat", "lon")),
        check_vma=False,
    )
```

```python
import functools

import jax
import jax.numpy as jnp
from jax import lax
from jax.sharding import PartitionSpec as P
from jax.experimental import pallas as pl
from jax.experimental.pallas import tpu as pltpu

SUBSTEPS = 2


air_gain = 0.3
ocean_gain = 0.5
drag_coeff = 0.5
heat_coeff = 0.5
gust_speed = 0.5
coriolis_scale = 0.25

HIGHEST = lax.Precision.HIGHEST
INTERPRET = False


def shifted(part, axis, closed, forward):
    count = lax.axis_size(axis)
    ends = count if closed else count - 1
    if forward:
        route = [(i, (i + 1) % count) for i in range(ends)]
    else:
        route = [((i + 1) % count, i) for i in range(ends)]
    flat = lax.ppermute(part.reshape(-1), axis, route)
    return flat.reshape(part.shape)


def stencil_kernel(total_rows, coef_ref, place_ref, wide_ref, out_ref, mid_ref):
    field_count, level_count, row_count, col_count = out_ref.shape[1:]
    wide_rows, wide_cols = wide_ref.shape[1:]
    local = lax.broadcasted_iota(jnp.int32, (wide_rows, wide_cols), 0)
    row_index = place_ref[1] * row_count + jnp.where(
        local < wide_rows // 2 + row_count // 2, local, local - wide_rows
    )
    latitude = jnp.pi * (
        -1.0 / 3.0 + 2.0 / 3.0 * (row_index.astype(jnp.float32) + 0.5) / total_rows
    )
    turning_wide = coriolis_scale * jnp.sin(latitude)
    inside = ((row_index >= 0) & (row_index < total_rows)).astype(jnp.float32)
    keep_wide = wide_ref[field_count * level_count] * inside

    def step(read, write, rows, cols):
        turning = turning_wide[:rows, :cols]
        keep = keep_wide[:rows, :cols]
        for field in range(field_count):
            for level in range(level_count):
                diffuse = coef_ref[0, 0, level]
                advect_east = coef_ref[0, 1, level]
                advect_north = coef_ref[0, 2, level]
                mixing = coef_ref[0, 3, level]
                own_weight = 1.0 - 4.0 * diffuse - 2.0 * mixing
                north_weight = diffuse - advect_north
                south_weight = diffuse + advect_north
                east_weight = diffuse - advect_east
                west_weight = diffuse + advect_east
                whole = read(field, level)
                north = pltpu.roll(whole, wide_rows - 1, 0)[:rows, :cols]
                south = pltpu.roll(whole, 1, 0)[:rows, :cols]
                east = pltpu.roll(whole, wide_cols - 1, 1)[:rows, :cols]
                west = pltpu.roll(whole, 1, 1)[:rows, :cols]
                center = whole[:rows, :cols]
                above = read(field, min(level + 1, level_count - 1))[:rows, :cols]
                below = read(field, max(level - 1, 0))[:rows, :cols]
                updated = (
                    own_weight * center
                    + north_weight * north
                    + south_weight * south
                    + east_weight * east
                    + west_weight * west
                    + mixing * (above + below)
                )
                if field == 0:
                    updated = updated + turning * read(1, level)[:rows, :cols]
                elif field == 1:
                    updated = updated + (-turning) * read(0, level)[:rows, :cols]
                write(field, level, updated * keep)

    def from_wide(field, level):
        return wide_ref[field * level_count + level]

    def to_mid(field, level, value):
        mid_ref[field * level_count + level] = value

    def from_mid(field, level):
        return mid_ref[field * level_count + level]

    def to_out(field, level, value):
        out_ref[0, field, level] = value

    step(from_wide, to_mid, wide_rows, wide_cols)
    step(from_mid, to_out, row_count, col_count)


def dynamics(coeffs, place, wide, field_count, level_count, row_count, col_count, total_rows):
    planes, wide_rows, wide_cols = wide.shape
    return pl.pallas_call(
        functools.partial(stencil_kernel, total_rows),
        out_shape=jax.ShapeDtypeStruct((1, field_count, level_count, row_count, col_count), jnp.float32),
        in_specs=[
            pl.BlockSpec(memory_space=pltpu.SMEM),
            pl.BlockSpec(memory_space=pltpu.SMEM),
            pl.BlockSpec(memory_space=pltpu.VMEM),
        ],
        out_specs=pl.BlockSpec(memory_space=pltpu.VMEM),
        scratch_shapes=[pltpu.VMEM((planes - 1, wide_rows, wide_cols), jnp.float32)],
        interpret=INTERPRET,
    )(coeffs, place, wide)


def export_kernel(
    flag_ref, ground_ref, head_ref, tail_ref, previous_ref, sea_ref, dest_ref, src_ref, dst_ref,
    tile_ref, mid_ref, up_ref, down_ref
):
    field_count, row_count, col_count = previous_ref.shape[1:]
    level_count = head_ref.shape[2]
    link_count = src_ref.shape[1]
    dest_col = dest_ref[0].astype(jnp.float32)
    dest_row = jnp.transpose(jnp.broadcast_to(dest_col, (link_count, link_count)))[0:1, :]
    link_rows = jnp.concatenate(
        [dest_row] + [ref[...].astype(jnp.float32) for ref in (src_ref, dst_ref, tile_ref)], 0
    )
    link_fields = link_rows.shape[0]
    ground = ground_ref[0, :, 0]
    previous = previous_ref[0]
    sea_float = sea_ref[0].astype(jnp.float32)
    ocean = (flag_ref[0] == 1).astype(jnp.float32)
    slip_east = ground[0] - previous[0]
    slip_north = ground[1] - previous[1]
    wind_speed = jnp.sqrt(slip_east * slip_east + slip_north * slip_north + gust_speed * gust_speed)
    bulk_flux = [
        drag_coeff * wind_speed * slip_east,
        drag_coeff * wind_speed * slip_north,
        heat_coeff * wind_speed * (previous[2] - ground[2]),
    ]
    base = field_count * row_count
    for out_ref in (mid_ref, up_ref, down_ref):
        for c in range(field_count):
            out_ref[c * row_count : (c + 1) * row_count, :] = (
                ground[c] * ocean + bulk_flux[c] * (1.0 - ocean)
            ) * sea_float
        out_ref[base : base + 8, :] = jnp.zeros((8, col_count), jnp.float32)
        out_ref[base : base + link_fields, :link_count] = link_rows
    gain = air_gain + (ocean_gain - air_gain) * ocean
    damping = air_gain * (1.0 - ocean)
    width = SUBSTEPS
    per_tile = 8 // width
    row_ids = lax.broadcasted_iota(jnp.int32, (8, col_count), 0)
    for edge_ref, out_ref, first in ((tail_ref, up_ref, 8 - width), (head_ref, down_ref, 0)):
        edge_prev = previous_ref[0, :, pl.ds(row_count - 8 if first else 0, 8), :]
        edge_sea = sea_ref[0, pl.ds(row_count - 8 if first else 0, 8), :].astype(jnp.float32)
        planes = []
        for c in range(field_count):
            for level in range(level_count):
                value = edge_ref[0, c, level]
                if level == 0:
                    value = value + edge_sea * (gain * edge_prev[c] - damping * value)
                planes.append(value)
        planes.append(edge_sea * ocean + (1.0 - ocean))
        tile_count = -(-len(planes) // per_tile)
        for tile in range(tile_count):
            packed = jnp.zeros((8, col_count), jnp.float32)
            for slot in range(per_tile):
                plane = tile * per_tile + slot
                if plane >= len(planes):
                    break
                offset = slot * width
                moved = pltpu.roll(planes[plane], (offset - first) % 8, 0)
                packed = jnp.where((row_ids >= offset) & (row_ids < offset + width), moved, packed)
            out_ref[base + 8 * (tile + 1) : base + 8 * (tile + 2), :] = packed


def exported_block(flag, state, surface, sea_mask, links, edge_rows):
    link_dest, link_src_row, link_dst_row, link_tile = links
    field_count, row_count, col_count = surface.shape[1:]
    level_count = state.shape[2]
    vmem = pl.BlockSpec(memory_space=pltpu.VMEM)
    base = field_count * row_count + 8
    wide_rows = base + -(-edge_rows // 8) * 8
    last = row_count // 8 - 1
    return pl.pallas_call(
        export_kernel,
        out_shape=[
            jax.ShapeDtypeStruct((base, col_count), jnp.float32),
            jax.ShapeDtypeStruct((wide_rows, col_count), jnp.float32),
            jax.ShapeDtypeStruct((wide_rows, col_count), jnp.float32),
        ],
        in_specs=[
            pl.BlockSpec(memory_space=pltpu.SMEM),
            pl.BlockSpec((1, field_count, 1, row_count, col_count), lambda i: (0, 0, 0, 0, 0)),
            pl.BlockSpec((1, field_count, level_count, 8, col_count), lambda i: (0, 0, 0, 0, 0)),
            pl.BlockSpec((1, field_count, level_count, 8, col_count), lambda i: (0, 0, 0, last, 0)),
            vmem,
            vmem,
            vmem,
            vmem,
            vmem,
            vmem,
        ],
        out_specs=[vmem, vmem, vmem],
        grid=(1,),
        interpret=INTERPRET,
    )(flag, state, state, state, surface, sea_mask, link_dest, link_src_row, link_dst_row, link_tile)


def remap_kernel(link_count, source_count, place_ref, *refs):
    source_refs = refs[:source_count]
    table_ref = refs[source_count]
    tile_count = table_ref.shape[1]
    out_refs = refs[source_count + 1 : -2]
    rows_ref, combo_ref = refs[-2:]
    owner_count = len(out_refs)
    field_count, row_count, col_count = out_refs[0].shape
    base = field_count * row_count
    my_lat = place_ref[1]
    my_lon = place_ref[2]
    for source in range(source_count):
        rows_ref[source * base : (source + 1) * base, :] = source_refs[source][:base, :]
    for tile in range(tile_count):
        weighted = jnp.dot(
            rows_ref[...], table_ref[0, tile], precision=lax.Precision.HIGH, preferred_element_type=jnp.float32
        )
        for source in range(source_count):
            for c in range(field_count):
                first = (source * tile_count + tile) * row_count
                combo_ref[c, first : first + row_count, :] = weighted[
                    source * base + c * row_count : source * base + (c + 1) * row_count
                ]
    pick_count = source_count * tile_count * row_count
    into = jnp.zeros((owner_count * row_count, pick_count), jnp.float32)
    for source in range(source_count):
        table = source_refs[source][base : base + 4, :link_count].astype(jnp.int32)
        dest, src_row, dst_row, tile = table[0:1], table[1:2], table[2:3], table[3:4]
        low = my_lat * owner_count
        valid = (dest >= low) & (dest < low + owner_count)
        shift = dest - low - my_lon
        shift = jnp.where(shift < 0, shift + owner_count, shift)
        dest_col = shift * row_count + dst_row
        pick_col = (source * tile_count + tile) * row_count + src_row
        to_rows = (
            (lax.broadcasted_iota(jnp.int32, (owner_count * row_count, link_count), 0) == dest_col)
            & valid
        ).astype(jnp.bfloat16)
        from_rows = (
            lax.broadcasted_iota(jnp.int32, (pick_count, link_count), 0) == pick_col
        ).astype(jnp.bfloat16)
        into = into + lax.dot_general(
            to_rows, from_rows, (((1,), (1,)), ((), ())), preferred_element_type=jnp.float32
        )
    for c in range(field_count):
        summed = jnp.dot(into, combo_ref[c], precision=lax.Precision.HIGH, preferred_element_type=jnp.float32)
        for owner in range(owner_count):
            out_refs[owner][c] = summed[owner * row_count : (owner + 1) * row_count]


def remapped(lat, sources, remap_weights, owner_count, field_count, row_count, link_count):
    source_count = len(sources)
    col_count = sources[0].shape[1]
    tile_count = remap_weights.shape[1]
    vmem = pl.BlockSpec(memory_space=pltpu.VMEM)
    return pl.pallas_call(
        functools.partial(remap_kernel, link_count, source_count),
        out_shape=[
            jax.ShapeDtypeStruct((field_count, row_count, col_count), jnp.float32)
            for owner in range(owner_count)
        ],
        in_specs=[pl.BlockSpec(memory_space=pltpu.SMEM)] + [vmem] * (source_count + 1),
        out_specs=[vmem] * owner_count,
        scratch_shapes=[
            pltpu.VMEM((source_count * field_count * row_count, col_count), jnp.float32),
            pltpu.VMEM(
                (field_count, source_count * tile_count * row_count, col_count), jnp.float32
            ),
        ],
        interpret=INTERPRET,
    )(lat, *sources, remap_weights)


def surface_export(ground, previous, sea_float, ocean_side):
    slip_east = ground[0] - previous[0]
    slip_north = ground[1] - previous[1]
    wind_speed = jnp.sqrt(slip_east * slip_east + slip_north * slip_north + gust_speed * gust_speed)
    bulk_flux = jnp.stack(
        [
            drag_coeff * wind_speed * slip_east,
            drag_coeff * wind_speed * slip_north,
            heat_coeff * wind_speed * (previous[2] - ground[2]),
        ]
    )
    return jnp.where(ocean_side, ground, bulk_flux) * sea_float


def body(
    state,
    surface,
    sea_mask,
    coeffs,
    remap_weights,
    link_dest,
    link_src_row,
    link_dst_row,
    link_tile,
):
    fields = state[0]
    previous = surface[0]
    sea_float = sea_mask[0].astype(jnp.float32)
    level_coef = coeffs[0]
    tile_table = remap_weights[0]
    field_count, level_count, row_count, col_count = fields.shape
    tile_count = tile_table.shape[0]
    ocean_side = lax.axis_index("grp") == 1
    first_row = lax.axis_index("lat") * row_count
    total_rows = row_count * lax.axis_size("lat")

    links = (link_dest, link_src_row, link_dst_row, link_tile)
    place = jnp.stack([lax.axis_index(axis) for axis in ("grp", "lat", "lon")]).astype(jnp.int32)
    lat_count = lax.axis_size("lat")
    lon_count = lax.axis_size("lon")
    plane_count = field_count * level_count + 1
    width = SUBSTEPS
    edge_rows = plane_count * width
    payload, upward, downward = exported_block(place, state, surface, sea_mask, links, edge_rows)
    base = payload.shape[0]
    gain = jnp.where(ocean_side, ocean_gain, air_gain)
    damping = jnp.where(ocean_side, 0.0, air_gain)
    ground = fields[:, 0] + sea_float * (gain * previous - damping * fields[:, 0])
    fields = jnp.concatenate([ground[:, None], fields[:, 1:]], 1)
    state_mask = jnp.where(ocean_side, sea_float, jnp.ones_like(sea_float))
    planes = jnp.concatenate(
        [fields.reshape(field_count * level_count, row_count, col_count), state_mask[None]], 0
    )
    sources = [payload]
    for shift in range(1, lat_count):
        sent = upward if shift == 1 else downward if shift == lat_count - 1 else payload
        got = lax.ppermute(sent, "lat", [(i, (i + shift) % lat_count) for i in range(lat_count)])
        sources.append(got)
        if shift == 1:
            south = got[base : base + edge_rows]
        if shift == lat_count - 1:
            north = got[base : base + edge_rows]
    my_lat = lax.axis_index("lat")
    south = south.reshape(plane_count, width, col_count) * (my_lat > 0).astype(jnp.float32)
    north = north.reshape(plane_count, width, col_count) * (my_lat < lat_count - 1).astype(jnp.float32)
    partial = remapped(place, sources, remap_weights, lon_count, field_count, row_count, link_src_row.shape[1])
    pieces = []
    for shift in range(lon_count):
        route = [
            (g * lon_count + j, (1 - g) * lon_count + (j + shift) % lon_count)
            for g in range(2)
            for j in range(lon_count)
        ]
        pieces.append(lax.ppermute(partial[shift], ("grp", "lon"), route))
    imported = functools.reduce(jnp.add, pieces) * sea_float

    wide_rows = -(-(row_count + 4 * SUBSTEPS) // 8) * 8
    wide_cols = -(-(col_count + 4 * SUBSTEPS) // 128) * 128
    row_gap = jnp.zeros((plane_count, wide_rows - row_count - 2 * width, col_count), jnp.float32)
    stacked = jnp.concatenate([planes, north, row_gap, south], 1)
    col_gap = jnp.zeros((plane_count, wide_rows, wide_cols - col_count - 2 * width), jnp.float32)
    wide = jnp.concatenate(
        [
            stacked,
            shifted(stacked[:, :, :width], "lon", True, False),
            col_gap,
            shifted(stacked[:, :, col_count - width :], "lon", True, True),
        ],
        2,
    )
    fields = dynamics(
        coeffs, place, wide, field_count, level_count, row_count, col_count, total_rows
    )
    return (fields, imported[None])


def solution(mesh):
    placed = (
        P("grp", None, None, "lat", "lon"),
        P("grp", None, "lat", "lon"),
        P("grp", "lat", "lon"),
        P("grp", None, None),
        P("grp", None, None, None),
        P("grp", ("lat", "lon"), None),
        P("grp", ("lat", "lon")),
        P("grp", ("lat", "lon")),
        P("grp", ("lat", "lon")),
    )
    return jax.shard_map(
        body,
        mesh=mesh,
        in_specs=placed,
        out_specs=(P("grp", None, None, "lat", "lon"), P("grp", None, "lat", "lon")),
        check_vma=False,
    )
```
